512 devices in a mesh: acq: 16 (over y_lo, x, core), pulse: 32 (over y_hi, z).
Axes of the slice: x: 4, y: 4 (y_hi: 2, y_lo: 2; y = y_hi * 2 + y_lo), z: 16, core: 2. Of those that a mesh axis runs over, the one named last changes fastest.
Arguments:
- raw_echo: bfloat16 [16, 2, 8192, 1535], P('acq', None, 'pulse'), may hold values from -6 to 6
- chirp_phase: float32 [1024], replicated, may hold values from -3.140625 to 3.140625
- pulse_counts: int32 [16], P('acq'), may hold values from 4096 to 8192, as said below
- azimuth_rate: float32 [512], P('pulse'), may hold values from 0.25 to 1
- partner_bits: int32 [16, 2], P('acq'), may hold values from 0 to 3, as said below
Outputs:
- interfere_real: float32 [16, 2, 128, 512], P('acq', None, 'pulse')
- interfere_imag: float32 [16, 2, 128, 512], P('acq', None, 'pulse')
The draws below stay inside these ranges and needn't reach their ends.
Inputs may be any that keep to these rules, and one draw needn't show every extreme that they name: `pulse_counts`: at least half of 8192; some acquisition records all 8192 pulses and some exactly half. `partner_bits`: the two bits of a row differ.
All inputs are finite; a program needn't handle non-finite values.
Results may differ from the reference program's by a relative error of at most 0.0065.
Values may be sent and summed in bfloat16 or wider, within the bound.
No kernel may reach another device: no remote copies, remote signals or barrier semaphores. Data moves between devices by JAX's collectives and lax.ppermute only.
A program may use at most 64 MiB of HBM per device.

```python
import math
import jax
import jax.numpy as jnp
from jax import lax

RNG = 512
TAPS = 1024
PULSES = 8192
LOOK_RNG = 4
LOOK_AZ = 16
ACQS = 16
ACQ_BITS = 4
ECHO = 1535


def draw_pulse_counts(key, part):
    first_key, second_key = jax.random.split(key)
    recorded = jax.random.randint(first_key, (ACQS,), PULSES // 2, PULSES + 1, dtype=jnp.int32)
    order = jax.random.permutation(second_key, ACQS)
    recorded = recorded.at[order[0]].set(PULSES)
    recorded = recorded.at[order[1]].set(PULSES // 2)
    return recorded.astype(jnp.int32)


def draw_partner_bits(key, part):
    first_key, second_key, third_key = jax.random.split(key, 3)
    leading = jax.random.randint(first_key, (ACQS,), 0, ACQ_BITS, dtype=jnp.int32)
    stride = jax.random.randint(second_key, (ACQS,), 1, ACQ_BITS, dtype=jnp.int32)
    trailing = (leading + stride) % ACQ_BITS
    chosen = jax.random.randint(third_key, (), 0, ACQS, dtype=jnp.int32)
    leading = leading.at[chosen].set(0)
    trailing = trailing.at[chosen].set(ACQ_BITS - 1)
    return jnp.stack([leading, trailing], axis=1).astype(jnp.int32)


def block_scale(own_key, dims, cuts, low, top_value):
    loudness, own = 1.0, jax.random.fold_in(own_key, 6)
    for axis_at, blocks in cuts:
        steps = jnp.exp(jax.random.uniform(jax.random.fold_in(own, axis_at), (blocks,), jnp.float32, low / len(cuts), top_value / len(cuts)))
        loudness = loudness * jnp.repeat(steps, dims[axis_at] // blocks).reshape([-1 if axis == axis_at else 1 for axis in range(len(dims))])
    return loudness


def scatter_about(own_key, dims, scale, most, shards=(), kind=jnp.bfloat16):
    array = jax.random.normal(own_key, dims, jnp.float32) * scale
    if len(shards) > 0:
        array = block_scale(own_key, dims, shards, -0.22, 0.18) * array
    return jnp.clip(array, min=-most, max=most).astype(kind)


def setup_inputs(seed: int = 0) -> dict:
    keys = jax.random.split(jax.random.key(seed), 6)
    return {
        "raw_echo": scatter_about(keys[0], (ACQS, 2, PULSES, ECHO), 1.0, 6.0, ((0, 16), (2, 32))),
        "chirp_phase": jnp.clip(jax.random.uniform(keys[1], (TAPS,), jnp.float32, -3.140625, 3.140625), -3.140625, 3.140625),
        "pulse_counts": draw_pulse_counts(jax.random.fold_in(keys[5], 71), 0),
        "azimuth_rate": jnp.clip(jnp.exp(math.log(1.0) - 1.3862944 * jax.random.uniform(keys[3], (RNG,), jnp.float32) ** block_scale(keys[3], (RNG,), ((0, 32),), -0.2, 0.2)), 0.25, 1.0),
        "partner_bits": draw_partner_bits(jax.random.fold_in(keys[5], 71), 0),
    }


def reference(raw_echo, chirp_phase, pulse_counts, azimuth_rate, partner_bits):
    amplitude = 2.0 / math.sqrt(TAPS)
    table_re = (amplitude * jnp.cos(chirp_phase)).astype(jnp.bfloat16).astype(jnp.float32)
    table_im = (amplitude * jnp.sin(chirp_phase)).astype(jnp.bfloat16).astype(jnp.float32)
    chirp = table_re + 1j * table_im
    span = RNG + TAPS
    chirp_spec = jnp.conj(jnp.fft.fft(chirp, n=span))
    freq_index = jnp.arange(PULSES, dtype=jnp.int32)
    signed = jnp.where(freq_index < PULSES // 2, freq_index, freq_index - PULSES).astype(jnp.float32)
    quad = signed * signed / PULSES
    phase = (jnp.pi * azimuth_rate)[:, None] * quad[None, :]
    matched = jnp.cos(phase) - 1j * jnp.sin(phase)
    pulse_index = jnp.arange(PULSES, dtype=jnp.int32)

    def focus(inputs):
        echoes, recorded = inputs
        signal = echoes[0].astype(jnp.float32) + 1j * echoes[1].astype(jnp.float32)
        spectrum = jnp.fft.fft(signal, n=span, axis=1)
        compressed = jnp.fft.ifft(spectrum * chirp_spec[None, :], axis=1)[:, :RNG]
        keep = (pulse_index < recorded).astype(jnp.float32)[:, None]
        comp_re = (jnp.real(compressed) * keep).astype(jnp.bfloat16).astype(jnp.float32)
        comp_im = (jnp.imag(compressed) * keep).astype(jnp.bfloat16).astype(jnp.float32)
        columns = (comp_re + 1j * comp_im).T
        focused = jnp.fft.ifft(jnp.fft.fft(columns, axis=1) * matched, axis=1)
        return jnp.stack([jnp.real(focused), jnp.imag(focused)]).astype(jnp.bfloat16)
    focused_all = lax.map(focus, (raw_echo, pulse_counts))
    acq_index = jnp.arange(ACQS, dtype=jnp.int32)

    def multilook(values):
        shaped = values.reshape(RNG // LOOK_RNG, LOOK_RNG, PULSES // LOOK_AZ, LOOK_AZ)
        return lax.optimization_barrier(jnp.mean(shaped, axis=(1, 3)))

    def interfere(inputs):
        number, chosen = inputs
        own_block = focused_all[number].astype(jnp.float32)
        real_parts = []
        imag_parts = []
        for slot in range(2):
            partner_index = jnp.bitwise_xor(number, jnp.left_shift(jnp.int32(1), chosen[slot]))
            partner = focused_all[partner_index].astype(jnp.float32)
            prod_re = own_block[0] * partner[0] + own_block[1] * partner[1]
            prod_im = own_block[1] * partner[0] - own_block[0] * partner[1]
            real_parts.append(multilook(prod_re))
            imag_parts.append(multilook(prod_im))
        return (jnp.stack(real_parts), jnp.stack(imag_parts))
    interfere_real, interfere_imag = lax.map(interfere, (acq_index, partner_bits))
    return (interfere_real, interfere_imag)
```

```python
import math

import jax
import jax.numpy as jnp
from jax import lax
from jax.sharding import PartitionSpec as P

RNG = 512
TAPS = 1024
LOOK_RNG = 4
LOOK_AZ = 16


def part_tables(length, inverse):
    steps = jnp.arange(length, dtype=jnp.int32)
    angle = 2.0 * jnp.pi * (steps[:, None] * steps[None, :] % length).astype(jnp.float32) / length
    cosine = jnp.cos(angle)
    sine = jnp.sin(angle)
    if inverse:
        sine = -sine
    return jnp.stack([jnp.stack([cosine, -sine]), jnp.stack([sine, cosine])])


def complex_product(left_re, left_im, right_re, right_im):
    return (left_re * right_re - left_im * right_im, left_re * right_im + left_im * right_re)


def compress(echoes, toeplitz, first_pulse, live_pulses, block_cols, window):
    pulse_rows = echoes.shape[1]
    parts_re = []
    parts_im = []
    for start in range(0, RNG, block_cols):
        segment = echoes[:, :, start : start + window]
        stacked = jnp.concatenate([segment[0], segment[1]], axis=1)
        result = lax.dot_general(
            toeplitz, stacked, (((1,), (1,)), ((), ())), preferred_element_type=jnp.float32
        )
        parts_re.append(result[:block_cols])
        parts_im.append(result[block_cols:])
    joined = jnp.stack([jnp.concatenate(parts_re, axis=0), jnp.concatenate(parts_im, axis=0)])
    pulse_ids = first_pulse + jnp.arange(pulse_rows, dtype=jnp.int32)
    keep = (pulse_ids < live_pulses).astype(jnp.float32)
    return (joined * keep[None, None, :]).astype(jnp.bfloat16)


def azimuth(turned, azimuth_rate):
    columns = turned.shape[1]
    length = turned.shape[2]
    outer_len = 64
    inner_len = length // outer_len
    highest = lax.Precision.HIGHEST
    signal = turned.astype(jnp.float32).reshape(2, columns, outer_len, inner_len)
    section_one = jnp.einsum(
        "pcab,pqak->qckb", signal, part_tables(outer_len, False), precision=highest
    )
    outer_ids = jnp.arange(outer_len, dtype=jnp.int32)
    inner_ids = jnp.arange(inner_len, dtype=jnp.int32)
    twist = (
        2.0
        * jnp.pi
        * (outer_ids[:, None] * inner_ids[None, :] % length).astype(jnp.float32)
        / length
    )
    twist_cos = jnp.cos(twist)
    twist_sin = jnp.sin(twist)
    turned_re, turned_im = complex_product(section_one[0], section_one[1], twist_cos, -twist_sin)
    spectrum = jnp.einsum(
        "pckb,pqbm->qckm",
        jnp.stack([turned_re, turned_im]),
        part_tables(inner_len, False),
        precision=highest,
    )
    freq_index = outer_ids[:, None] + outer_len * inner_ids[None, :]
    signed = jnp.where(freq_index < length // 2, freq_index, freq_index - length).astype(
        jnp.float32
    )
    quad = signed * signed / length
    phase = (jnp.pi * azimuth_rate)[:, None, None] * quad[None, :, :]
    filt_re, filt_im = complex_product(spectrum[0], spectrum[1], jnp.cos(phase), -jnp.sin(phase))
    back_one = jnp.einsum(
        "pckm,pqmb->qckb",
        jnp.stack([filt_re, filt_im]),
        part_tables(inner_len, True),
        precision=highest,
    )
    undo_re, undo_im = complex_product(back_one[0], back_one[1], twist_cos, twist_sin)
    restored = jnp.einsum(
        "pckb,pqka->qcab",
        jnp.stack([undo_re, undo_im]),
        part_tables(outer_len, True),
        precision=highest,
    )
    return (restored / length).reshape(2, columns, length)


def parity(index):
    return bin(index).count("1") % 2


def multilook(stacked):
    count, columns, pulse_len = stacked.shape
    inner = 128
    shaped = stacked.reshape(count, columns // LOOK_RNG, LOOK_RNG, pulse_len // inner, inner)
    summed = jnp.sum(shaped, axis=2)
    lanes = jnp.arange(inner, dtype=jnp.int32)
    groups = jnp.arange(inner // LOOK_AZ, dtype=jnp.int32)
    pool = (lanes[:, None] // LOOK_AZ == groups[None, :]).astype(jnp.float32)
    looked = jnp.einsum("nrab,bg->nrag", summed, pool, precision=lax.Precision.HIGHEST)
    scale = 1.0 / (LOOK_RNG * LOOK_AZ)
    return looked.reshape(count, columns // LOOK_RNG, pulse_len // LOOK_AZ) * scale


def cross_looks(own_block, partners):
    own_f = own_block.astype(jnp.float32)
    prods = []
    for partner in partners:
        other_f = partner.astype(jnp.float32)
        prods.append(own_f[0] * other_f[0] + own_f[1] * other_f[1])
        prods.append(own_f[1] * other_f[0] - own_f[0] * other_f[1])
    looked = multilook(jnp.stack(prods))
    return looked.reshape(len(partners), 2, *looked.shape[1:])


def per_device(raw_echo, chirp_phase, pulse_counts, azimuth_rate, partner_bits):
    echoes = raw_echo[0]
    pulses_dev = echoes.shape[1]
    block_cols = min(256, RNG)
    window = block_cols + TAPS - 1
    amplitude = 2.0 / math.sqrt(TAPS)
    table_re = (amplitude * jnp.cos(chirp_phase)).astype(jnp.bfloat16)
    table_im = (amplitude * jnp.sin(chirp_phase)).astype(jnp.bfloat16)
    padding = jnp.zeros((block_cols,), jnp.bfloat16)
    band_re = jnp.tile(jnp.concatenate([table_re, padding]), block_cols)[
        : block_cols * window
    ].reshape(block_cols, window)
    band_im = jnp.tile(jnp.concatenate([table_im, padding]), block_cols)[
        : block_cols * window
    ].reshape(block_cols, window)
    toeplitz = jnp.concatenate(
        [jnp.concatenate([band_re, band_im], axis=1), jnp.concatenate([-band_im, band_re], axis=1)],
        axis=0,
    )
    live_pulses = pulse_counts[0]
    first_pulse = lax.axis_index("pulse") * pulses_dev
    compressed = compress(echoes, toeplitz, first_pulse, live_pulses, block_cols, window)
    turned = lax.all_to_all(compressed, "pulse", split_axis=1, concat_axis=2, tiled=True)
    focused = azimuth(turned, azimuth_rate).astype(jnp.bfloat16)
    chosen = partner_bits[0]
    acq_size = lax.axis_size("acq")
    me = lax.axis_index("acq")
    me_parity = jnp.int32(0)
    for which in range(acq_size.bit_length() - 1):
        me_parity = me_parity ^ ((me >> which) & 1)
    low_bits = (0, 1)
    high_bits = (2, 3)
    edge_pairs = []
    for slot in range(2):
        edge_pairs.append(
            [
                (i, i ^ (1 << (high_bits[slot] if parity(i) else low_bits[slot])))
                for i in range(acq_size)
            ]
        )
    arrived = [lax.ppermute(focused, "acq", pairs) for pairs in edge_pairs]
    looked = cross_looks(focused, arrived)
    returned = [
        lax.ppermute(looked[slot], "acq", [(dst, src) for src, dst in edge_pairs[slot]])
        for slot in range(2)
    ]
    candidates = []
    for slot in range(2):
        recv_bit = jnp.where(me_parity == 1, low_bits[slot], high_bits[slot])
        send_bit = jnp.where(me_parity == 1, high_bits[slot], low_bits[slot])
        candidates.append((recv_bit, looked[slot]))
        back = returned[slot]
        candidates.append((send_bit, jnp.stack([back[0], -back[1]])))
    results = []
    for slot in range(2):
        pick = candidates[0][1]
        for bit, value in candidates[1:]:
            pick = jnp.where(chosen[slot] == bit, value, pick)
        results.append(pick)
    interfere_real = jnp.stack([item[0] for item in results])[None]
    interfere_imag = jnp.stack([item[1] for item in results])[None]
    return (interfere_real, interfere_imag)


def solution(mesh):
    in_specs = (P("acq", None, "pulse", None), P(), P("acq"), P("pulse"), P("acq", None))
    out_specs = (P("acq", None, "pulse", None), P("acq", None, "pulse", None))
    return jax.shard_map(
        per_device, mesh=mesh, in_specs=in_specs, out_specs=out_specs, check_vma=False
    )
```

```python
import math

import jax
import jax.numpy as jnp
from jax import lax
from jax.experimental import pallas as pl
from jax.experimental.pallas import tpu as pltpu
from jax.sharding import PartitionSpec as P

RNG = 512
TAPS = 1024
LOOK_RNG = 4
LOOK_AZ = 16


def part_tables(length, inverse):
    steps = jnp.arange(length, dtype=jnp.int32)
    angle = 2.0 * jnp.pi * (steps[:, None] * steps[None, :] % length).astype(jnp.float32) / length
    cosine = jnp.cos(angle)
    sine = jnp.sin(angle)
    if inverse:
        sine = -sine
    return jnp.stack([jnp.stack([cosine, -sine]), jnp.stack([sine, cosine])])


def complex_product(left_re, left_im, right_re, right_im):
    return (left_re * right_re - left_im * right_im, left_re * right_im + left_im * right_re)


def band_kernel(re_ref, im_ref, first_ref, second_ref):
    width = first_ref.shape[1]
    span = re_ref.shape[1]
    block = 128
    for start in range(0, RNG, block):
        re_band = pltpu.roll(jnp.broadcast_to(re_ref[...], (block, span)), start, 1, stride=1, stride_axis=0)
        im_band = pltpu.roll(jnp.broadcast_to(im_ref[...], (block, span)), start, 1, stride=1, stride_axis=0)
        first_ref[start : start + block, :] = re_band[:, :width].astype(first_ref.dtype)
        first_ref[RNG + start : RNG + start + block, :] = (-im_band)[:, :width].astype(first_ref.dtype)
        second_ref[start : start + block, :] = im_band[:, :width].astype(second_ref.dtype)
        second_ref[RNG + start : RNG + start + block, :] = re_band[:, :width].astype(second_ref.dtype)


def band_tables(table_re, table_im, width):
    span = -(-(width + 1) // 128) * 128
    pad = jnp.zeros((span - table_re.shape[0],), jnp.float32)
    re_row = jnp.concatenate([table_re.astype(jnp.float32), pad])[None]
    im_row = jnp.concatenate([table_im.astype(jnp.float32), pad])[None]
    shape = jax.ShapeDtypeStruct((2 * RNG, width), jnp.bfloat16)
    return pl.pallas_call(band_kernel, out_shape=[shape, shape])(re_row, im_row)


def compress(echoes, first_band, second_band, first_pulse, live_pulses):
    pulse_rows = echoes.shape[1]
    dims = (((1,), (1,)), ((), ()))
    result = lax.dot_general(
        first_band, echoes[0], dims, preferred_element_type=jnp.float32
    ) + lax.dot_general(second_band, echoes[1], dims, preferred_element_type=jnp.float32)
    joined = result.reshape(2, RNG, pulse_rows)
    pulse_ids = first_pulse + jnp.arange(pulse_rows, dtype=jnp.int32)
    keep = (pulse_ids < live_pulses).astype(jnp.float32)
    return (joined * keep[None, None, :]).astype(jnp.bfloat16)


def azimuth(turned, azimuth_rate):
    columns = turned.shape[1]
    length = turned.shape[2]
    outer_len = 64
    inner_len = length // outer_len
    highest = lax.Precision.HIGHEST
    signal = turned.astype(jnp.float32).reshape(2, columns, outer_len, inner_len)
    section_one = jnp.einsum(
        "pcab,pqak->qckb", signal, part_tables(outer_len, False), precision=highest
    )
    outer_ids = jnp.arange(outer_len, dtype=jnp.int32)
    inner_ids = jnp.arange(inner_len, dtype=jnp.int32)
    twist = (
        2.0
        * jnp.pi
        * (outer_ids[:, None] * inner_ids[None, :] % length).astype(jnp.float32)
        / length
    )
    twist_cos = jnp.cos(twist)
    twist_sin = jnp.sin(twist)
    turned_re, turned_im = complex_product(section_one[0], section_one[1], twist_cos, -twist_sin)
    spectrum = jnp.einsum(
        "pckb,pqbm->qckm",
        jnp.stack([turned_re, turned_im]),
        part_tables(inner_len, False),
        precision=highest,
    )
    freq_index = outer_ids[:, None] + outer_len * inner_ids[None, :]
    signed = jnp.where(freq_index < length // 2, freq_index, freq_index - length).astype(
        jnp.float32
    )
    quad = signed * signed / length
    phase = (jnp.pi * azimuth_rate)[:, None, None] * quad[None, :, :]
    filt_re, filt_im = complex_product(spectrum[0], spectrum[1], jnp.cos(phase), -jnp.sin(phase))
    back_one = jnp.einsum(
        "pckm,pqmb->qckb",
        jnp.stack([filt_re, filt_im]),
        part_tables(inner_len, True),
        precision=highest,
    )
    undo_re, undo_im = complex_product(back_one[0], back_one[1], twist_cos, twist_sin)
    restored = jnp.einsum(
        "pckb,pqka->qcab",
        jnp.stack([undo_re, undo_im]),
        part_tables(outer_len, True),
        precision=highest,
    )
    return (restored / length).reshape(2, columns, length)


def parity(index):
    return bin(index).count("1") % 2


def multilook(stacked):
    count, columns, pulse_len = stacked.shape
    inner = 128
    shaped = stacked.reshape(count, columns // LOOK_RNG, LOOK_RNG, pulse_len // inner, inner)
    summed = jnp.sum(shaped, axis=2)
    lanes = jnp.arange(inner, dtype=jnp.int32)
    groups = jnp.arange(inner // LOOK_AZ, dtype=jnp.int32)
    pool = (lanes[:, None] // LOOK_AZ == groups[None, :]).astype(jnp.float32)
    looked = jnp.einsum("nrab,bg->nrag", summed, pool, precision=lax.Precision.HIGHEST)
    scale = 1.0 / (LOOK_RNG * LOOK_AZ)
    return looked.reshape(count, columns // LOOK_RNG, pulse_len // LOOK_AZ) * scale


def cross_looks(own_block, partners):
    own_f = own_block.astype(jnp.float32)
    prods = []
    for partner in partners:
        other_f = partner.astype(jnp.float32)
        prods.append(own_f[0] * other_f[0] + own_f[1] * other_f[1])
        prods.append(own_f[1] * other_f[0] - own_f[0] * other_f[1])
    looked = multilook(jnp.stack(prods))
    return looked.reshape(len(partners), 2, *looked.shape[1:])


def per_device(raw_echo, chirp_phase, pulse_counts, azimuth_rate, partner_bits):
    echoes = raw_echo[0]
    pulses_dev = echoes.shape[1]
    amplitude = 2.0 / math.sqrt(TAPS)
    table_re = (amplitude * jnp.cos(chirp_phase)).astype(jnp.bfloat16)
    table_im = (amplitude * jnp.sin(chirp_phase)).astype(jnp.bfloat16)
    first_band, second_band = band_tables(table_re, table_im, echoes.shape[2])
    live_pulses = pulse_counts[0]
    first_pulse = lax.axis_index("pulse") * pulses_dev
    compressed = compress(echoes, first_band, second_band, first_pulse, live_pulses)
    turned = lax.all_to_all(compressed, "pulse", split_axis=1, concat_axis=2, tiled=True)
    focused = azimuth(turned, azimuth_rate).astype(jnp.bfloat16)
    chosen = partner_bits[0]
    acq_size = lax.axis_size("acq")
    me = lax.axis_index("acq")
    me_parity = jnp.int32(0)
    for which in range(acq_size.bit_length() - 1):
        me_parity = me_parity ^ ((me >> which) & 1)
    low_bits = (0, 1)
    high_bits = (2, 3)
    edge_pairs = []
    for slot in range(2):
        edge_pairs.append(
            [
                (i, i ^ (1 << (high_bits[slot] if parity(i) else low_bits[slot])))
                for i in range(acq_size)
            ]
        )
    arrived = [lax.ppermute(focused, "acq", pairs) for pairs in edge_pairs]
    looked = cross_looks(focused, arrived)
    returned = [
        lax.ppermute(looked[slot], "acq", [(dst, src) for src, dst in edge_pairs[slot]])
        for slot in range(2)
    ]
    candidates = []
    for slot in range(2):
        recv_bit = jnp.where(me_parity == 1, low_bits[slot], high_bits[slot])
        send_bit = jnp.where(me_parity == 1, high_bits[slot], low_bits[slot])
        candidates.append((recv_bit, looked[slot]))
        back = returned[slot]
        candidates.append((send_bit, jnp.stack([back[0], -back[1]])))
    results = []
    for slot in range(2):
        pick = candidates[0][1]
        for bit, value in candidates[1:]:
            pick = jnp.where(chosen[slot] == bit, value, pick)
        results.append(pick)
    interfere_real = jnp.stack([item[0] for item in results])[None]
    interfere_imag = jnp.stack([item[1] for item in results])[None]
    return (interfere_real, interfere_imag)


def solution(mesh):
    in_specs = (P("acq", None, "pulse", None), P(), P("acq"), P("pulse"), P("acq", None))
    out_specs = (P("acq", None, "pulse", None), P("acq", None, "pulse", None))
    return jax.shard_map(
        per_device, mesh=mesh, in_specs=in_specs, out_specs=out_specs, check_vma=False
    )
```

```python
import math

import jax
import jax.numpy as jnp
from jax import lax
from jax.experimental import pallas as pl
from jax.experimental.pallas import tpu as pltpu
from jax.sharding import PartitionSpec as P

RNG = 512
TAPS = 1024
LOOK_RNG = 4
LOOK_AZ = 16


def part_tables(length, inverse):
    steps = jnp.arange(length, dtype=jnp.int32)
    angle = 2.0 * jnp.pi * (steps[:, None] * steps[None, :] % length).astype(jnp.float32) / length
    cosine = jnp.cos(angle)
    sine = jnp.sin(angle)
    if inverse:
        sine = -sine
    return jnp.stack([jnp.stack([cosine, -sine]), jnp.stack([sine, cosine])])


def complex_product(left_re, left_im, right_re, right_im):
    return (left_re * right_re - left_im * right_im, left_re * right_im + left_im * right_re)


def band_kernel(re_ref, im_ref, band_ref):
    block = band_ref.shape[2]
    width = band_ref.shape[3]
    span = re_ref.shape[1]
    re_band = pltpu.roll(jnp.broadcast_to(re_ref[0:1, :], (block, span)), 0, 1, stride=1, stride_axis=0)
    im_band = pltpu.roll(jnp.broadcast_to(im_ref[0:1, :], (block, span)), 0, 1, stride=1, stride_axis=0)
    band_ref[0, 0] = re_band[:, :width].astype(band_ref.dtype)
    band_ref[0, 1] = (-im_band)[:, :width].astype(band_ref.dtype)
    band_ref[1, 0] = im_band[:, :width].astype(band_ref.dtype)
    band_ref[1, 1] = re_band[:, :width].astype(band_ref.dtype)


def band_tables(table_re, table_im, width):
    span = -(-(width + 1) // 128) * 128
    block = 128
    steps = RNG // block
    pad = jnp.zeros((span - table_re.shape[0],), jnp.float32)
    rows = []
    for table in (table_re, table_im):
        row = jnp.concatenate([table.astype(jnp.float32), pad])
        shifted = jnp.stack([jnp.roll(row, block * step) for step in range(steps)])
        rows.append(jnp.repeat(shifted, 8, axis=0))
    row_spec = pl.BlockSpec((8, span), lambda i: (i, 0))
    out_spec = pl.BlockSpec((2, 2, block, width), lambda i: (0, 0, i, 0))
    shape = jax.ShapeDtypeStruct((2, 2, RNG, width), jnp.bfloat16)
    band = pl.pallas_call(
        band_kernel,
        grid=(steps,),
        in_specs=[row_spec, row_spec],
        out_specs=out_spec,
        out_shape=shape,
    )(*rows)
    return band.reshape(2, 2 * RNG, width)


def compress(echoes, band, first_pulse, live_pulses):
    pulse_rows = echoes.shape[1]
    dims = (((0, 2), (0, 2)), ((), ()))
    result = lax.dot_general(band, echoes, dims, preferred_element_type=jnp.float32)
    joined = result.reshape(2, RNG, pulse_rows)
    pulse_ids = first_pulse + jnp.arange(pulse_rows, dtype=jnp.int32)
    keep = (pulse_ids < live_pulses).astype(jnp.float32)
    return (joined * keep[None, None, :]).astype(jnp.bfloat16)


def azimuth(turned, azimuth_rate):
    columns = turned.shape[1]
    length = turned.shape[2]
    outer_len = 64
    inner_len = length // outer_len
    highest = lax.Precision.HIGHEST
    signal = turned.astype(jnp.float32).reshape(2, columns, outer_len, inner_len)
    section_one = jnp.einsum(
        "pcab,pqak->qckb", signal, part_tables(outer_len, False), precision=highest
    )
    outer_ids = jnp.arange(outer_len, dtype=jnp.int32)
    inner_ids = jnp.arange(inner_len, dtype=jnp.int32)
    twist = (
        2.0
        * jnp.pi
        * (outer_ids[:, None] * inner_ids[None, :] % length).astype(jnp.float32)
        / length
    )
    twist_cos = jnp.cos(twist)
    twist_sin = jnp.sin(twist)
    turned_re, turned_im = complex_product(section_one[0], section_one[1], twist_cos, -twist_sin)
    spectrum = jnp.einsum(
        "pckb,pqbm->qckm",
        jnp.stack([turned_re, turned_im]),
        part_tables(inner_len, False),
        precision=highest,
    )
    freq_index = outer_ids[:, None] + outer_len * inner_ids[None, :]
    signed = jnp.where(freq_index < length // 2, freq_index, freq_index - length).astype(
        jnp.float32
    )
    quad = signed * signed / length
    phase = (jnp.pi * azimuth_rate)[:, None, None] * quad[None, :, :]
    filt_re, filt_im = complex_product(spectrum[0], spectrum[1], jnp.cos(phase), -jnp.sin(phase))
    back_one = jnp.einsum(
        "pckm,pqmb->qckb",
        jnp.stack([filt_re, filt_im]),
        part_tables(inner_len, True),
        precision=highest,
    )
    undo_re, undo_im = complex_product(back_one[0], back_one[1], twist_cos, twist_sin)
    restored = jnp.einsum(
        "pckb,pqka->qcab",
        jnp.stack([undo_re, undo_im]),
        part_tables(outer_len, True),
        precision=highest,
    )
    return (restored / length).reshape(2, columns, length)


def parity(index):
    return bin(index).count("1") % 2


def multilook(stacked):
    count, columns, pulse_len = stacked.shape
    inner = 128
    shaped = stacked.reshape(count, columns // LOOK_RNG, LOOK_RNG, pulse_len // inner, inner)
    summed = jnp.sum(shaped, axis=2)
    lanes = jnp.arange(inner, dtype=jnp.int32)
    groups = jnp.arange(inner // LOOK_AZ, dtype=jnp.int32)
    pool = (lanes[:, None] // LOOK_AZ == groups[None, :]).astype(jnp.float32)
    looked = jnp.einsum("nrab,bg->nrag", summed, pool, precision=lax.Precision.HIGHEST)
    scale = 1.0 / (LOOK_RNG * LOOK_AZ)
    return looked.reshape(count, columns // LOOK_RNG, pulse_len // LOOK_AZ) * scale


def cross_looks(own_block, partners):
    own_f = own_block.astype(jnp.float32)
    prods = []
    for partner in partners:
        other_f = partner.astype(jnp.float32)
        prods.append(own_f[0] * other_f[0] + own_f[1] * other_f[1])
        prods.append(own_f[1] * other_f[0] - own_f[0] * other_f[1])
    looked = multilook(jnp.stack(prods))
    return looked.reshape(len(partners), 2, *looked.shape[1:])


def per_device(raw_echo, chirp_phase, pulse_counts, azimuth_rate, partner_bits):
    echoes = raw_echo[0]
    pulses_dev = echoes.shape[1]
    amplitude = 2.0 / math.sqrt(TAPS)
    table_re = (amplitude * jnp.cos(chirp_phase)).astype(jnp.bfloat16)
    table_im = (amplitude * jnp.sin(chirp_phase)).astype(jnp.bfloat16)
    band = band_tables(table_re, table_im, echoes.shape[2])
    live_pulses = pulse_counts[0]
    first_pulse = lax.axis_index("pulse") * pulses_dev
    compressed = compress(echoes, band, first_pulse, live_pulses)
    turned = lax.all_to_all(compressed, "pulse", split_axis=1, concat_axis=2, tiled=True)
    focused = azimuth(turned, azimuth_rate).astype(jnp.bfloat16)
    chosen = partner_bits[0]
    acq_size = lax.axis_size("acq")
    me = lax.axis_index("acq")
    me_parity = jnp.int32(0)
    for which in range(acq_size.bit_length() - 1):
        me_parity = me_parity ^ ((me >> which) & 1)
    low_bits = (0, 1)
    high_bits = (2, 3)
    edge_pairs = []
    for slot in range(2):
        edge_pairs.append(
            [
                (i, i ^ (1 << (high_bits[slot] if parity(i) else low_bits[slot])))
                for i in range(acq_size)
            ]
        )
    arrived = [lax.ppermute(focused, "acq", pairs) for pairs in edge_pairs]
    looked = cross_looks(focused, arrived)
    returned = [
        lax.ppermute(looked[slot], "acq", [(dst, src) for src, dst in edge_pairs[slot]])
        for slot in range(2)
    ]
    candidates = []
    for slot in range(2):
        recv_bit = jnp.where(me_parity == 1, low_bits[slot], high_bits[slot])
        send_bit = jnp.where(me_parity == 1, high_bits[slot], low_bits[slot])
        candidates.append((recv_bit, looked[slot]))
        back = returned[slot]
        candidates.append((send_bit, jnp.stack([back[0], -back[1]])))
    results = []
    for slot in range(2):
        pick = candidates[0][1]
        for bit, value in candidates[1:]:
            pick = jnp.where(chosen[slot] == bit, value, pick)
        results.append(pick)
    interfere_real = jnp.stack([item[0] for item in results])[None]
    interfere_imag = jnp.stack([item[1] for item in results])[None]
    return (interfere_real, interfere_imag)


def solution(mesh):
    in_specs = (P("acq", None, "pulse", None), P(), P("acq"), P("pulse"), P("acq", None))
    out_specs = (P("acq", None, "pulse", None), P("acq", None, "pulse", None))
    return jax.shard_map(
        per_device, mesh=mesh, in_specs=in_specs, out_specs=out_specs, check_vma=False
    )
```

```python
import math

import jax
import jax.numpy as jnp
from jax import lax
from jax.experimental import pallas as pl
from jax.experimental.pallas import tpu as pltpu
from jax.sharding import PartitionSpec as P

RNG = 512
TAPS = 1024
LOOK_RNG = 4
LOOK_AZ = 16


def part_tables(length, inverse):
    steps = jnp.arange(length, dtype=jnp.int32)
    angle = 2.0 * jnp.pi * (steps[:, None] * steps[None, :] % length).astype(jnp.float32) / length
    cosine = jnp.cos(angle)
    sine = jnp.sin(angle)
    if inverse:
        sine = -sine
    return jnp.stack([jnp.stack([cosine, -sine]), jnp.stack([sine, cosine])])


def complex_product(left_re, left_im, right_re, right_im):
    return (left_re * right_re - left_im * right_im, left_re * right_im + left_im * right_re)


def band_kernel(re_ref, im_ref, band_ref):
    block = band_ref.shape[2]
    width = band_ref.shape[3]
    span = re_ref.shape[1]
    re_band = pltpu.roll(jnp.broadcast_to(re_ref[0:1, :], (block, span)), 0, 1, stride=1, stride_axis=0)
    im_band = pltpu.roll(jnp.broadcast_to(im_ref[0:1, :], (block, span)), 0, 1, stride=1, stride_axis=0)
    band_ref[0, 0] = re_band[:, :width].astype(band_ref.dtype)
    band_ref[0, 1] = (-im_band)[:, :width].astype(band_ref.dtype)
    band_ref[1, 0] = im_band[:, :width].astype(band_ref.dtype)
    band_ref[1, 1] = re_band[:, :width].astype(band_ref.dtype)


def band_tables(table_re, table_im, width):
    span = -(-(width + 1) // 128) * 128
    block = 128
    steps = RNG // block
    pad = jnp.zeros((span - table_re.shape[0],), jnp.float32)
    rows = []
    for table in (table_re, table_im):
        row = jnp.concatenate([table.astype(jnp.float32), pad])
        shifted = jnp.stack([jnp.roll(row, block * step) for step in range(steps)])
        rows.append(jnp.repeat(shifted, 8, axis=0))
    row_spec = pl.BlockSpec((8, span), lambda i: (i, 0))
    out_spec = pl.BlockSpec((2, 2, block, width), lambda i: (0, 0, i, 0))
    shape = jax.ShapeDtypeStruct((2, 2, RNG, width), jnp.bfloat16)
    band = pl.pallas_call(
        band_kernel,
        grid=(steps,),
        in_specs=[row_spec, row_spec],
        out_specs=out_spec,
        out_shape=shape,
    )(*rows)
    return band.reshape(2, 2 * RNG, width)


def compress(echoes, band, first_pulse, live_pulses):
    pulse_rows = echoes.shape[1]
    dims = (((0, 2), (0, 2)), ((), ()))
    result = lax.dot_general(band, echoes, dims, preferred_element_type=jnp.float32)
    joined = result.reshape(2, RNG, pulse_rows)
    pulse_ids = first_pulse + jnp.arange(pulse_rows, dtype=jnp.int32)
    keep = (pulse_ids < live_pulses).astype(jnp.float32)
    return (joined * keep[None, None, :]).astype(jnp.bfloat16)


def azimuth(turned, azimuth_rate):
    columns = turned.shape[1]
    length = turned.shape[2]
    outer_len = 64
    inner_len = length // outer_len
    highest = lax.Precision.HIGHEST
    signal = turned.astype(jnp.float32).reshape(2, columns, outer_len, inner_len)
    section_one = jnp.einsum(
        "pcab,pqak->qckb", signal, part_tables(outer_len, False), precision=highest
    )
    outer_ids = jnp.arange(outer_len, dtype=jnp.int32)
    inner_ids = jnp.arange(inner_len, dtype=jnp.int32)
    twist = (
        2.0
        * jnp.pi
        * (outer_ids[:, None] * inner_ids[None, :] % length).astype(jnp.float32)
        / length
    )
    twist_cos = jnp.cos(twist)
    twist_sin = jnp.sin(twist)
    turned_re, turned_im = complex_product(section_one[0], section_one[1], twist_cos, -twist_sin)
    spectrum = jnp.einsum(
        "pckb,pqbm->qckm",
        jnp.stack([turned_re, turned_im]),
        part_tables(inner_len, False),
        precision=highest,
    )
    freq_index = outer_ids[:, None] + outer_len * inner_ids[None, :]
    signed = jnp.where(freq_index < length // 2, freq_index, freq_index - length).astype(
        jnp.float32
    )
    quad = signed * signed / length
    phase = (jnp.pi * azimuth_rate)[:, None, None] * quad[None, :, :]
    filt_re, filt_im = complex_product(spectrum[0], spectrum[1], jnp.cos(phase), -jnp.sin(phase))
    back_one = jnp.einsum(
        "pckm,pqmb->qckb",
        jnp.stack([filt_re, filt_im]),
        part_tables(inner_len, True),
        precision=highest,
    )
    undo_re, undo_im = complex_product(back_one[0], back_one[1], twist_cos, twist_sin)
    restored = jnp.einsum(
        "pckb,pqka->qcab",
        jnp.stack([undo_re, undo_im]),
        part_tables(outer_len, True),
        precision=highest,
    )
    return (restored / length).reshape(2, columns, length)


def parity(index):
    return bin(index).count("1") % 2


def multilook(stacked):
    count, columns, pulse_len = stacked.shape
    inner = 128
    shaped = stacked.reshape(count, columns // LOOK_RNG, LOOK_RNG, pulse_len // inner, inner)
    summed = jnp.sum(shaped, axis=2)
    lanes = jnp.arange(inner, dtype=jnp.int32)
    groups = jnp.arange(inner // LOOK_AZ, dtype=jnp.int32)
    pool = (lanes[:, None] // LOOK_AZ == groups[None, :]).astype(jnp.float32)
    looked = jnp.einsum("nrab,bg->nrag", summed, pool, precision=lax.Precision.HIGHEST)
    scale = 1.0 / (LOOK_RNG * LOOK_AZ)
    return looked.reshape(count, columns // LOOK_RNG, pulse_len // LOOK_AZ) * scale


def cross_looks(own_block, partners):
    own_f = own_block.astype(jnp.float32)
    prods = []
    for partner in partners:
        other_f = partner.astype(jnp.float32)
        prods.append(own_f[0] * other_f[0] + own_f[1] * other_f[1])
        prods.append(own_f[1] * other_f[0] - own_f[0] * other_f[1])
    looked = multilook(jnp.stack(prods))
    return looked.reshape(len(partners), 2, *looked.shape[1:])


def per_device(raw_echo, chirp_phase, pulse_counts, azimuth_rate, partner_bits):
    echoes = raw_echo[0]
    pulses_dev = echoes.shape[1]
    amplitude = 2.0 / math.sqrt(TAPS)
    table_re = (amplitude * jnp.cos(chirp_phase)).astype(jnp.bfloat16)
    table_im = (amplitude * jnp.sin(chirp_phase)).astype(jnp.bfloat16)
    band = band_tables(table_re, table_im, echoes.shape[2])
    live_pulses = pulse_counts[0]
    first_pulse = lax.axis_index(("pulse_hi", "pulse_lo")) * pulses_dev
    compressed = compress(echoes, band, first_pulse, live_pulses)
    outer = lax.axis_size("pulse_hi")
    inner = lax.axis_size("pulse_lo")
    cells = RNG // (outer * inner)
    parts = compressed.reshape(2, outer, inner, cells, pulses_dev)
    parts = lax.all_to_all(parts, "pulse_lo", 2, 2, tiled=True)
    parts = lax.all_to_all(parts, "pulse_hi", 1, 1, tiled=True)
    turned = parts.transpose(0, 3, 1, 2, 4).reshape(2, cells, outer * inner * pulses_dev)
    focused = azimuth(turned, azimuth_rate).astype(jnp.bfloat16)
    chosen = partner_bits[0]
    acq_size = lax.axis_size("acq")
    me = lax.axis_index("acq")
    me_parity = jnp.int32(0)
    for which in range(acq_size.bit_length() - 1):
        me_parity = me_parity ^ ((me >> which) & 1)
    low_bits = (0, 1)
    high_bits = (2, 3)
    edge_pairs = []
    for slot in range(2):
        edge_pairs.append(
            [
                (i, i ^ (1 << (high_bits[slot] if parity(i) else low_bits[slot])))
                for i in range(acq_size)
            ]
        )
    arrived = [lax.ppermute(focused, "acq", pairs) for pairs in edge_pairs]
    looked = cross_looks(focused, arrived)
    returned = [
        lax.ppermute(looked[slot], "acq", [(dst, src) for src, dst in edge_pairs[slot]])
        for slot in range(2)
    ]
    candidates = []
    for slot in range(2):
        recv_bit = jnp.where(me_parity == 1, low_bits[slot], high_bits[slot])
        send_bit = jnp.where(me_parity == 1, high_bits[slot], low_bits[slot])
        candidates.append((recv_bit, looked[slot]))
        back = returned[slot]
        candidates.append((send_bit, jnp.stack([back[0], -back[1]])))
    results = []
    for slot in range(2):
        pick = candidates[0][1]
        for bit, value in candidates[1:]:
            pick = jnp.where(chosen[slot] == bit, value, pick)
        results.append(pick)
    interfere_real = jnp.stack([item[0] for item in results])[None]
    interfere_imag = jnp.stack([item[1] for item in results])[None]
    return (interfere_real, interfere_imag)


def solution(mesh):
    pulse_axis = mesh.devices.shape[1]
    outer = 2 if pulse_axis % 2 == 0 else 1
    devices = mesh.devices.reshape(mesh.devices.shape[0], outer, pulse_axis // outer)
    split_mesh = jax.sharding.Mesh(devices, ("acq", "pulse_hi", "pulse_lo"))
    pulse = ("pulse_hi", "pulse_lo")
    in_specs = (P("acq", None, pulse, None), P(), P("acq"), P(pulse), P("acq", None))
    out_specs = (P("acq", None, pulse, None), P("acq", None, pulse, None))
    return jax.shard_map(
        per_device, mesh=split_mesh, in_specs=in_specs, out_specs=out_specs, check_vma=False
    )
```

```python
import math

import jax
import jax.numpy as jnp
from jax import lax
from jax.experimental import pallas as pl
from jax.experimental.pallas import tpu as pltpu
from jax.sharding import PartitionSpec as P

RNG = 512
TAPS = 1024
LOOK_RNG = 4
LOOK_AZ = 16
CHUNKS = 2


def part_tables(length, inverse):
    steps = jnp.arange(length, dtype=jnp.int32)
    angle = 2.0 * jnp.pi * (steps[:, None] * steps[None, :] % length).astype(jnp.float32) / length
    cosine = jnp.cos(angle)
    sine = jnp.sin(angle)
    if inverse:
        sine = -sine
    return jnp.stack([jnp.stack([cosine, -sine]), jnp.stack([sine, cosine])])


def complex_product(left_re, left_im, right_re, right_im):
    return (left_re * right_re - left_im * right_im, left_re * right_im + left_im * right_re)


def band_kernel(re_ref, im_ref, band_ref):
    block = band_ref.shape[2]
    width = band_ref.shape[3]
    span = re_ref.shape[1]
    re_band = pltpu.roll(jnp.broadcast_to(re_ref[0:1, :], (block, span)), 0, 1, stride=1, stride_axis=0)
    im_band = pltpu.roll(jnp.broadcast_to(im_ref[0:1, :], (block, span)), 0, 1, stride=1, stride_axis=0)
    band_ref[0, 0] = re_band[:, :width].astype(band_ref.dtype)
    band_ref[0, 1] = (-im_band)[:, :width].astype(band_ref.dtype)
    band_ref[1, 0] = im_band[:, :width].astype(band_ref.dtype)
    band_ref[1, 1] = re_band[:, :width].astype(band_ref.dtype)


def band_tables(table_re, table_im, width):
    span = -(-(width + 1) // 128) * 128
    block = 128
    steps = RNG // block
    pad = jnp.zeros((span - table_re.shape[0],), jnp.float32)
    rows = []
    for table in (table_re, table_im):
        row = jnp.concatenate([table.astype(jnp.float32), pad])
        shifted = jnp.stack([jnp.roll(row, block * step) for step in range(steps)])
        rows.append(jnp.repeat(shifted, 8, axis=0))
    row_spec = pl.BlockSpec((8, span), lambda i: (i, 0))
    out_spec = pl.BlockSpec((2, 2, block, width), lambda i: (0, 0, i, 0))
    shape = jax.ShapeDtypeStruct((2, 2, RNG, width), jnp.bfloat16)
    band = pl.pallas_call(
        band_kernel,
        grid=(steps,),
        in_specs=[row_spec, row_spec],
        out_specs=out_spec,
        out_shape=shape,
    )(*rows)
    return band.reshape(2, 2 * RNG, width)


def compress(echoes, band, first_pulse, live_pulses):
    pulse_rows = echoes.shape[1]
    dims = (((0, 2), (0, 2)), ((), ()))
    result = lax.dot_general(band, echoes, dims, preferred_element_type=jnp.float32)
    joined = result.reshape(2, RNG, pulse_rows)
    pulse_ids = first_pulse + jnp.arange(pulse_rows, dtype=jnp.int32)
    keep = (pulse_ids < live_pulses).astype(jnp.float32)
    return (joined * keep[None, None, :]).astype(jnp.bfloat16)


def azimuth(turned, azimuth_rate):
    columns = turned.shape[1]
    length = turned.shape[2]
    outer_len = 64
    inner_len = length // outer_len
    highest = lax.Precision.HIGHEST
    signal = turned.astype(jnp.float32).reshape(2, columns, outer_len, inner_len)
    section_one = jnp.einsum(
        "pcab,pqak->qckb", signal, part_tables(outer_len, False), precision=highest
    )
    outer_ids = jnp.arange(outer_len, dtype=jnp.int32)
    inner_ids = jnp.arange(inner_len, dtype=jnp.int32)
    twist = (
        2.0
        * jnp.pi
        * (outer_ids[:, None] * inner_ids[None, :] % length).astype(jnp.float32)
        / length
    )
    twist_cos = jnp.cos(twist)
    twist_sin = jnp.sin(twist)
    turned_re, turned_im = complex_product(section_one[0], section_one[1], twist_cos, -twist_sin)
    spectrum = jnp.einsum(
        "pckb,pqbm->qckm",
        jnp.stack([turned_re, turned_im]),
        part_tables(inner_len, False),
        precision=highest,
    )
    freq_index = outer_ids[:, None] + outer_len * inner_ids[None, :]
    signed = jnp.where(freq_index < length // 2, freq_index, freq_index - length).astype(
        jnp.float32
    )
    quad = signed * signed / length
    phase = (jnp.pi * azimuth_rate)[:, None, None] * quad[None, :, :]
    filt_re, filt_im = complex_product(spectrum[0], spectrum[1], jnp.cos(phase), -jnp.sin(phase))
    back_one = jnp.einsum(
        "pckm,pqmb->qckb",
        jnp.stack([filt_re, filt_im]),
        part_tables(inner_len, True),
        precision=highest,
    )
    undo_re, undo_im = complex_product(back_one[0], back_one[1], twist_cos, twist_sin)
    restored = jnp.einsum(
        "pckb,pqka->qcab",
        jnp.stack([undo_re, undo_im]),
        part_tables(outer_len, True),
        precision=highest,
    )
    return (restored / length).reshape(2, columns, length)


def parity(index):
    return bin(index).count("1") % 2


def multilook(stacked):
    count, columns, pulse_len = stacked.shape
    inner = 128
    shaped = stacked.reshape(count, columns // LOOK_RNG, LOOK_RNG, pulse_len // inner, inner)
    summed = jnp.sum(shaped, axis=2)
    lanes = jnp.arange(inner, dtype=jnp.int32)
    groups = jnp.arange(inner // LOOK_AZ, dtype=jnp.int32)
    pool = (lanes[:, None] // LOOK_AZ == groups[None, :]).astype(jnp.float32)
    looked = jnp.einsum("nrab,bg->nrag", summed, pool, precision=lax.Precision.HIGHEST)
    scale = 1.0 / (LOOK_RNG * LOOK_AZ)
    return looked.reshape(count, columns // LOOK_RNG, pulse_len // LOOK_AZ) * scale


def cross_looks(own_block, partners):
    own_f = own_block.astype(jnp.float32)
    prods = []
    for partner in partners:
        other_f = partner.astype(jnp.float32)
        prods.append(own_f[0] * other_f[0] + own_f[1] * other_f[1])
        prods.append(own_f[1] * other_f[0] - own_f[0] * other_f[1])
    looked = multilook(jnp.stack(prods))
    return looked.reshape(len(partners), 2, *looked.shape[1:])


def per_device(raw_echo, chirp_phase, pulse_counts, azimuth_rate, partner_bits):
    echoes = raw_echo[0]
    pulses_dev = echoes.shape[1]
    amplitude = 2.0 / math.sqrt(TAPS)
    table_re = (amplitude * jnp.cos(chirp_phase)).astype(jnp.bfloat16)
    table_im = (amplitude * jnp.sin(chirp_phase)).astype(jnp.bfloat16)
    band = band_tables(table_re, table_im, echoes.shape[2])
    live_pulses = pulse_counts[0]
    first_pulse = lax.axis_index("pulse") * pulses_dev
    compressed = compress(echoes, band, first_pulse, live_pulses)
    devices = lax.axis_size("pulse")
    cells = RNG // devices
    chunk_cells = cells // CHUNKS
    pieces = compressed.reshape(2, devices, CHUNKS, chunk_cells, pulses_dev).transpose(2, 0, 1, 3, 4)
    chosen = partner_bits[0]
    acq_size = lax.axis_size("acq")
    me = lax.axis_index("acq")
    me_parity = jnp.int32(0)
    for which in range(acq_size.bit_length() - 1):
        me_parity = me_parity ^ ((me >> which) & 1)
    low_bits = (0, 1)
    high_bits = (2, 3)
    edge_pairs = []
    for slot in range(2):
        edge_pairs.append(
            [
                (i, i ^ (1 << (high_bits[slot] if parity(i) else low_bits[slot])))
                for i in range(acq_size)
            ]
        )
    def finish(focused, arrived, chunk):
        looked = cross_looks(focused, arrived)
        returned = [
            lax.ppermute(looked[slot], "acq", [(dst, src) for src, dst in edge_pairs[slot]])
            for slot in range(2)
        ]
        candidates = []
        for slot in range(2):
            recv_bit = jnp.where(me_parity == 1, low_bits[slot], high_bits[slot])
            send_bit = jnp.where(me_parity == 1, high_bits[slot], low_bits[slot])
            candidates.append((recv_bit, looked[slot]))
            back = returned[slot]
            candidates.append((send_bit, jnp.stack([back[0], -back[1]])))
        for slot in range(2):
            pick = candidates[0][1]
            for bit, value in candidates[1:]:
                pick = jnp.where(chosen[slot] == bit, value, pick)
            looks[slot].append(pick)

    looks = [[], []]
    previous = None
    for chunk in range(CHUNKS):
        piece = pieces[chunk].reshape(2, devices * chunk_cells, pulses_dev)
        if previous is not None:
            previous, piece = lax.optimization_barrier((previous, piece))
            arrived = [lax.ppermute(previous, "acq", pairs) for pairs in edge_pairs]
            finish(previous, arrived, chunk - 1)
        turned = lax.all_to_all(piece, "pulse", split_axis=1, concat_axis=2, tiled=True)
        rate = azimuth_rate[chunk * chunk_cells : (chunk + 1) * chunk_cells]
        previous = azimuth(turned, rate).astype(jnp.bfloat16)
    arrived = [lax.ppermute(previous, "acq", pairs) for pairs in edge_pairs]
    finish(previous, arrived, CHUNKS - 1)
    results = [jnp.concatenate(parts, axis=1) for parts in looks]

    interfere_real = jnp.stack([item[0] for item in results])[None]
    interfere_imag = jnp.stack([item[1] for item in results])[None]
    return (interfere_real, interfere_imag)


def solution(mesh):
    in_specs = (P("acq", None, "pulse", None), P(), P("acq"), P("pulse"), P("acq", None))
    out_specs = (P("acq", None, "pulse", None), P("acq", None, "pulse", None))
    return jax.shard_map(
        per_device, mesh=mesh, in_specs=in_specs, out_specs=out_specs, check_vma=False
    )
```

```python
import math

import jax
import jax.numpy as jnp
from jax import lax
from jax.experimental import pallas as pl
from jax.experimental.pallas import tpu as pltpu
from jax.sharding import PartitionSpec as P

RNG = 512
TAPS = 1024
LOOK_RNG = 4
LOOK_AZ = 16


def part_tables(length, inverse):
    steps = jnp.arange(length, dtype=jnp.int32)
    angle = 2.0 * jnp.pi * (steps[:, None] * steps[None, :] % length).astype(jnp.float32) / length
    cosine = jnp.cos(angle)
    sine = jnp.sin(angle)
    if inverse:
        sine = -sine
    return jnp.stack([jnp.stack([cosine, -sine]), jnp.stack([sine, cosine])])


def complex_product(left_re, left_im, right_re, right_im):
    return (left_re * right_re - left_im * right_im, left_re * right_im + left_im * right_re)


def band_kernel(re_ref, im_ref, band_ref):
    block = band_ref.shape[2]
    width = band_ref.shape[3]
    span = re_ref.shape[1]
    re_band = pltpu.roll(jnp.broadcast_to(re_ref[0:1, :], (block, span)), 0, 1, stride=1, stride_axis=0)
    im_band = pltpu.roll(jnp.broadcast_to(im_ref[0:1, :], (block, span)), 0, 1, stride=1, stride_axis=0)
    band_ref[0, 0] = re_band[:, :width].astype(band_ref.dtype)
    band_ref[0, 1] = (-im_band)[:, :width].astype(band_ref.dtype)
    band_ref[1, 0] = im_band[:, :width].astype(band_ref.dtype)
    band_ref[1, 1] = re_band[:, :width].astype(band_ref.dtype)


def band_tables(table_re, table_im, width):
    span = -(-(width + 1) // 128) * 128
    block = 128
    steps = RNG // block
    pad = jnp.zeros((span - table_re.shape[0],), jnp.float32)
    rows = []
    for table in (table_re, table_im):
        row = jnp.concatenate([table.astype(jnp.float32), pad])
        shifted = jnp.stack([jnp.roll(row, block * step) for step in range(steps)])
        rows.append(jnp.repeat(shifted, 8, axis=0))
    row_spec = pl.BlockSpec((8, span), lambda i: (i, 0))
    out_spec = pl.BlockSpec((2, 2, block, width), lambda i: (0, 0, i, 0))
    shape = jax.ShapeDtypeStruct((2, 2, RNG, width), jnp.bfloat16)
    band = pl.pallas_call(
        band_kernel,
        grid=(steps,),
        in_specs=[row_spec, row_spec],
        out_specs=out_spec,
        out_shape=shape,
    )(*rows)
    return band.reshape(2, 2 * RNG, width)


def compress(echoes, band, first_pulse, live_pulses):
    pulse_rows = echoes.shape[1]
    dims = (((0, 2), (0, 2)), ((), ()))
    result = lax.dot_general(band, echoes, dims, preferred_element_type=jnp.float32)
    joined = result.reshape(2, RNG, pulse_rows)
    pulse_ids = first_pulse + jnp.arange(pulse_rows, dtype=jnp.int32)
    keep = (pulse_ids < live_pulses).astype(jnp.float32)
    return (joined * keep[None, None, :]).astype(jnp.bfloat16)


def azimuth(turned, azimuth_rate):
    columns = turned.shape[1]
    length = turned.shape[2]
    outer_len = 64
    inner_len = length // outer_len
    highest = lax.Precision.HIGHEST
    signal = turned.astype(jnp.float32).reshape(2, columns, outer_len, inner_len)
    section_one = jnp.einsum(
        "pcab,pqak->qckb", signal, part_tables(outer_len, False), precision=highest
    )
    outer_ids = jnp.arange(outer_len, dtype=jnp.int32)
    inner_ids = jnp.arange(inner_len, dtype=jnp.int32)
    twist = (
        2.0
        * jnp.pi
        * (outer_ids[:, None] * inner_ids[None, :] % length).astype(jnp.float32)
        / length
    )
    twist_cos = jnp.cos(twist)
    twist_sin = jnp.sin(twist)
    turned_re, turned_im = complex_product(section_one[0], section_one[1], twist_cos, -twist_sin)
    spectrum = jnp.einsum(
        "pckb,pqbm->qckm",
        jnp.stack([turned_re, turned_im]),
        part_tables(inner_len, False),
        precision=highest,
    )
    freq_index = outer_ids[:, None] + outer_len * inner_ids[None, :]
    signed = jnp.where(freq_index < length // 2, freq_index, freq_index - length).astype(
        jnp.float32
    )
    quad = signed * signed / length
    phase = (jnp.pi * azimuth_rate)[:, None, None] * quad[None, :, :]
    filt_re, filt_im = complex_product(spectrum[0], spectrum[1], jnp.cos(phase), -jnp.sin(phase))
    back_one = jnp.einsum(
        "pckm,pqmb->qckb",
        jnp.stack([filt_re, filt_im]),
        part_tables(inner_len, True),
        precision=highest,
    )
    undo_re, undo_im = complex_product(back_one[0], back_one[1], twist_cos, twist_sin)
    restored = jnp.einsum(
        "pckb,pqka->qcab",
        jnp.stack([undo_re, undo_im]),
        part_tables(outer_len, True),
        precision=highest,
    )
    return (restored / length).reshape(2, columns, length)


def parity(index):
    return bin(index).count("1") % 2


def multilook(stacked):
    count, columns, pulse_len = stacked.shape
    inner = 128
    shaped = stacked.reshape(count, columns // LOOK_RNG, LOOK_RNG, pulse_len // inner, inner)
    summed = jnp.sum(shaped, axis=2)
    lanes = jnp.arange(inner, dtype=jnp.int32)
    groups = jnp.arange(inner // LOOK_AZ, dtype=jnp.int32)
    pool = (lanes[:, None] // LOOK_AZ == groups[None, :]).astype(jnp.float32)
    looked = jnp.einsum("nrab,bg->nrag", summed, pool, precision=lax.Precision.HIGHEST)
    scale = 1.0 / (LOOK_RNG * LOOK_AZ)
    return looked.reshape(count, columns // LOOK_RNG, pulse_len // LOOK_AZ) * scale


def cross_looks(own_block, partners):
    own_f = own_block.astype(jnp.float32)
    prods = []
    for partner in partners:
        other_f = partner.astype(jnp.float32)
        prods.append(own_f[0] * other_f[0] + own_f[1] * other_f[1])
        prods.append(own_f[1] * other_f[0] - own_f[0] * other_f[1])
    looked = multilook(jnp.stack(prods))
    return looked.reshape(len(partners), 2, *looked.shape[1:])


def per_device(raw_echo, chirp_phase, pulse_counts, azimuth_rate, partner_bits):
    echoes = raw_echo[0]
    pulses_dev = echoes.shape[1]
    amplitude = 2.0 / math.sqrt(TAPS)
    table_re = (amplitude * jnp.cos(chirp_phase)).astype(jnp.bfloat16)
    table_im = (amplitude * jnp.sin(chirp_phase)).astype(jnp.bfloat16)
    band = band_tables(table_re, table_im, echoes.shape[2])
    live_pulses = pulse_counts[0]
    first_pulse = lax.axis_index("pulse") * pulses_dev
    compressed = compress(echoes, band, first_pulse, live_pulses)
    chosen = partner_bits[0]
    acq_size = lax.axis_size("acq")
    me = lax.axis_index("acq")
    me_parity = jnp.int32(0)
    for which in range(acq_size.bit_length() - 1):
        me_parity = me_parity ^ ((me >> which) & 1)
    low_bits = (0, 1)
    high_bits = (2, 3)
    edge_pairs = []
    for slot in range(2):
        edge_pairs.append(
            [
                (i, i ^ (1 << (high_bits[slot] if parity(i) else low_bits[slot])))
                for i in range(acq_size)
            ]
        )
    cand_bits = []
    for slot in range(2):
        cand_bits.append(jnp.where(me_parity == 1, low_bits[slot], high_bits[slot]))
        cand_bits.append(jnp.where(me_parity == 1, high_bits[slot], low_bits[slot]))
    masks = jnp.stack([jnp.stack([chosen[slot] == bit for bit in cand_bits]) for slot in range(2)])
    masks, compressed = lax.optimization_barrier((masks, compressed))
    turned = lax.all_to_all(compressed, "pulse", split_axis=1, concat_axis=2, tiled=True)
    focused = azimuth(turned, azimuth_rate).astype(jnp.bfloat16)
    arrived = [lax.ppermute(focused, "acq", pairs) for pairs in edge_pairs]
    looked = cross_looks(focused, arrived)
    returned = [
        lax.ppermute(looked[slot], "acq", [(dst, src) for src, dst in edge_pairs[slot]])
        for slot in range(2)
    ]
    candidates = []
    for slot in range(2):
        candidates.append(looked[slot])
        back = returned[slot]
        candidates.append(jnp.stack([back[0], -back[1]]))
    results = []
    for slot in range(2):
        pick = candidates[0]
        for index in range(1, len(candidates)):
            pick = jnp.where(masks[slot, index], candidates[index], pick)
        results.append(pick)
    interfere_real = jnp.stack([item[0] for item in results])[None]
    interfere_imag = jnp.stack([item[1] for item in results])[None]
    return (interfere_real, interfere_imag)


def solution(mesh):
    in_specs = (P("acq", None, "pulse", None), P(), P("acq"), P("pulse"), P("acq", None))
    out_specs = (P("acq", None, "pulse", None), P("acq", None, "pulse", None))
    return jax.shard_map(
        per_device, mesh=mesh, in_specs=in_specs, out_specs=out_specs, check_vma=False
    )
```

```python
import math

import jax
import jax.numpy as jnp
from jax import lax
from jax.experimental import pallas as pl
from jax.experimental.pallas import tpu as pltpu
from jax.sharding import PartitionSpec as P

RNG = 512
TAPS = 1024
LOOK_RNG = 4
LOOK_AZ = 16


def part_tables(length, inverse):
    steps = jnp.arange(length, dtype=jnp.int32)
    angle = 2.0 * jnp.pi * (steps[:, None] * steps[None, :] % length).astype(jnp.float32) / length
    cosine = jnp.cos(angle)
    sine = jnp.sin(angle)
    if inverse:
        sine = -sine
    return jnp.stack([jnp.stack([cosine, -sine]), jnp.stack([sine, cosine])])


def complex_product(left_re, left_im, right_re, right_im):
    return (left_re * right_re - left_im * right_im, left_re * right_im + left_im * right_re)


def band_kernel(re_ref, im_ref, band_ref):
    block = band_ref.shape[2]
    width = band_ref.shape[3]
    span = re_ref.shape[1]
    re_band = pltpu.roll(jnp.broadcast_to(re_ref[0:1, :], (block, span)), 0, 1, stride=1, stride_axis=0)
    im_band = pltpu.roll(jnp.broadcast_to(im_ref[0:1, :], (block, span)), 0, 1, stride=1, stride_axis=0)
    band_ref[0, 0] = re_band[:, :width].astype(band_ref.dtype)
    band_ref[0, 1] = (-im_band)[:, :width].astype(band_ref.dtype)
    band_ref[1, 0] = im_band[:, :width].astype(band_ref.dtype)
    band_ref[1, 1] = re_band[:, :width].astype(band_ref.dtype)


def band_tables(table_re, table_im, width):
    span = -(-(width + 1) // 128) * 128
    block = 128
    steps = RNG // block
    pad = jnp.zeros((span - table_re.shape[0],), jnp.float32)
    rows = []
    for table in (table_re, table_im):
        row = jnp.concatenate([table.astype(jnp.float32), pad])
        shifted = jnp.stack([jnp.roll(row, block * step) for step in range(steps)])
        rows.append(jnp.repeat(shifted, 8, axis=0))
    row_spec = pl.BlockSpec((8, span), lambda i: (i, 0))
    out_spec = pl.BlockSpec((2, 2, block, width), lambda i: (0, 0, i, 0))
    shape = jax.ShapeDtypeStruct((2, 2, RNG, width), jnp.bfloat16)
    band = pl.pallas_call(
        band_kernel,
        grid=(steps,),
        in_specs=[row_spec, row_spec],
        out_specs=out_spec,
        out_shape=shape,
    )(*rows)
    return band.reshape(2, 2 * RNG, width)


def compress(echoes, band, first_pulse, live_pulses):
    pulse_rows = echoes.shape[1]
    dims = (((0, 2), (0, 2)), ((), ()))
    result = lax.dot_general(band, echoes, dims, preferred_element_type=jnp.float32)
    joined = result.reshape(2, RNG, pulse_rows)
    pulse_ids = first_pulse + jnp.arange(pulse_rows, dtype=jnp.int32)
    keep = (pulse_ids < live_pulses).astype(jnp.float32)
    return (joined * keep[None, None, :]).astype(jnp.bfloat16)


def azimuth(turned, azimuth_rate):
    columns = turned.shape[1]
    length = turned.shape[2]
    outer_len = 64
    inner_len = length // outer_len
    highest = lax.Precision.HIGHEST
    signal = turned.astype(jnp.float32).reshape(2, columns, outer_len, inner_len)
    section_one = jnp.einsum(
        "pcab,pqak->qckb", signal, part_tables(outer_len, False), precision=highest
    )
    outer_ids = jnp.arange(outer_len, dtype=jnp.int32)
    inner_ids = jnp.arange(inner_len, dtype=jnp.int32)
    twist = (
        2.0
        * jnp.pi
        * (outer_ids[:, None] * inner_ids[None, :] % length).astype(jnp.float32)
        / length
    )
    twist_cos = jnp.cos(twist)
    twist_sin = jnp.sin(twist)
    turned_re, turned_im = complex_product(section_one[0], section_one[1], twist_cos, -twist_sin)
    spectrum = jnp.einsum(
        "pckb,pqbm->qckm",
        jnp.stack([turned_re, turned_im]),
        part_tables(inner_len, False),
        precision=highest,
    )
    freq_index = outer_ids[:, None] + outer_len * inner_ids[None, :]
    signed = jnp.where(freq_index < length // 2, freq_index, freq_index - length).astype(
        jnp.float32
    )
    quad = signed * signed / length
    phase = (jnp.pi * azimuth_rate)[:, None, None] * quad[None, :, :]
    filt_re, filt_im = complex_product(spectrum[0], spectrum[1], jnp.cos(phase), -jnp.sin(phase))
    back_one = jnp.einsum(
        "pckm,pqmb->qckb",
        jnp.stack([filt_re, filt_im]),
        part_tables(inner_len, True),
        precision=highest,
    )
    undo_re, undo_im = complex_product(back_one[0], back_one[1], twist_cos, twist_sin)
    restored = jnp.einsum(
        "pckb,pqka->qcab",
        jnp.stack([undo_re, undo_im]),
        part_tables(outer_len, True),
        precision=highest,
    )
    return (restored / length).reshape(2, columns, length)


def parity(index):
    return bin(index).count("1") % 2


def multilook(stacked):
    count, columns, pulse_len = stacked.shape
    inner = 128
    shaped = stacked.reshape(count, columns // LOOK_RNG, LOOK_RNG, pulse_len // inner, inner)
    summed = jnp.sum(shaped, axis=2)
    lanes = jnp.arange(inner, dtype=jnp.int32)
    groups = jnp.arange(inner // LOOK_AZ, dtype=jnp.int32)
    pool = (lanes[:, None] // LOOK_AZ == groups[None, :]).astype(jnp.float32)
    looked = jnp.einsum("nrab,bg->nrag", summed, pool, precision=lax.Precision.HIGHEST)
    scale = 1.0 / (LOOK_RNG * LOOK_AZ)
    return looked.reshape(count, columns // LOOK_RNG, pulse_len // LOOK_AZ) * scale


def cross_looks(own_block, partners):
    own_f = own_block.astype(jnp.float32)
    prods = []
    for partner in partners:
        other_f = partner.astype(jnp.float32)
        prods.append(own_f[0] * other_f[0] + own_f[1] * other_f[1])
        prods.append(own_f[1] * other_f[0] - own_f[0] * other_f[1])
    looked = multilook(jnp.stack(prods))
    return looked.reshape(len(partners), 2, *looked.shape[1:])


def per_device(raw_echo, chirp_phase, pulse_counts, azimuth_rate, partner_bits):
    echoes = raw_echo[0]
    pulses_dev = echoes.shape[1]
    devices = lax.axis_size("pulse")
    warm = jnp.broadcast_to(azimuth_rate[:1], (devices, 128))
    warm = lax.all_to_all(warm, "pulse", 0, 0, tiled=True)
    amplitude = 2.0 / math.sqrt(TAPS)
    table_re = (amplitude * jnp.cos(chirp_phase)).astype(jnp.bfloat16)
    table_im = (amplitude * jnp.sin(chirp_phase)).astype(jnp.bfloat16)
    band = band_tables(table_re, table_im, echoes.shape[2])
    live_pulses = pulse_counts[0]
    first_pulse = lax.axis_index("pulse") * pulses_dev
    compressed = compress(echoes, band, first_pulse, live_pulses)
    warm, compressed = lax.optimization_barrier((warm, compressed))
    live_rate = azimuth_rate + 0.0 * warm[0, 0]
    turned = lax.all_to_all(compressed, "pulse", split_axis=1, concat_axis=2, tiled=True)
    focused = azimuth(turned, live_rate).astype(jnp.bfloat16)
    chosen = partner_bits[0]
    acq_size = lax.axis_size("acq")
    me = lax.axis_index("acq")
    me_parity = jnp.int32(0)
    for which in range(acq_size.bit_length() - 1):
        me_parity = me_parity ^ ((me >> which) & 1)
    low_bits = (0, 1)
    high_bits = (2, 3)
    edge_pairs = []
    for slot in range(2):
        edge_pairs.append(
            [
                (i, i ^ (1 << (high_bits[slot] if parity(i) else low_bits[slot])))
                for i in range(acq_size)
            ]
        )
    arrived = [lax.ppermute(focused, "acq", pairs) for pairs in edge_pairs]
    looked = cross_looks(focused, arrived)
    returned = [
        lax.ppermute(looked[slot], "acq", [(dst, src) for src, dst in edge_pairs[slot]])
        for slot in range(2)
    ]
    candidates = []
    for slot in range(2):
        recv_bit = jnp.where(me_parity == 1, low_bits[slot], high_bits[slot])
        send_bit = jnp.where(me_parity == 1, high_bits[slot], low_bits[slot])
        candidates.append((recv_bit, looked[slot]))
        back = returned[slot]
        candidates.append((send_bit, jnp.stack([back[0], -back[1]])))
    results = []
    for slot in range(2):
        pick = candidates[0][1]
        for bit, value in candidates[1:]:
            pick = jnp.where(chosen[slot] == bit, value, pick)
        results.append(pick)
    interfere_real = jnp.stack([item[0] for item in results])[None]
    interfere_imag = jnp.stack([item[1] for item in results])[None]
    return (interfere_real, interfere_imag)


def solution(mesh):
    in_specs = (P("acq", None, "pulse", None), P(), P("acq"), P("pulse"), P("acq", None))
    out_specs = (P("acq", None, "pulse", None), P("acq", None, "pulse", None))
    return jax.shard_map(
        per_device, mesh=mesh, in_specs=in_specs, out_specs=out_specs, check_vma=False
    )
```

```python
import math

import jax
import jax.numpy as jnp
from jax import lax
from jax.experimental import pallas as pl
from jax.experimental.pallas import tpu as pltpu
from jax.sharding import PartitionSpec as P

RNG = 512
TAPS = 1024
LOOK_RNG = 4
LOOK_AZ = 16


def part_tables(length, inverse):
    steps = jnp.arange(length, dtype=jnp.int32)
    angle = 2.0 * jnp.pi * (steps[:, None] * steps[None, :] % length).astype(jnp.float32) / length
    cosine = jnp.cos(angle)
    sine = jnp.sin(angle)
    if inverse:
        sine = -sine
    return jnp.stack([jnp.stack([cosine, -sine]), jnp.stack([sine, cosine])])


def complex_product(left_re, left_im, right_re, right_im):
    return (left_re * right_re - left_im * right_im, left_re * right_im + left_im * right_re)


def band_kernel(re_ref, im_ref, band_ref):
    block = band_ref.shape[2]
    width = band_ref.shape[3]
    span = re_ref.shape[1]
    re_band = pltpu.roll(jnp.broadcast_to(re_ref[0:1, :], (block, span)), 0, 1, stride=1, stride_axis=0)
    im_band = pltpu.roll(jnp.broadcast_to(im_ref[0:1, :], (block, span)), 0, 1, stride=1, stride_axis=0)
    band_ref[0, 0] = re_band[:, :width].astype(band_ref.dtype)
    band_ref[0, 1] = (-im_band)[:, :width].astype(band_ref.dtype)
    band_ref[1, 0] = im_band[:, :width].astype(band_ref.dtype)
    band_ref[1, 1] = re_band[:, :width].astype(band_ref.dtype)


def band_tables(table_re, table_im, width):
    span = -(-(width + 1) // 128) * 128
    block = 128
    steps = RNG // block
    pad = jnp.zeros((span - table_re.shape[0],), jnp.float32)
    rows = []
    for table in (table_re, table_im):
        row = jnp.concatenate([table.astype(jnp.float32), pad])
        shifted = jnp.stack([jnp.roll(row, block * step) for step in range(steps)])
        rows.append(jnp.repeat(shifted, 8, axis=0))
    row_spec = pl.BlockSpec((8, span), lambda i: (i, 0))
    out_spec = pl.BlockSpec((2, 2, block, width), lambda i: (0, 0, i, 0))
    shape = jax.ShapeDtypeStruct((2, 2, RNG, width), jnp.bfloat16)
    band = pl.pallas_call(
        band_kernel,
        grid=(steps,),
        in_specs=[row_spec, row_spec],
        out_specs=out_spec,
        out_shape=shape,
    )(*rows)
    return band.reshape(2, 2 * RNG, width)


def compress(echoes, band, first_pulse, live_pulses):
    pulse_rows = echoes.shape[1]
    dims = (((0, 2), (0, 2)), ((), ()))
    result = lax.dot_general(band, echoes, dims, preferred_element_type=jnp.float32)
    joined = result.reshape(2, RNG, pulse_rows)
    pulse_ids = first_pulse + jnp.arange(pulse_rows, dtype=jnp.int32)
    keep = (pulse_ids < live_pulses).astype(jnp.float32)
    return (joined * keep[None, None, :]).astype(jnp.bfloat16)


def azimuth(turned, azimuth_rate):
    columns = turned.shape[1]
    length = turned.shape[2]
    outer_len = 64
    inner_len = length // outer_len
    highest = lax.Precision.HIGHEST
    signal = turned.astype(jnp.float32).reshape(2, columns, outer_len, inner_len)
    section_one = jnp.einsum(
        "pcab,pqak->qckb", signal, part_tables(outer_len, False), precision=highest
    )
    outer_ids = jnp.arange(outer_len, dtype=jnp.int32)
    inner_ids = jnp.arange(inner_len, dtype=jnp.int32)
    twist = (
        2.0
        * jnp.pi
        * (outer_ids[:, None] * inner_ids[None, :] % length).astype(jnp.float32)
        / length
    )
    twist_cos = jnp.cos(twist)
    twist_sin = jnp.sin(twist)
    turned_re, turned_im = complex_product(section_one[0], section_one[1], twist_cos, -twist_sin)
    spectrum = jnp.einsum(
        "pckb,pqbm->qckm",
        jnp.stack([turned_re, turned_im]),
        part_tables(inner_len, False),
        precision=highest,
    )
    freq_index = outer_ids[:, None] + outer_len * inner_ids[None, :]
    signed = jnp.where(freq_index < length // 2, freq_index, freq_index - length).astype(
        jnp.float32
    )
    quad = signed * signed / length
    phase = (jnp.pi * azimuth_rate)[:, None, None] * quad[None, :, :]
    filt_re, filt_im = complex_product(spectrum[0], spectrum[1], jnp.cos(phase), -jnp.sin(phase))
    back_one = jnp.einsum(
        "pckm,pqmb->qckb",
        jnp.stack([filt_re, filt_im]),
        part_tables(inner_len, True),
        precision=highest,
    )
    undo_re, undo_im = complex_product(back_one[0], back_one[1], twist_cos, twist_sin)
    restored = jnp.einsum(
        "pckb,pqka->qcab",
        jnp.stack([undo_re, undo_im]),
        part_tables(outer_len, True),
        precision=highest,
    )
    return (restored / length).reshape(2, columns, length)


def parity(index):
    return bin(index).count("1") % 2


def multilook(stacked):
    count, columns, pulse_len = stacked.shape
    inner = 128
    shaped = stacked.reshape(count, columns // LOOK_RNG, LOOK_RNG, pulse_len // inner, inner)
    summed = jnp.sum(shaped, axis=2)
    lanes = jnp.arange(inner, dtype=jnp.int32)
    groups = jnp.arange(inner // LOOK_AZ, dtype=jnp.int32)
    pool = (lanes[:, None] // LOOK_AZ == groups[None, :]).astype(jnp.float32)
    looked = jnp.einsum("nrab,bg->nrag", summed, pool, precision=lax.Precision.HIGHEST)
    scale = 1.0 / (LOOK_RNG * LOOK_AZ)
    return looked.reshape(count, columns // LOOK_RNG, pulse_len // LOOK_AZ) * scale


def cross_looks(own_block, partners):
    own_f = own_block.astype(jnp.float32)
    prods = []
    for partner in partners:
        other_f = partner.astype(jnp.float32)
        prods.append(own_f[0] * other_f[0] + own_f[1] * other_f[1])
        prods.append(own_f[1] * other_f[0] - own_f[0] * other_f[1])
    looked = multilook(jnp.stack(prods))
    return looked.reshape(len(partners), 2, *looked.shape[1:])


def per_device(raw_echo, chirp_phase, pulse_counts, azimuth_rate, partner_bits):
    echoes = raw_echo[0]
    pulses_dev = echoes.shape[1]
    amplitude = 2.0 / math.sqrt(TAPS)
    table_re = (amplitude * jnp.cos(chirp_phase)).astype(jnp.bfloat16)
    table_im = (amplitude * jnp.sin(chirp_phase)).astype(jnp.bfloat16)
    band = band_tables(table_re, table_im, echoes.shape[2])
    live_pulses = pulse_counts[0]
    first_pulse = lax.axis_index("pulse") * pulses_dev
    compressed = compress(echoes, band, first_pulse, live_pulses)
    chosen = partner_bits[0]
    acq_size = lax.axis_size("acq")
    me = lax.axis_index("acq")
    me_parity = jnp.int32(0)
    for which in range(acq_size.bit_length() - 1):
        me_parity = me_parity ^ ((me >> which) & 1)
    low_bits = (0, 1)
    high_bits = (2, 3)
    edge_pairs = []
    for slot in range(2):
        edge_pairs.append(
            [
                (i, i ^ (1 << (high_bits[slot] if parity(i) else low_bits[slot])))
                for i in range(acq_size)
            ]
        )
    cand_bits = []
    for slot in range(2):
        cand_bits.append(jnp.where(me_parity == 1, low_bits[slot], high_bits[slot]))
        cand_bits.append(jnp.where(me_parity == 1, high_bits[slot], low_bits[slot]))
    preds = tuple(chosen[slot] == bit for slot in range(2) for bit in cand_bits)
    turned = lax.all_to_all(compressed, "pulse", split_axis=1, concat_axis=2, tiled=True)
    *preds, turned = lax.optimization_barrier((*preds, turned))
    focused = azimuth(turned, azimuth_rate).astype(jnp.bfloat16)
    arrived = [lax.ppermute(focused, "acq", pairs) for pairs in edge_pairs]
    looked = cross_looks(focused, arrived)
    returned = [
        lax.ppermute(looked[slot], "acq", [(dst, src) for src, dst in edge_pairs[slot]])
        for slot in range(2)
    ]
    candidates = []
    for slot in range(2):
        candidates.append(looked[slot])
        back = returned[slot]
        candidates.append(jnp.stack([back[0], -back[1]]))
    results = []
    for slot in range(2):
        pick = candidates[0]
        for index in range(1, len(candidates)):
            pick = jnp.where(preds[slot * len(candidates) + index], candidates[index], pick)
        results.append(pick)
    interfere_real = jnp.stack([item[0] for item in results])[None]
    interfere_imag = jnp.stack([item[1] for item in results])[None]
    return (interfere_real, interfere_imag)


def solution(mesh):
    in_specs = (P("acq", None, "pulse", None), P(), P("acq"), P("pulse"), P("acq", None))
    out_specs = (P("acq", None, "pulse", None), P("acq", None, "pulse", None))
    return jax.shard_map(
        per_device, mesh=mesh, in_specs=in_specs, out_specs=out_specs, check_vma=False
    )
```

```python
import math

import jax
import jax.numpy as jnp
from jax import lax
from jax.experimental import pallas as pl
from jax.experimental.pallas import tpu as pltpu
from jax.sharding import PartitionSpec as P

RNG = 512
TAPS = 1024
LOOK_RNG = 4
LOOK_AZ = 16
BAND_ROWS = 128


def part_tables(length, inverse):
    steps = jnp.arange(length, dtype=jnp.int32)
    angle = 2.0 * jnp.pi * (steps[:, None] * steps[None, :] % length).astype(jnp.float32) / length
    cosine = jnp.cos(angle)
    sine = jnp.sin(angle)
    if inverse:
        sine = -sine
    return jnp.stack([jnp.stack([cosine, -sine]), jnp.stack([sine, cosine])])


def complex_product(left_re, left_im, right_re, right_im):
    return (left_re * right_re - left_im * right_im, left_re * right_im + left_im * right_re)


def band_kernel(re_ref, im_ref, band_ref):
    rows = BAND_ROWS
    strip = re_ref.shape[1]
    width = band_ref.shape[3]
    dtype = band_ref.dtype
    re_strip = pltpu.roll(jnp.broadcast_to(re_ref[...], (rows, strip)), 0, 1, stride=1, stride_axis=0)
    im_strip = pltpu.roll(jnp.broadcast_to(im_ref[...], (rows, strip)), 0, 1, stride=1, stride_axis=0)
    pieces = (
        (0, 0, re_strip.astype(dtype)),
        (0, 1, (-im_strip).astype(dtype)),
        (1, 0, im_strip.astype(dtype)),
        (1, 1, re_strip.astype(dtype)),
    )
    for start in range(0, band_ref.shape[2], rows):
        stop = min(start + strip, width)
        for part, half, values in pieces:
            band_ref[part, half, start : start + rows, start:stop] = values[:, : stop - start]
            if start > 0:
                band_ref[part, half, start : start + rows, :start] = jnp.zeros((rows, start), dtype)
            if stop < width:
                band_ref[part, half, start : start + rows, stop:] = jnp.zeros((rows, width - stop), dtype)


def band_tables(table_re, table_im, width):
    rows = BAND_ROWS
    strip = -(-(TAPS + rows - 1) // 128) * 128
    pad = jnp.zeros((strip - table_re.shape[0],), jnp.float32)
    re_row = jnp.concatenate([table_re.astype(jnp.float32), pad])[None]
    im_row = jnp.concatenate([table_im.astype(jnp.float32), pad])[None]
    shape = jax.ShapeDtypeStruct((2, 2, RNG, width), jnp.bfloat16)
    band = pl.pallas_call(band_kernel, out_shape=shape)(re_row, im_row)
    return band.reshape(2, 2 * RNG, width)


def compress(echoes, band, first_pulse, live_pulses):
    pulse_rows = echoes.shape[1]
    dims = (((0, 2), (0, 2)), ((), ()))
    result = lax.dot_general(band, echoes, dims, preferred_element_type=jnp.float32)
    joined = result.reshape(2, RNG, pulse_rows)
    pulse_ids = first_pulse + jnp.arange(pulse_rows, dtype=jnp.int32)
    keep = (pulse_ids < live_pulses).astype(jnp.float32)
    return (joined * keep[None, None, :]).astype(jnp.bfloat16)


def azimuth(turned, azimuth_rate):
    columns = turned.shape[1]
    length = turned.shape[2]
    outer_len = 64
    inner_len = length // outer_len
    highest = lax.Precision.HIGHEST
    signal = turned.astype(jnp.float32).reshape(2, columns, outer_len, inner_len)
    section_one = jnp.einsum(
        "pcab,pqak->qckb", signal, part_tables(outer_len, False), precision=highest
    )
    outer_ids = jnp.arange(outer_len, dtype=jnp.int32)
    inner_ids = jnp.arange(inner_len, dtype=jnp.int32)
    twist = (
        2.0
        * jnp.pi
        * (outer_ids[:, None] * inner_ids[None, :] % length).astype(jnp.float32)
        / length
    )
    twist_cos = jnp.cos(twist)
    twist_sin = jnp.sin(twist)
    turned_re, turned_im = complex_product(section_one[0], section_one[1], twist_cos, -twist_sin)
    spectrum = jnp.einsum(
        "pckb,pqbm->qckm",
        jnp.stack([turned_re, turned_im]),
        part_tables(inner_len, False),
        precision=highest,
    )
    freq_index = outer_ids[:, None] + outer_len * inner_ids[None, :]
    signed = jnp.where(freq_index < length // 2, freq_index, freq_index - length).astype(
        jnp.float32
    )
    quad = signed * signed / length
    phase = (jnp.pi * azimuth_rate)[:, None, None] * quad[None, :, :]
    filt_re, filt_im = complex_product(spectrum[0], spectrum[1], jnp.cos(phase), -jnp.sin(phase))
    back_one = jnp.einsum(
        "pckm,pqmb->qckb",
        jnp.stack([filt_re, filt_im]),
        part_tables(inner_len, True),
        precision=highest,
    )
    undo_re, undo_im = complex_product(back_one[0], back_one[1], twist_cos, twist_sin)
    restored = jnp.einsum(
        "pckb,pqka->qcab",
        jnp.stack([undo_re, undo_im]),
        part_tables(outer_len, True),
        precision=highest,
    )
    return (restored / length).reshape(2, columns, length)


def parity(index):
    return bin(index).count("1") % 2


def multilook(stacked):
    count, columns, pulse_len = stacked.shape
    inner = 128
    shaped = stacked.reshape(count, columns // LOOK_RNG, LOOK_RNG, pulse_len // inner, inner)
    summed = jnp.sum(shaped, axis=2)
    lanes = jnp.arange(inner, dtype=jnp.int32)
    groups = jnp.arange(inner // LOOK_AZ, dtype=jnp.int32)
    pool = (lanes[:, None] // LOOK_AZ == groups[None, :]).astype(jnp.float32)
    looked = jnp.einsum("nrab,bg->nrag", summed, pool, precision=lax.Precision.HIGHEST)
    scale = 1.0 / (LOOK_RNG * LOOK_AZ)
    return looked.reshape(count, columns // LOOK_RNG, pulse_len // LOOK_AZ) * scale


def cross_looks(own_block, partners):
    own_f = own_block.astype(jnp.float32)
    prods = []
    for partner in partners:
        other_f = partner.astype(jnp.float32)
        prods.append(own_f[0] * other_f[0] + own_f[1] * other_f[1])
        prods.append(own_f[1] * other_f[0] - own_f[0] * other_f[1])
    looked = multilook(jnp.stack(prods))
    return looked.reshape(len(partners), 2, *looked.shape[1:])


def per_device(raw_echo, chirp_phase, pulse_counts, azimuth_rate, partner_bits):
    echoes = raw_echo[0]
    pulses_dev = echoes.shape[1]
    amplitude = 2.0 / math.sqrt(TAPS)
    table_re = (amplitude * jnp.cos(chirp_phase)).astype(jnp.bfloat16)
    table_im = (amplitude * jnp.sin(chirp_phase)).astype(jnp.bfloat16)
    band = band_tables(table_re, table_im, echoes.shape[2])
    live_pulses = pulse_counts[0]
    first_pulse = lax.axis_index("pulse") * pulses_dev
    compressed = compress(echoes, band, first_pulse, live_pulses)
    chosen = partner_bits[0]
    acq_size = lax.axis_size("acq")
    me = lax.axis_index("acq")
    me_parity = jnp.int32(0)
    for which in range(acq_size.bit_length() - 1):
        me_parity = me_parity ^ ((me >> which) & 1)
    low_bits = (0, 1)
    high_bits = (2, 3)
    edge_pairs = []
    for slot in range(2):
        edge_pairs.append(
            [
                (i, i ^ (1 << (high_bits[slot] if parity(i) else low_bits[slot])))
                for i in range(acq_size)
            ]
        )
    cand_bits = []
    for slot in range(2):
        cand_bits.append(jnp.where(me_parity == 1, low_bits[slot], high_bits[slot]))
        cand_bits.append(jnp.where(me_parity == 1, high_bits[slot], low_bits[slot]))
    preds = tuple(chosen[slot] == bit for slot in range(2) for bit in cand_bits)
    turned = lax.all_to_all(compressed, "pulse", split_axis=1, concat_axis=2, tiled=True)
    *preds, turned = lax.optimization_barrier((*preds, turned))
    focused = azimuth(turned, azimuth_rate).astype(jnp.bfloat16)
    arrived = [lax.ppermute(focused, "acq", pairs) for pairs in edge_pairs]
    looked = cross_looks(focused, arrived)
    returned = [
        lax.ppermute(looked[slot], "acq", [(dst, src) for src, dst in edge_pairs[slot]])
        for slot in range(2)
    ]
    candidates = []
    for slot in range(2):
        candidates.append(looked[slot])
        back = returned[slot]
        candidates.append(jnp.stack([back[0], -back[1]]))
    results = []
    for slot in range(2):
        pick = candidates[0]
        for index in range(1, len(candidates)):
            pick = jnp.where(preds[slot * len(candidates) + index], candidates[index], pick)
        results.append(pick)
    interfere_real = jnp.stack([item[0] for item in results])[None]
    interfere_imag = jnp.stack([item[1] for item in results])[None]
    return (interfere_real, interfere_imag)


def solution(mesh):
    in_specs = (P("acq", None, "pulse", None), P(), P("acq"), P("pulse"), P("acq", None))
    out_specs = (P("acq", None, "pulse", None), P("acq", None, "pulse", None))
    return jax.shard_map(
        per_device, mesh=mesh, in_specs=in_specs, out_specs=out_specs, check_vma=False
    )
```

```python
import math

import jax
import jax.numpy as jnp
from jax import lax
from jax.experimental import pallas as pl
from jax.experimental.pallas import tpu as pltpu
from jax.sharding import PartitionSpec as P

RNG = 512
TAPS = 1024
LOOK_RNG = 4
LOOK_AZ = 16
BAND_ROWS = 128


def part_tables(length, inverse):
    steps = jnp.arange(length, dtype=jnp.int32)
    angle = 2.0 * jnp.pi * (steps[:, None] * steps[None, :] % length).astype(jnp.float32) / length
    cosine = jnp.cos(angle)
    sine = jnp.sin(angle)
    if inverse:
        sine = -sine
    return jnp.stack([jnp.stack([cosine, -sine]), jnp.stack([sine, cosine])])


def complex_product(left_re, left_im, right_re, right_im):
    return (left_re * right_re - left_im * right_im, left_re * right_im + left_im * right_re)


def band_kernel(re_ref, im_ref, band_ref):
    rows = BAND_ROWS
    strip = re_ref.shape[1]
    width = band_ref.shape[3]
    dtype = band_ref.dtype
    re_strip = pltpu.roll(jnp.broadcast_to(re_ref[...], (rows, strip)), 0, 1, stride=1, stride_axis=0)
    im_strip = pltpu.roll(jnp.broadcast_to(im_ref[...], (rows, strip)), 0, 1, stride=1, stride_axis=0)
    pieces = (
        (0, 0, re_strip.astype(dtype)),
        (0, 1, (-im_strip).astype(dtype)),
        (1, 0, im_strip.astype(dtype)),
        (1, 1, re_strip.astype(dtype)),
    )
    for start in range(0, band_ref.shape[2], rows):
        stop = min(start + strip, width)
        for part, half, values in pieces:
            band_ref[part, half, start : start + rows, start:stop] = values[:, : stop - start]
            if start > 0:
                band_ref[part, half, start : start + rows, :start] = jnp.zeros((rows, start), dtype)
            if stop < width:
                band_ref[part, half, start : start + rows, stop:] = jnp.zeros((rows, width - stop), dtype)


def band_tables(table_re, table_im, width):
    rows = BAND_ROWS
    strip = -(-(TAPS + rows - 1) // 128) * 128
    pad = jnp.zeros((strip - table_re.shape[0],), jnp.float32)
    re_row = jnp.concatenate([table_re.astype(jnp.float32), pad])[None]
    im_row = jnp.concatenate([table_im.astype(jnp.float32), pad])[None]
    shape = jax.ShapeDtypeStruct((2, 2, RNG, width), jnp.bfloat16)
    band = pl.pallas_call(band_kernel, out_shape=shape)(re_row, im_row)
    return band.reshape(2, 2 * RNG, width)


def compress(echoes, band, first_pulse, live_pulses):
    pulse_rows = echoes.shape[1]
    dims = (((0, 2), (0, 2)), ((), ()))
    result = lax.dot_general(band, echoes, dims, preferred_element_type=jnp.float32)
    joined = result.reshape(2, RNG, pulse_rows)
    pulse_ids = first_pulse + jnp.arange(pulse_rows, dtype=jnp.int32)
    keep = (pulse_ids < live_pulses).astype(jnp.float32)
    return (joined * keep[None, None, :]).astype(jnp.bfloat16)


def azimuth(turned, azimuth_rate):
    columns = turned.shape[1]
    length = turned.shape[2]
    outer_len = 64
    inner_len = length // outer_len
    highest = lax.Precision.HIGH
    signal = turned.astype(jnp.float32).reshape(2, columns, outer_len, inner_len)
    section_one = jnp.einsum(
        "pcab,pqak->qckb", signal, part_tables(outer_len, False), precision=highest
    )
    outer_ids = jnp.arange(outer_len, dtype=jnp.int32)
    inner_ids = jnp.arange(inner_len, dtype=jnp.int32)
    twist = (
        2.0
        * jnp.pi
        * (outer_ids[:, None] * inner_ids[None, :] % length).astype(jnp.float32)
        / length
    )
    twist_cos = jnp.cos(twist)
    twist_sin = jnp.sin(twist)
    turned_re, turned_im = complex_product(section_one[0], section_one[1], twist_cos, -twist_sin)
    spectrum = jnp.einsum(
        "pckb,pqbm->qckm",
        jnp.stack([turned_re, turned_im]),
        part_tables(inner_len, False),
        precision=highest,
    )
    freq_index = outer_ids[:, None] + outer_len * inner_ids[None, :]
    signed = jnp.where(freq_index < length // 2, freq_index, freq_index - length).astype(
        jnp.float32
    )
    quad = signed * signed / length
    phase = (jnp.pi * azimuth_rate)[:, None, None] * quad[None, :, :]
    filt_re, filt_im = complex_product(spectrum[0], spectrum[1], jnp.cos(phase), -jnp.sin(phase))
    back_one = jnp.einsum(
        "pckm,pqmb->qckb",
        jnp.stack([filt_re, filt_im]),
        part_tables(inner_len, True),
        precision=highest,
    )
    undo_re, undo_im = complex_product(back_one[0], back_one[1], twist_cos, twist_sin)
    restored = jnp.einsum(
        "pckb,pqka->qcab",
        jnp.stack([undo_re, undo_im]),
        part_tables(outer_len, True),
        precision=highest,
    )
    return (restored / length).reshape(2, columns, length)


def parity(index):
    return bin(index).count("1") % 2


def multilook(stacked):
    count, columns, pulse_len = stacked.shape
    inner = 128
    shaped = stacked.reshape(count, columns // LOOK_RNG, LOOK_RNG, pulse_len // inner, inner)
    summed = jnp.sum(shaped, axis=2)
    lanes = jnp.arange(inner, dtype=jnp.int32)
    groups = jnp.arange(inner // LOOK_AZ, dtype=jnp.int32)
    pool = (lanes[:, None] // LOOK_AZ == groups[None, :]).astype(jnp.float32)
    looked = jnp.einsum("nrab,bg->nrag", summed, pool, precision=lax.Precision.HIGHEST)
    scale = 1.0 / (LOOK_RNG * LOOK_AZ)
    return looked.reshape(count, columns // LOOK_RNG, pulse_len // LOOK_AZ) * scale


def cross_looks(own_block, partners):
    own_f = own_block.astype(jnp.float32)
    prods = []
    for partner in partners:
        other_f = partner.astype(jnp.float32)
        prods.append(own_f[0] * other_f[0] + own_f[1] * other_f[1])
        prods.append(own_f[1] * other_f[0] - own_f[0] * other_f[1])
    looked = multilook(jnp.stack(prods))
    return looked.reshape(len(partners), 2, *looked.shape[1:])


def per_device(raw_echo, chirp_phase, pulse_counts, azimuth_rate, partner_bits):
    echoes = raw_echo[0]
    pulses_dev = echoes.shape[1]
    amplitude = 2.0 / math.sqrt(TAPS)
    table_re = (amplitude * jnp.cos(chirp_phase)).astype(jnp.bfloat16)
    table_im = (amplitude * jnp.sin(chirp_phase)).astype(jnp.bfloat16)
    band = band_tables(table_re, table_im, echoes.shape[2])
    live_pulses = pulse_counts[0]
    first_pulse = lax.axis_index("pulse") * pulses_dev
    compressed = compress(echoes, band, first_pulse, live_pulses)
    chosen = partner_bits[0]
    acq_size = lax.axis_size("acq")
    me = lax.axis_index("acq")
    me_parity = jnp.int32(0)
    for which in range(acq_size.bit_length() - 1):
        me_parity = me_parity ^ ((me >> which) & 1)
    low_bits = (0, 1)
    high_bits = (2, 3)
    edge_pairs = []
    for slot in range(2):
        edge_pairs.append(
            [
                (i, i ^ (1 << (high_bits[slot] if parity(i) else low_bits[slot])))
                for i in range(acq_size)
            ]
        )
    cand_bits = []
    for slot in range(2):
        cand_bits.append(jnp.where(me_parity == 1, low_bits[slot], high_bits[slot]))
        cand_bits.append(jnp.where(me_parity == 1, high_bits[slot], low_bits[slot]))
    preds = tuple(chosen[slot] == bit for slot in range(2) for bit in cand_bits)
    turned = lax.all_to_all(compressed, "pulse", split_axis=1, concat_axis=2, tiled=True)
    *preds, turned = lax.optimization_barrier((*preds, turned))
    focused = azimuth(turned, azimuth_rate).astype(jnp.bfloat16)
    arrived = [lax.ppermute(focused, "acq", pairs) for pairs in edge_pairs]
    looked = cross_looks(focused, arrived)
    returned = [
        lax.ppermute(looked[slot], "acq", [(dst, src) for src, dst in edge_pairs[slot]])
        for slot in range(2)
    ]
    candidates = []
    for slot in range(2):
        candidates.append(looked[slot])
        back = returned[slot]
        candidates.append(jnp.stack([back[0], -back[1]]))
    results = []
    for slot in range(2):
        pick = candidates[0]
        for index in range(1, len(candidates)):
            pick = jnp.where(preds[slot * len(candidates) + index], candidates[index], pick)
        results.append(pick)
    interfere_real = jnp.stack([item[0] for item in results])[None]
    interfere_imag = jnp.stack([item[1] for item in results])[None]
    return (interfere_real, interfere_imag)


def solution(mesh):
    in_specs = (P("acq", None, "pulse", None), P(), P("acq"), P("pulse"), P("acq", None))
    out_specs = (P("acq", None, "pulse", None), P("acq", None, "pulse", None))
    return jax.shard_map(
        per_device, mesh=mesh, in_specs=in_specs, out_specs=out_specs, check_vma=False
    )
```

```python
import math

import jax
import jax.numpy as jnp
from jax import lax
from jax.experimental import pallas as pl
from jax.experimental.pallas import tpu as pltpu
from jax.sharding import PartitionSpec as P

RNG = 512
TAPS = 1024
LOOK_RNG = 4
LOOK_AZ = 16
BAND_ROWS = 128


def part_tables(length, inverse):
    steps = jnp.arange(length, dtype=jnp.int32)
    angle = 2.0 * jnp.pi * (steps[:, None] * steps[None, :] % length).astype(jnp.float32) / length
    cosine = jnp.cos(angle)
    sine = jnp.sin(angle)
    if inverse:
        sine = -sine
    return jnp.stack([jnp.stack([cosine, -sine]), jnp.stack([sine, cosine])])


def complex_product(left_re, left_im, right_re, right_im):
    return (left_re * right_re - left_im * right_im, left_re * right_im + left_im * right_re)


def band_kernel(re_ref, im_ref, band_ref, strip_ref):
    rows = BAND_ROWS
    span = re_ref.shape[1]
    width = band_ref.shape[3]
    dtype = band_ref.dtype
    step = pl.program_id(0)

    @pl.when(step == 0)
    def _():
        strip_ref[0] = pltpu.roll(jnp.broadcast_to(re_ref[...], (rows, span)), 0, 1, stride=1, stride_axis=0)
        strip_ref[1] = pltpu.roll(jnp.broadcast_to(im_ref[...], (rows, span)), 0, 1, stride=1, stride_axis=0)

    shift = pl.multiple_of(step * rows, rows)
    re_band = pltpu.roll(strip_ref[0], shift, 1)[:, :width]
    im_band = pltpu.roll(strip_ref[1], shift, 1)[:, :width]
    band_ref[0, 0] = re_band.astype(dtype)
    band_ref[0, 1] = (-im_band).astype(dtype)
    band_ref[1, 0] = im_band.astype(dtype)
    band_ref[1, 1] = re_band.astype(dtype)


def band_tables(table_re, table_im, width):
    rows = BAND_ROWS
    span = -(-(width + 1) // 128) * 128
    pad = jnp.zeros((span - table_re.shape[0],), jnp.float32)
    re_row = jnp.concatenate([table_re.astype(jnp.float32), pad])[None]
    im_row = jnp.concatenate([table_im.astype(jnp.float32), pad])[None]
    row_spec = pl.BlockSpec((1, span), lambda i: (0, 0))
    out_spec = pl.BlockSpec((2, 2, rows, width), lambda i: (0, 0, i, 0))
    shape = jax.ShapeDtypeStruct((2, 2, RNG, width), jnp.bfloat16)
    band = pl.pallas_call(
        band_kernel,
        grid=(RNG // rows,),
        in_specs=[row_spec, row_spec],
        out_specs=out_spec,
        out_shape=shape,
        scratch_shapes=[pltpu.VMEM((2, rows, span), jnp.float32)],
        compiler_params=pltpu.CompilerParams(dimension_semantics=("arbitrary",)),
    )(re_row, im_row)
    return band.reshape(2, 2 * RNG, width)


def compress(echoes, band, first_pulse, live_pulses):
    pulse_rows = echoes.shape[1]
    dims = (((0, 2), (0, 2)), ((), ()))
    result = lax.dot_general(band, echoes, dims, preferred_element_type=jnp.float32)
    joined = result.reshape(2, RNG, pulse_rows)
    pulse_ids = first_pulse + jnp.arange(pulse_rows, dtype=jnp.int32)
    keep = (pulse_ids < live_pulses).astype(jnp.float32)
    return (joined * keep[None, None, :]).astype(jnp.bfloat16)


def azimuth(turned, azimuth_rate):
    columns = turned.shape[1]
    length = turned.shape[2]
    outer_len = 64
    inner_len = length // outer_len
    highest = lax.Precision.HIGH
    signal = turned.astype(jnp.float32).reshape(2, columns, outer_len, inner_len)
    section_one = jnp.einsum(
        "pcab,pqak->qckb", signal, part_tables(outer_len, False), precision=highest
    )
    outer_ids = jnp.arange(outer_len, dtype=jnp.int32)
    inner_ids = jnp.arange(inner_len, dtype=jnp.int32)
    twist = (
        2.0
        * jnp.pi
        * (outer_ids[:, None] * inner_ids[None, :] % length).astype(jnp.float32)
        / length
    )
    twist_cos = jnp.cos(twist)
    twist_sin = jnp.sin(twist)
    turned_re, turned_im = complex_product(section_one[0], section_one[1], twist_cos, -twist_sin)
    spectrum = jnp.einsum(
        "pckb,pqbm->qckm",
        jnp.stack([turned_re, turned_im]),
        part_tables(inner_len, False),
        precision=highest,
    )
    freq_index = outer_ids[:, None] + outer_len * inner_ids[None, :]
    signed = jnp.where(freq_index < length // 2, freq_index, freq_index - length).astype(
        jnp.float32
    )
    quad = signed * signed / length
    phase = (jnp.pi * azimuth_rate)[:, None, None] * quad[None, :, :]
    filt_re, filt_im = complex_product(spectrum[0], spectrum[1], jnp.cos(phase), -jnp.sin(phase))
    back_one = jnp.einsum(
        "pckm,pqmb->qckb",
        jnp.stack([filt_re, filt_im]),
        part_tables(inner_len, True),
        precision=highest,
    )
    undo_re, undo_im = complex_product(back_one[0], back_one[1], twist_cos, twist_sin)
    restored = jnp.einsum(
        "pckb,pqka->qcab",
        jnp.stack([undo_re, undo_im]),
        part_tables(outer_len, True),
        precision=highest,
    )
    return (restored / length).reshape(2, columns, length)


def parity(index):
    return bin(index).count("1") % 2


def multilook(stacked):
    count, columns, pulse_len = stacked.shape
    inner = 128
    shaped = stacked.reshape(count, columns // LOOK_RNG, LOOK_RNG, pulse_len // inner, inner)
    summed = jnp.sum(shaped, axis=2)
    lanes = jnp.arange(inner, dtype=jnp.int32)
    groups = jnp.arange(inner // LOOK_AZ, dtype=jnp.int32)
    pool = (lanes[:, None] // LOOK_AZ == groups[None, :]).astype(jnp.float32)
    looked = jnp.einsum("nrab,bg->nrag", summed, pool, precision=lax.Precision.HIGHEST)
    scale = 1.0 / (LOOK_RNG * LOOK_AZ)
    return looked.reshape(count, columns // LOOK_RNG, pulse_len // LOOK_AZ) * scale


def cross_looks(own_block, partners):
    own_f = own_block.astype(jnp.float32)
    prods = []
    for partner in partners:
        other_f = partner.astype(jnp.float32)
        prods.append(own_f[0] * other_f[0] + own_f[1] * other_f[1])
        prods.append(own_f[1] * other_f[0] - own_f[0] * other_f[1])
    looked = multilook(jnp.stack(prods))
    return looked.reshape(len(partners), 2, *looked.shape[1:])


def per_device(raw_echo, chirp_phase, pulse_counts, azimuth_rate, partner_bits):
    echoes = raw_echo[0]
    pulses_dev = echoes.shape[1]
    amplitude = 2.0 / math.sqrt(TAPS)
    table_re = (amplitude * jnp.cos(chirp_phase)).astype(jnp.bfloat16)
    table_im = (amplitude * jnp.sin(chirp_phase)).astype(jnp.bfloat16)
    band = band_tables(table_re, table_im, echoes.shape[2])
    live_pulses = pulse_counts[0]
    first_pulse = lax.axis_index("pulse") * pulses_dev
    compressed = compress(echoes, band, first_pulse, live_pulses)
    chosen = partner_bits[0]
    acq_size = lax.axis_size("acq")
    me = lax.axis_index("acq")
    me_parity = jnp.int32(0)
    for which in range(acq_size.bit_length() - 1):
        me_parity = me_parity ^ ((me >> which) & 1)
    low_bits = (0, 1)
    high_bits = (2, 3)
    edge_pairs = []
    for slot in range(2):
        edge_pairs.append(
            [
                (i, i ^ (1 << (high_bits[slot] if parity(i) else low_bits[slot])))
                for i in range(acq_size)
            ]
        )
    cand_bits = []
    for slot in range(2):
        cand_bits.append(jnp.where(me_parity == 1, low_bits[slot], high_bits[slot]))
        cand_bits.append(jnp.where(me_parity == 1, high_bits[slot], low_bits[slot]))
    preds = tuple(chosen[slot] == bit for slot in range(2) for bit in cand_bits)
    turned = lax.all_to_all(compressed, "pulse", split_axis=1, concat_axis=2, tiled=True)
    *preds, turned = lax.optimization_barrier((*preds, turned))
    focused = azimuth(turned, azimuth_rate).astype(jnp.bfloat16)
    arrived = [lax.ppermute(focused, "acq", pairs) for pairs in edge_pairs]
    looked = cross_looks(focused, arrived)
    returned = [
        lax.ppermute(looked[slot], "acq", [(dst, src) for src, dst in edge_pairs[slot]])
        for slot in range(2)
    ]
    candidates = []
    for slot in range(2):
        candidates.append(looked[slot])
        back = returned[slot]
        candidates.append(jnp.stack([back[0], -back[1]]))
    results = []
    for slot in range(2):
        pick = candidates[0]
        for index in range(1, len(candidates)):
            pick = jnp.where(preds[slot * len(candidates) + index], candidates[index], pick)
        results.append(pick)
    interfere_real = jnp.stack([item[0] for item in results])[None]
    interfere_imag = jnp.stack([item[1] for item in results])[None]
    return (interfere_real, interfere_imag)


def solution(mesh):
    in_specs = (P("acq", None, "pulse", None), P(), P("acq"), P("pulse"), P("acq", None))
    out_specs = (P("acq", None, "pulse", None), P("acq", None, "pulse", None))
    return jax.shard_map(
        per_device, mesh=mesh, in_specs=in_specs, out_specs=out_specs, check_vma=False
    )
```

```python
import math

import jax
import jax.numpy as jnp
from jax import lax
from jax.experimental import pallas as pl
from jax.experimental.pallas import tpu as pltpu
from jax.sharding import PartitionSpec as P

RNG = 512
TAPS = 1024
LOOK_RNG = 4
LOOK_AZ = 16
BAND_ROWS = 128


def part_tables(length, inverse):
    steps = jnp.arange(length, dtype=jnp.int32)
    angle = 2.0 * jnp.pi * (steps[:, None] * steps[None, :] % length).astype(jnp.float32) / length
    cosine = jnp.cos(angle)
    sine = jnp.sin(angle)
    if inverse:
        sine = -sine
    return jnp.stack([jnp.stack([cosine, -sine]), jnp.stack([sine, cosine])])


def complex_product(left_re, left_im, right_re, right_im):
    return (left_re * right_re - left_im * right_im, left_re * right_im + left_im * right_re)


def band_kernel(re_ref, im_ref, band_ref):
    rows = BAND_ROWS
    strip = re_ref.shape[1]
    width = band_ref.shape[3]
    dtype = band_ref.dtype
    re_strip = pltpu.roll(jnp.broadcast_to(re_ref[...], (rows, strip)), 0, 1, stride=1, stride_axis=0)
    im_strip = pltpu.roll(jnp.broadcast_to(im_ref[...], (rows, strip)), 0, 1, stride=1, stride_axis=0)
    pieces = (
        (0, 0, re_strip.astype(dtype)),
        (0, 1, (-im_strip).astype(dtype)),
        (1, 0, im_strip.astype(dtype)),
        (1, 1, re_strip.astype(dtype)),
    )
    for start in range(0, band_ref.shape[2], rows):
        stop = min(start + strip, width)
        for part, half, values in pieces:
            band_ref[part, half, start : start + rows, start:stop] = values[:, : stop - start]
            if start > 0:
                band_ref[part, half, start : start + rows, :start] = jnp.zeros((rows, start), dtype)
            if stop < width:
                band_ref[part, half, start : start + rows, stop:] = jnp.zeros((rows, width - stop), dtype)


def band_tables(table_re, table_im, width):
    rows = BAND_ROWS
    strip = -(-(TAPS + rows - 1) // 128) * 128
    pad = jnp.zeros((strip - table_re.shape[0],), jnp.float32)
    re_row = jnp.concatenate([table_re.astype(jnp.float32), pad])[None]
    im_row = jnp.concatenate([table_im.astype(jnp.float32), pad])[None]
    shape = jax.ShapeDtypeStruct((2, 2, RNG, width), jnp.bfloat16)
    band = pl.pallas_call(band_kernel, out_shape=shape)(re_row, im_row)
    return band.reshape(2, 2 * RNG, width)


def compress(echoes, band, first_pulse, live_pulses):
    pulse_rows = echoes.shape[1]
    dims = (((0, 2), (0, 2)), ((), ()))
    result = lax.dot_general(band, echoes, dims, preferred_element_type=jnp.float32)
    joined = result.reshape(2, RNG, pulse_rows)
    pulse_ids = first_pulse + jnp.arange(pulse_rows, dtype=jnp.int32)
    keep = (pulse_ids < live_pulses).astype(jnp.float32)
    return (joined * keep[None, None, :]).astype(jnp.bfloat16)


def azimuth(turned, azimuth_rate):
    columns = turned.shape[1]
    length = turned.shape[2]
    outer_len = 64
    inner_len = length // outer_len
    highest = lax.Precision.HIGH
    signal = turned.astype(jnp.float32).reshape(2, columns, outer_len, inner_len)
    section_one = jnp.einsum(
        "pcab,pqak->qckb", signal, part_tables(outer_len, False), precision=highest
    )
    outer_ids = jnp.arange(outer_len, dtype=jnp.int32)
    inner_ids = jnp.arange(inner_len, dtype=jnp.int32)
    twist = (
        2.0
        * jnp.pi
        * (outer_ids[:, None] * inner_ids[None, :] % length).astype(jnp.float32)
        / length
    )
    twist_cos = jnp.cos(twist)
    twist_sin = jnp.sin(twist)
    turned_re, turned_im = complex_product(section_one[0], section_one[1], twist_cos, -twist_sin)
    spectrum = jnp.einsum(
        "pckb,pqbm->qckm",
        jnp.stack([turned_re, turned_im]),
        part_tables(inner_len, False),
        precision=highest,
    )
    freq_index = outer_ids[:, None] + outer_len * inner_ids[None, :]
    signed = jnp.where(freq_index < length // 2, freq_index, freq_index - length).astype(
        jnp.float32
    )
    quad = signed * signed / length
    phase = (jnp.pi * azimuth_rate)[:, None, None] * quad[None, :, :]
    filt_re, filt_im = complex_product(spectrum[0], spectrum[1], jnp.cos(phase), -jnp.sin(phase))
    back_one = jnp.einsum(
        "pckm,pqmb->qckb",
        jnp.stack([filt_re, filt_im]),
        part_tables(inner_len, True),
        precision=highest,
    )
    undo_re, undo_im = complex_product(back_one[0], back_one[1], twist_cos, twist_sin)
    restored = jnp.einsum(
        "pckb,pqka->qcab",
        jnp.stack([undo_re, undo_im]),
        part_tables(outer_len, True),
        precision=highest,
    )
    return (restored / length).reshape(2, columns, length)


def parity(index):
    return bin(index).count("1") % 2


def multilook(stacked):
    count, columns, pulse_len = stacked.shape
    inner = 128
    shaped = stacked.reshape(count, columns // LOOK_RNG, LOOK_RNG, pulse_len // inner, inner)
    summed = jnp.sum(shaped, axis=2)
    lanes = jnp.arange(inner, dtype=jnp.int32)
    groups = jnp.arange(inner // LOOK_AZ, dtype=jnp.int32)
    pool = (lanes[:, None] // LOOK_AZ == groups[None, :]).astype(jnp.float32)
    looked = jnp.einsum("nrab,bg->nrag", summed, pool, precision=lax.Precision.HIGHEST)
    scale = 1.0 / (LOOK_RNG * LOOK_AZ)
    return looked.reshape(count, columns // LOOK_RNG, pulse_len // LOOK_AZ) * scale


def cross_looks(own_block, partners):
    own_f = own_block.astype(jnp.float32)
    prods = []
    for partner in partners:
        other_f = partner.astype(jnp.float32)
        prods.append(own_f[0] * other_f[0] + own_f[1] * other_f[1])
        prods.append(own_f[1] * other_f[0] - own_f[0] * other_f[1])
    looked = multilook(jnp.stack(prods))
    return looked.reshape(len(partners), 2, *looked.shape[1:])


def per_device(raw_echo, chirp_phase, pulse_counts, azimuth_rate, partner_bits):
    echoes = raw_echo[0]
    pulses_dev = echoes.shape[1]
    amplitude = 2.0 / math.sqrt(TAPS)
    table_re = (amplitude * jnp.cos(chirp_phase)).astype(jnp.bfloat16)
    table_im = (amplitude * jnp.sin(chirp_phase)).astype(jnp.bfloat16)
    band = band_tables(table_re, table_im, echoes.shape[2])
    live_pulses = pulse_counts[0]
    first_pulse = lax.axis_index("pulse") * pulses_dev
    compressed = compress(echoes, band, first_pulse, live_pulses)
    chosen = partner_bits[0]
    acq_size = lax.axis_size("acq")
    me = lax.axis_index("acq")
    bit_count = acq_size.bit_length() - 1
    preds = tuple(chosen[slot] == which for slot in range(2) for which in range(bit_count))
    turned = lax.all_to_all(compressed, "pulse", split_axis=1, concat_axis=2, tiled=True)
    *preds, turned = lax.optimization_barrier((*preds, turned))
    focused = azimuth(turned, azimuth_rate).astype(jnp.bfloat16)
    arrived = [
        lax.ppermute(focused, "acq", [(i, i ^ (1 << which)) for i in range(acq_size)])
        for which in range(bit_count)
    ]
    partners = []
    for slot in range(2):
        pick = arrived[0]
        for which in range(1, bit_count):
            pick = jnp.where(preds[slot * bit_count + which], arrived[which], pick)
        partners.append(pick)
    looked = cross_looks(focused, partners)
    results = [looked[slot] for slot in range(2)]
    interfere_real = jnp.stack([item[0] for item in results])[None]
    interfere_imag = jnp.stack([item[1] for item in results])[None]
    return (interfere_real, interfere_imag)


def solution(mesh):
    in_specs = (P("acq", None, "pulse", None), P(), P("acq"), P("pulse"), P("acq", None))
    out_specs = (P("acq", None, "pulse", None), P("acq", None, "pulse", None))
    return jax.shard_map(
        per_device, mesh=mesh, in_specs=in_specs, out_specs=out_specs, check_vma=False
    )
```

```python
import math

import jax
import jax.numpy as jnp
from jax import lax
from jax.experimental import pallas as pl
from jax.experimental.pallas import tpu as pltpu
from jax.sharding import PartitionSpec as P

RNG = 512
TAPS = 1024
LOOK_RNG = 4
LOOK_AZ = 16
BAND_ROWS = 128


def part_tables(length, inverse):
    steps = jnp.arange(length, dtype=jnp.int32)
    angle = 2.0 * jnp.pi * (steps[:, None] * steps[None, :] % length).astype(jnp.float32) / length
    cosine = jnp.cos(angle)
    sine = jnp.sin(angle)
    if inverse:
        sine = -sine
    return jnp.stack([jnp.stack([cosine, -sine]), jnp.stack([sine, cosine])])


def complex_product(left_re, left_im, right_re, right_im):
    return (left_re * right_re - left_im * right_im, left_re * right_im + left_im * right_re)


def band_kernel(re_ref, im_ref, band_ref):
    rows = BAND_ROWS
    strip = re_ref.shape[1]
    width = band_ref.shape[3]
    dtype = band_ref.dtype
    re_strip = pltpu.roll(jnp.broadcast_to(re_ref[...], (rows, strip)), 0, 1, stride=1, stride_axis=0)
    im_strip = pltpu.roll(jnp.broadcast_to(im_ref[...], (rows, strip)), 0, 1, stride=1, stride_axis=0)
    pieces = (
        (0, 0, re_strip.astype(dtype)),
        (0, 1, (-im_strip).astype(dtype)),
        (1, 0, im_strip.astype(dtype)),
        (1, 1, re_strip.astype(dtype)),
    )
    for start in range(0, band_ref.shape[2], rows):
        stop = min(start + strip, width)
        for part, half, values in pieces:
            band_ref[part, half, start : start + rows, start:stop] = values[:, : stop - start]
            if start > 0:
                band_ref[part, half, start : start + rows, :start] = jnp.zeros((rows, start), dtype)
            if stop < width:
                band_ref[part, half, start : start + rows, stop:] = jnp.zeros((rows, width - stop), dtype)


def band_tables(table_re, table_im, width):
    rows = BAND_ROWS
    strip = -(-(TAPS + rows - 1) // 128) * 128
    pad = jnp.zeros((strip - table_re.shape[0],), jnp.float32)
    re_row = jnp.concatenate([table_re.astype(jnp.float32), pad])[None]
    im_row = jnp.concatenate([table_im.astype(jnp.float32), pad])[None]
    shape = jax.ShapeDtypeStruct((2, 2, RNG, width), jnp.bfloat16)
    band = pl.pallas_call(band_kernel, out_shape=shape)(re_row, im_row)
    return band.reshape(2, 2 * RNG, width)


def compress(echoes, band, first_pulse, live_pulses):
    pulse_rows = echoes.shape[1]
    dims = (((0, 2), (0, 2)), ((), ()))
    result = lax.dot_general(band, echoes, dims, preferred_element_type=jnp.float32)
    joined = result.reshape(2, RNG, pulse_rows)
    pulse_ids = first_pulse + jnp.arange(pulse_rows, dtype=jnp.int32)
    keep = (pulse_ids < live_pulses).astype(jnp.float32)
    return (joined * keep[None, None, :]).astype(jnp.bfloat16)


def filter_tables(azimuth_rate, length):
    outer_len = 64
    inner_len = length // outer_len
    outer_ids = jnp.arange(outer_len, dtype=jnp.int32)
    inner_ids = jnp.arange(inner_len, dtype=jnp.int32)
    freq_index = outer_ids[:, None] + outer_len * inner_ids[None, :]
    signed = jnp.where(freq_index < length // 2, freq_index, freq_index - length).astype(
        jnp.float32
    )
    quad = signed * signed / length
    phase = (jnp.pi * azimuth_rate)[:, None, None] * quad[None, :, :]
    return jnp.cos(phase), jnp.sin(phase)


def azimuth(turned, filt_cos, filt_sin):
    columns = turned.shape[1]
    length = turned.shape[2]
    outer_len = 64
    inner_len = length // outer_len
    highest = lax.Precision.HIGH
    signal = turned.astype(jnp.float32).reshape(2, columns, outer_len, inner_len)
    section_one = jnp.einsum(
        "pcab,pqak->qckb", signal, part_tables(outer_len, False), precision=highest
    )
    outer_ids = jnp.arange(outer_len, dtype=jnp.int32)
    inner_ids = jnp.arange(inner_len, dtype=jnp.int32)
    twist = (
        2.0
        * jnp.pi
        * (outer_ids[:, None] * inner_ids[None, :] % length).astype(jnp.float32)
        / length
    )
    twist_cos = jnp.cos(twist)
    twist_sin = jnp.sin(twist)
    turned_re, turned_im = complex_product(section_one[0], section_one[1], twist_cos, -twist_sin)
    spectrum = jnp.einsum(
        "pckb,pqbm->qckm",
        jnp.stack([turned_re, turned_im]),
        part_tables(inner_len, False),
        precision=highest,
    )
    filt_re, filt_im = complex_product(spectrum[0], spectrum[1], filt_cos, -filt_sin)
    back_one = jnp.einsum(
        "pckm,pqmb->qckb",
        jnp.stack([filt_re, filt_im]),
        part_tables(inner_len, True),
        precision=highest,
    )
    undo_re, undo_im = complex_product(back_one[0], back_one[1], twist_cos, twist_sin)
    restored = jnp.einsum(
        "pckb,pqka->qcab",
        jnp.stack([undo_re, undo_im]),
        part_tables(outer_len, True),
        precision=highest,
    )
    return (restored / length).reshape(2, columns, length)


def parity(index):
    return bin(index).count("1") % 2


def multilook(stacked):
    count, columns, pulse_len = stacked.shape
    inner = 128
    shaped = stacked.reshape(count, columns // LOOK_RNG, LOOK_RNG, pulse_len // inner, inner)
    summed = jnp.sum(shaped, axis=2)
    lanes = jnp.arange(inner, dtype=jnp.int32)
    groups = jnp.arange(inner // LOOK_AZ, dtype=jnp.int32)
    pool = (lanes[:, None] // LOOK_AZ == groups[None, :]).astype(jnp.float32)
    looked = jnp.einsum("nrab,bg->nrag", summed, pool, precision=lax.Precision.HIGHEST)
    scale = 1.0 / (LOOK_RNG * LOOK_AZ)
    return looked.reshape(count, columns // LOOK_RNG, pulse_len // LOOK_AZ) * scale


def cross_looks(own_block, partners):
    own_f = own_block.astype(jnp.float32)
    prods = []
    for partner in partners:
        other_f = partner.astype(jnp.float32)
        prods.append(own_f[0] * other_f[0] + own_f[1] * other_f[1])
        prods.append(own_f[1] * other_f[0] - own_f[0] * other_f[1])
    looked = multilook(jnp.stack(prods))
    return looked.reshape(len(partners), 2, *looked.shape[1:])


def per_device(raw_echo, chirp_phase, pulse_counts, azimuth_rate, partner_bits):
    echoes = raw_echo[0]
    pulses_dev = echoes.shape[1]
    amplitude = 2.0 / math.sqrt(TAPS)
    table_re = (amplitude * jnp.cos(chirp_phase)).astype(jnp.bfloat16)
    table_im = (amplitude * jnp.sin(chirp_phase)).astype(jnp.bfloat16)
    band = band_tables(table_re, table_im, echoes.shape[2])
    live_pulses = pulse_counts[0]
    first_pulse = lax.axis_index("pulse") * pulses_dev
    compressed = compress(echoes, band, first_pulse, live_pulses)
    chosen = partner_bits[0]
    acq_size = lax.axis_size("acq")
    me = lax.axis_index("acq")
    me_parity = jnp.int32(0)
    for which in range(acq_size.bit_length() - 1):
        me_parity = me_parity ^ ((me >> which) & 1)
    low_bits = (0, 1)
    high_bits = (2, 3)
    edge_pairs = []
    for slot in range(2):
        edge_pairs.append(
            [
                (i, i ^ (1 << (high_bits[slot] if parity(i) else low_bits[slot])))
                for i in range(acq_size)
            ]
        )
    cand_bits = []
    for slot in range(2):
        cand_bits.append(jnp.where(me_parity == 1, low_bits[slot], high_bits[slot]))
        cand_bits.append(jnp.where(me_parity == 1, high_bits[slot], low_bits[slot]))
    preds = tuple(chosen[slot] == bit for slot in range(2) for bit in cand_bits)
    turned = lax.all_to_all(compressed, "pulse", split_axis=1, concat_axis=2, tiled=True)
    filt_cos, filt_sin = filter_tables(azimuth_rate, pulses_dev * lax.axis_size("pulse"))
    *preds, filt_cos, filt_sin, turned = lax.optimization_barrier((*preds, filt_cos, filt_sin, turned))
    focused = azimuth(turned, filt_cos, filt_sin).astype(jnp.bfloat16)
    arrived = [lax.ppermute(focused, "acq", pairs) for pairs in edge_pairs]
    looked = cross_looks(focused, arrived)
    returned = [
        lax.ppermute(looked[slot], "acq", [(dst, src) for src, dst in edge_pairs[slot]])
        for slot in range(2)
    ]
    candidates = []
    for slot in range(2):
        candidates.append(looked[slot])
        back = returned[slot]
        candidates.append(jnp.stack([back[0], -back[1]]))
    results = []
    for slot in range(2):
        pick = candidates[0]
        for index in range(1, len(candidates)):
            pick = jnp.where(preds[slot * len(candidates) + index], candidates[index], pick)
        results.append(pick)
    interfere_real = jnp.stack([item[0] for item in results])[None]
    interfere_imag = jnp.stack([item[1] for item in results])[None]
    return (interfere_real, interfere_imag)


def solution(mesh):
    in_specs = (P("acq", None, "pulse", None), P(), P("acq"), P("pulse"), P("acq", None))
    out_specs = (P("acq", None, "pulse", None), P("acq", None, "pulse", None))
    return jax.shard_map(
        per_device, mesh=mesh, in_specs=in_specs, out_specs=out_specs, check_vma=False
    )
```

```python
import math

import jax
import jax.numpy as jnp
from jax import lax
from jax.experimental import pallas as pl
from jax.experimental.pallas import tpu as pltpu
from jax.sharding import PartitionSpec as P

RNG = 512
TAPS = 1024
LOOK_RNG = 4
LOOK_AZ = 16
BAND_ROWS = 128


def part_tables(length, inverse):
    steps = jnp.arange(length, dtype=jnp.int32)
    angle = 2.0 * jnp.pi * (steps[:, None] * steps[None, :] % length).astype(jnp.float32) / length
    cosine = jnp.cos(angle)
    sine = jnp.sin(angle)
    if inverse:
        sine = -sine
    return jnp.stack([jnp.stack([cosine, -sine]), jnp.stack([sine, cosine])])


def complex_product(left_re, left_im, right_re, right_im):
    return (left_re * right_re - left_im * right_im, left_re * right_im + left_im * right_re)


def band_kernel(re_ref, im_ref, band_ref):
    rows = BAND_ROWS
    strip = re_ref.shape[1]
    width = band_ref.shape[3]
    dtype = band_ref.dtype
    re_strip = pltpu.roll(jnp.broadcast_to(re_ref[...], (rows, strip)), 0, 1, stride=1, stride_axis=0)
    im_strip = pltpu.roll(jnp.broadcast_to(im_ref[...], (rows, strip)), 0, 1, stride=1, stride_axis=0)
    pieces = (
        (0, 0, re_strip.astype(dtype)),
        (0, 1, (-im_strip).astype(dtype)),
        (1, 0, im_strip.astype(dtype)),
        (1, 1, re_strip.astype(dtype)),
    )
    for start in range(0, band_ref.shape[2], rows):
        stop = min(start + strip, width)
        for part, half, values in pieces:
            band_ref[part, half, start : start + rows, start:stop] = values[:, : stop - start]
            if start > 0:
                band_ref[part, half, start : start + rows, :start] = jnp.zeros((rows, start), dtype)
            if stop < width:
                band_ref[part, half, start : start + rows, stop:] = jnp.zeros((rows, width - stop), dtype)


def band_tables(table_re, table_im, width):
    rows = BAND_ROWS
    strip = -(-(TAPS + rows - 1) // 128) * 128
    pad = jnp.zeros((strip - table_re.shape[0],), jnp.float32)
    re_row = jnp.concatenate([table_re.astype(jnp.float32), pad])[None]
    im_row = jnp.concatenate([table_im.astype(jnp.float32), pad])[None]
    shape = jax.ShapeDtypeStruct((2, 2, RNG, width), jnp.bfloat16)
    band = pl.pallas_call(band_kernel, out_shape=shape)(re_row, im_row)
    return band.reshape(2, 2 * RNG, width)


def compress(echoes, band, first_pulse, live_pulses):
    pulse_rows = echoes.shape[1]
    dims = (((0, 2), (0, 2)), ((), ()))
    result = lax.dot_general(band, echoes, dims, preferred_element_type=jnp.float32)
    joined = result.reshape(2, RNG, pulse_rows)
    pulse_ids = first_pulse + jnp.arange(pulse_rows, dtype=jnp.int32)
    keep = (pulse_ids < live_pulses).astype(jnp.float32)
    return (joined * keep[None, None, :]).astype(jnp.bfloat16)


def filter_tables(azimuth_rate, length):
    outer_len = 64
    inner_len = length // outer_len
    outer_ids = jnp.arange(outer_len, dtype=jnp.int32)
    inner_ids = jnp.arange(inner_len, dtype=jnp.int32)
    freq_index = outer_ids[:, None] + outer_len * inner_ids[None, :]
    signed = jnp.where(freq_index < length // 2, freq_index, freq_index - length).astype(
        jnp.float32
    )
    quad = signed * signed / length
    phase = (jnp.pi * azimuth_rate)[:, None, None] * quad[None, :, :]
    return jnp.cos(phase), jnp.sin(phase)


def azimuth(turned, filt_cos, filt_sin):
    columns = turned.shape[1]
    length = turned.shape[2]
    outer_len = 64
    inner_len = length // outer_len
    highest = lax.Precision.HIGH
    signal = turned.astype(jnp.float32).reshape(2, columns, outer_len, inner_len)
    section_one = jnp.einsum(
        "pcab,pqak->qckb", signal, part_tables(outer_len, False), precision=highest
    )
    outer_ids = jnp.arange(outer_len, dtype=jnp.int32)
    inner_ids = jnp.arange(inner_len, dtype=jnp.int32)
    twist = (
        2.0
        * jnp.pi
        * (outer_ids[:, None] * inner_ids[None, :] % length).astype(jnp.float32)
        / length
    )
    twist_cos = jnp.cos(twist)
    twist_sin = jnp.sin(twist)
    turned_re, turned_im = complex_product(section_one[0], section_one[1], twist_cos, -twist_sin)
    spectrum = jnp.einsum(
        "pckb,pqbm->qckm",
        jnp.stack([turned_re, turned_im]),
        part_tables(inner_len, False),
        precision=highest,
    )
    filt_re, filt_im = complex_product(spectrum[0], spectrum[1], filt_cos, -filt_sin)
    back_one = jnp.einsum(
        "pckm,pqmb->qckb",
        jnp.stack([filt_re, filt_im]),
        part_tables(inner_len, True),
        precision=highest,
    )
    undo_re, undo_im = complex_product(back_one[0], back_one[1], twist_cos, twist_sin)
    restored = jnp.einsum(
        "pckb,pqka->qcab",
        jnp.stack([undo_re, undo_im]),
        part_tables(outer_len, True),
        precision=highest,
    )
    return (restored / length).reshape(2, columns, length)


def parity(index):
    return bin(index).count("1") % 2


def multilook(stacked):
    count, columns, pulse_len = stacked.shape
    inner = 128
    shaped = stacked.reshape(count, columns // LOOK_RNG, LOOK_RNG, pulse_len // inner, inner)
    summed = jnp.sum(shaped, axis=2)
    lanes = jnp.arange(inner, dtype=jnp.int32)
    groups = jnp.arange(inner // LOOK_AZ, dtype=jnp.int32)
    pool = (lanes[:, None] // LOOK_AZ == groups[None, :]).astype(jnp.float32)
    looked = jnp.einsum("nrab,bg->nrag", summed, pool, precision=lax.Precision.HIGHEST)
    scale = 1.0 / (LOOK_RNG * LOOK_AZ)
    return looked.reshape(count, columns // LOOK_RNG, pulse_len // LOOK_AZ) * scale


def cross_looks(own_block, partners):
    own_f = own_block.astype(jnp.float32)
    prods = []
    for partner in partners:
        other_f = partner.astype(jnp.float32)
        prods.append(own_f[0] * other_f[0] + own_f[1] * other_f[1])
        prods.append(own_f[1] * other_f[0] - own_f[0] * other_f[1])
    looked = multilook(jnp.stack(prods))
    return looked.reshape(len(partners), 2, *looked.shape[1:])


def per_device(raw_echo, chirp_phase, pulse_counts, azimuth_rate, partner_bits):
    echoes = raw_echo[0]
    pulses_dev = echoes.shape[1]
    amplitude = 2.0 / math.sqrt(TAPS)
    table_re = (amplitude * jnp.cos(chirp_phase)).astype(jnp.bfloat16)
    table_im = (amplitude * jnp.sin(chirp_phase)).astype(jnp.bfloat16)
    band = band_tables(table_re, table_im, echoes.shape[2])
    live_pulses = pulse_counts[0]
    first_pulse = lax.axis_index("pulse") * pulses_dev
    compressed = compress(echoes, band, first_pulse, live_pulses)
    chosen = partner_bits[0]
    acq_size = lax.axis_size("acq")
    me = lax.axis_index("acq")
    me_parity = jnp.int32(0)
    for which in range(acq_size.bit_length() - 1):
        me_parity = me_parity ^ ((me >> which) & 1)
    low_bits = (0, 1)
    high_bits = (2, 3)
    edge_pairs = []
    for slot in range(2):
        edge_pairs.append(
            [
                (i, i ^ (1 << (high_bits[slot] if parity(i) else low_bits[slot])))
                for i in range(acq_size)
            ]
        )
    cand_bits = []
    for slot in range(2):
        cand_bits.append(jnp.where(me_parity == 1, low_bits[slot], high_bits[slot]))
        cand_bits.append(jnp.where(me_parity == 1, high_bits[slot], low_bits[slot]))
    preds = tuple(chosen[slot] == bit for slot in range(2) for bit in cand_bits)
    turned = lax.all_to_all(compressed, "pulse", split_axis=1, concat_axis=2, tiled=True)
    filt_cos, filt_sin = filter_tables(azimuth_rate, pulses_dev * lax.axis_size("pulse"))
    *preds, filt_cos, filt_sin, turned = lax.optimization_barrier((*preds, filt_cos, filt_sin, turned))
    focused = azimuth(turned, filt_cos, filt_sin).astype(jnp.bfloat16)
    fast, slow = 1, 0
    arrived = [None, None]
    looked = [None, None]
    returned = [None, None]
    arrived[fast] = lax.ppermute(focused, "acq", edge_pairs[fast])
    looked[fast] = cross_looks(focused, [arrived[fast]])[0]
    returned[fast] = lax.ppermute(
        looked[fast], "acq", [(dst, src) for src, dst in edge_pairs[fast]]
    )
    gate, held = lax.optimization_barrier((looked[fast], focused))
    arrived[slow] = lax.ppermute(held, "acq", edge_pairs[slow])
    looked[slow] = cross_looks(focused, [arrived[slow]])[0]
    returned[slow] = lax.ppermute(
        looked[slow], "acq", [(dst, src) for src, dst in edge_pairs[slow]]
    )
    candidates = []
    for slot in range(2):
        candidates.append(looked[slot])
        back = returned[slot]
        candidates.append(jnp.stack([back[0], -back[1]]))
    results = []
    for slot in range(2):
        pick = candidates[0]
        for index in range(1, len(candidates)):
            pick = jnp.where(preds[slot * len(candidates) + index], candidates[index], pick)
        results.append(pick)
    interfere_real = jnp.stack([item[0] for item in results])[None]
    interfere_imag = jnp.stack([item[1] for item in results])[None]
    return (interfere_real, interfere_imag)


def solution(mesh):
    in_specs = (P("acq", None, "pulse", None), P(), P("acq"), P("pulse"), P("acq", None))
    out_specs = (P("acq", None, "pulse", None), P("acq", None, "pulse", None))
    return jax.shard_map(
        per_device, mesh=mesh, in_specs=in_specs, out_specs=out_specs, check_vma=False
    )
```

```python
import math

import jax
import jax.numpy as jnp
from jax import lax
from jax.experimental import pallas as pl
from jax.experimental.pallas import tpu as pltpu
from jax.sharding import PartitionSpec as P

RNG = 512
TAPS = 1024
LOOK_RNG = 4
LOOK_AZ = 16
BAND_ROWS = 128


def part_tables(length, inverse):
    steps = jnp.arange(length, dtype=jnp.int32)
    angle = 2.0 * jnp.pi * (steps[:, None] * steps[None, :] % length).astype(jnp.float32) / length
    cosine = jnp.cos(angle)
    sine = jnp.sin(angle)
    if inverse:
        sine = -sine
    return jnp.stack([jnp.stack([cosine, -sine]), jnp.stack([sine, cosine])])


def complex_product(left_re, left_im, right_re, right_im):
    return (left_re * right_re - left_im * right_im, left_re * right_im + left_im * right_re)


def band_kernel(re_ref, im_ref, band_ref):
    rows = BAND_ROWS
    strip = -(-(TAPS + BAND_ROWS - 1) // 128) * 128
    width = band_ref.shape[3]
    dtype = band_ref.dtype
    pad = jnp.zeros((1, strip - re_ref.shape[1]), jnp.float32)
    re_row = jnp.concatenate([re_ref[...].astype(jnp.float32), pad], axis=1)
    im_row = jnp.concatenate([im_ref[...].astype(jnp.float32), pad], axis=1)
    re_strip = pltpu.roll(jnp.broadcast_to(re_row, (rows, strip)), 0, 1, stride=1, stride_axis=0)
    im_strip = pltpu.roll(jnp.broadcast_to(im_row, (rows, strip)), 0, 1, stride=1, stride_axis=0)
    pieces = (
        (0, 0, re_strip.astype(dtype)),
        (0, 1, (-im_strip).astype(dtype)),
        (1, 0, im_strip.astype(dtype)),
        (1, 1, re_strip.astype(dtype)),
    )
    for start in range(0, band_ref.shape[2], rows):
        stop = min(start + strip, width)
        for part, half, values in pieces:
            band_ref[part, half, start : start + rows, start:stop] = values[:, : stop - start]
            if start > 0:
                band_ref[part, half, start : start + rows, :start] = jnp.zeros((rows, start), dtype)
            if stop < width:
                band_ref[part, half, start : start + rows, stop:] = jnp.zeros((rows, width - stop), dtype)


def band_tables(table_re, table_im, width):
    re_row = table_re.astype(jnp.float32)[None]
    im_row = table_im.astype(jnp.float32)[None]
    shape = jax.ShapeDtypeStruct((2, 2, RNG, width), jnp.bfloat16)
    band = pl.pallas_call(band_kernel, out_shape=shape)(re_row, im_row)
    return band.reshape(2, 2 * RNG, width)


def compress(echoes, band, first_pulse, live_pulses):
    pulse_rows = echoes.shape[1]
    dims = (((0, 2), (0, 2)), ((), ()))
    result = lax.dot_general(band, echoes, dims, preferred_element_type=jnp.float32)
    joined = result.reshape(2, RNG, pulse_rows)
    pulse_ids = first_pulse + jnp.arange(pulse_rows, dtype=jnp.int32)
    keep = (pulse_ids < live_pulses).astype(jnp.float32)
    return (joined * keep[None, None, :]).astype(jnp.bfloat16)


def filter_tables(azimuth_rate, length):
    outer_len = 64
    inner_len = length // outer_len
    outer_ids = jnp.arange(outer_len, dtype=jnp.int32)
    inner_ids = jnp.arange(inner_len, dtype=jnp.int32)
    freq_index = outer_ids[:, None] + outer_len * inner_ids[None, :]
    signed = jnp.where(freq_index < length // 2, freq_index, freq_index - length).astype(
        jnp.float32
    )
    quad = signed * signed / length
    phase = (jnp.pi * azimuth_rate)[:, None, None] * quad[None, :, :]
    return jnp.cos(phase), jnp.sin(phase)


def azimuth(turned, filt_cos, filt_sin):
    columns = turned.shape[1]
    length = turned.shape[2]
    outer_len = 64
    inner_len = length // outer_len
    highest = lax.Precision.HIGH
    signal = turned.astype(jnp.float32).reshape(2, columns, outer_len, inner_len)
    section_one = jnp.einsum(
        "pcab,pqak->qckb", signal, part_tables(outer_len, False), precision=highest
    )
    outer_ids = jnp.arange(outer_len, dtype=jnp.int32)
    inner_ids = jnp.arange(inner_len, dtype=jnp.int32)
    twist = (
        2.0
        * jnp.pi
        * (outer_ids[:, None] * inner_ids[None, :] % length).astype(jnp.float32)
        / length
    )
    twist_cos = jnp.cos(twist)
    twist_sin = jnp.sin(twist)
    turned_re, turned_im = complex_product(section_one[0], section_one[1], twist_cos, -twist_sin)
    spectrum = jnp.einsum(
        "pckb,pqbm->qckm",
        jnp.stack([turned_re, turned_im]),
        part_tables(inner_len, False),
        precision=highest,
    )
    filt_re, filt_im = complex_product(spectrum[0], spectrum[1], filt_cos, -filt_sin)
    back_one = jnp.einsum(
        "pckm,pqmb->qckb",
        jnp.stack([filt_re, filt_im]),
        part_tables(inner_len, True),
        precision=highest,
    )
    undo_re, undo_im = complex_product(back_one[0], back_one[1], twist_cos, twist_sin)
    restored = jnp.einsum(
        "pckb,pqka->qcab",
        jnp.stack([undo_re, undo_im]),
        part_tables(outer_len, True),
        precision=highest,
    )
    return (restored / length).reshape(2, columns, length)


def parity(index):
    return bin(index).count("1") % 2


def multilook(stacked):
    count, columns, pulse_len = stacked.shape
    inner = 128
    shaped = stacked.reshape(count, columns // LOOK_RNG, LOOK_RNG, pulse_len // inner, inner)
    summed = jnp.sum(shaped, axis=2)
    lanes = jnp.arange(inner, dtype=jnp.int32)
    groups = jnp.arange(inner // LOOK_AZ, dtype=jnp.int32)
    pool = (lanes[:, None] // LOOK_AZ == groups[None, :]).astype(jnp.float32)
    looked = jnp.einsum("nrab,bg->nrag", summed, pool, precision=lax.Precision.HIGHEST)
    scale = 1.0 / (LOOK_RNG * LOOK_AZ)
    return looked.reshape(count, columns // LOOK_RNG, pulse_len // LOOK_AZ) * scale


def cross_looks(own_block, partners):
    own_f = own_block.astype(jnp.float32)
    prods = []
    for partner in partners:
        other_f = partner.astype(jnp.float32)
        prods.append(own_f[0] * other_f[0] + own_f[1] * other_f[1])
        prods.append(own_f[1] * other_f[0] - own_f[0] * other_f[1])
    looked = multilook(jnp.stack(prods))
    return looked.reshape(len(partners), 2, *looked.shape[1:])


def per_device(raw_echo, chirp_phase, pulse_counts, azimuth_rate, partner_bits):
    echoes = raw_echo[0]
    pulses_dev = echoes.shape[1]
    amplitude = 2.0 / math.sqrt(TAPS)
    table_re = (amplitude * jnp.cos(chirp_phase)).astype(jnp.bfloat16)
    table_im = (amplitude * jnp.sin(chirp_phase)).astype(jnp.bfloat16)
    band = band_tables(table_re, table_im, echoes.shape[2])
    live_pulses = pulse_counts[0]
    first_pulse = lax.axis_index("pulse") * pulses_dev
    compressed = compress(echoes, band, first_pulse, live_pulses)
    chosen = partner_bits[0]
    acq_size = lax.axis_size("acq")
    me = lax.axis_index("acq")
    me_parity = jnp.int32(0)
    for which in range(acq_size.bit_length() - 1):
        me_parity = me_parity ^ ((me >> which) & 1)
    low_bits = (0, 1)
    high_bits = (2, 3)
    edge_pairs = []
    for slot in range(2):
        edge_pairs.append(
            [
                (i, i ^ (1 << (high_bits[slot] if parity(i) else low_bits[slot])))
                for i in range(acq_size)
            ]
        )
    cand_bits = []
    for slot in range(2):
        cand_bits.append(jnp.where(me_parity == 1, low_bits[slot], high_bits[slot]))
        cand_bits.append(jnp.where(me_parity == 1, high_bits[slot], low_bits[slot]))
    preds = tuple(chosen[slot] == bit for slot in range(2) for bit in cand_bits)
    turned = lax.all_to_all(compressed, "pulse", split_axis=1, concat_axis=2, tiled=True)
    filt_cos, filt_sin = filter_tables(azimuth_rate, pulses_dev * lax.axis_size("pulse"))
    *preds, filt_cos, filt_sin, turned = lax.optimization_barrier((*preds, filt_cos, filt_sin, turned))
    focused = azimuth(turned, filt_cos, filt_sin).astype(jnp.bfloat16)
    arrived = [lax.ppermute(focused, "acq", pairs) for pairs in edge_pairs]
    looked = cross_looks(focused, arrived)
    returned = [
        lax.ppermute(looked[slot], "acq", [(dst, src) for src, dst in edge_pairs[slot]])
        for slot in range(2)
    ]
    candidates = []
    for slot in range(2):
        candidates.append(looked[slot])
        back = returned[slot]
        candidates.append(jnp.stack([back[0], -back[1]]))
    results = []
    for slot in range(2):
        pick = candidates[0]
        for index in range(1, len(candidates)):
            pick = jnp.where(preds[slot * len(candidates) + index], candidates[index], pick)
        results.append(pick)
    interfere_real = jnp.stack([item[0] for item in results])[None]
    interfere_imag = jnp.stack([item[1] for item in results])[None]
    return (interfere_real, interfere_imag)


def solution(mesh):
    in_specs = (P("acq", None, "pulse", None), P(), P("acq"), P("pulse"), P("acq", None))
    out_specs = (P("acq", None, "pulse", None), P("acq", None, "pulse", None))
    return jax.shard_map(
        per_device, mesh=mesh, in_specs=in_specs, out_specs=out_specs, check_vma=False
    )
```

```python
import math

import jax
import jax.numpy as jnp
from jax import lax
from jax.experimental import pallas as pl
from jax.experimental.pallas import tpu as pltpu
from jax.sharding import PartitionSpec as P

RNG = 512
TAPS = 1024
LOOK_RNG = 4
LOOK_AZ = 16
BAND_ROWS = 128


def part_tables(length, inverse):
    steps = jnp.arange(length, dtype=jnp.int32)
    angle = 2.0 * jnp.pi * (steps[:, None] * steps[None, :] % length).astype(jnp.float32) / length
    cosine = jnp.cos(angle)
    sine = jnp.sin(angle)
    if inverse:
        sine = -sine
    return jnp.stack([jnp.stack([cosine, -sine]), jnp.stack([sine, cosine])])


def complex_product(left_re, left_im, right_re, right_im):
    return (left_re * right_re - left_im * right_im, left_re * right_im + left_im * right_re)


def band_kernel(phase_ref, band_ref):
    rows = BAND_ROWS
    strip = -(-(TAPS + BAND_ROWS - 1) // 128) * 128
    width = band_ref.shape[3]
    dtype = band_ref.dtype
    amplitude = 2.0 / math.sqrt(TAPS)
    phase = phase_ref[...]
    table_re = (amplitude * jnp.cos(phase)).astype(dtype).astype(jnp.float32)
    table_im = (amplitude * jnp.sin(phase)).astype(dtype).astype(jnp.float32)
    pad = jnp.zeros((1, strip - phase_ref.shape[1]), jnp.float32)
    re_row = jnp.concatenate([table_re, pad], axis=1)
    im_row = jnp.concatenate([table_im, pad], axis=1)
    re_strip = pltpu.roll(jnp.broadcast_to(re_row, (rows, strip)), 0, 1, stride=1, stride_axis=0)
    im_strip = pltpu.roll(jnp.broadcast_to(im_row, (rows, strip)), 0, 1, stride=1, stride_axis=0)
    pieces = (
        (0, 0, re_strip.astype(dtype)),
        (0, 1, (-im_strip).astype(dtype)),
        (1, 0, im_strip.astype(dtype)),
        (1, 1, re_strip.astype(dtype)),
    )
    for start in range(0, band_ref.shape[2], rows):
        stop = min(start + strip, width)
        for part, half, values in pieces:
            band_ref[part, half, start : start + rows, start:stop] = values[:, : stop - start]
            if start > 0:
                band_ref[part, half, start : start + rows, :start] = jnp.zeros((rows, start), dtype)
            if stop < width:
                band_ref[part, half, start : start + rows, stop:] = jnp.zeros((rows, width - stop), dtype)


def band_tables(chirp_phase, width):
    shape = jax.ShapeDtypeStruct((2, 2, RNG, width), jnp.bfloat16)
    band = pl.pallas_call(band_kernel, out_shape=shape)(chirp_phase[None])
    return band.reshape(2, 2 * RNG, width)


def compress(echoes, band, first_pulse, live_pulses):
    pulse_rows = echoes.shape[1]
    dims = (((0, 2), (0, 2)), ((), ()))
    result = lax.dot_general(band, echoes, dims, preferred_element_type=jnp.float32)
    joined = result.reshape(2, RNG, pulse_rows)
    pulse_ids = first_pulse + jnp.arange(pulse_rows, dtype=jnp.int32)
    keep = (pulse_ids < live_pulses).astype(jnp.float32)
    return (joined * keep[None, None, :]).astype(jnp.bfloat16)


def filter_tables(azimuth_rate, length):
    outer_len = 64
    inner_len = length // outer_len
    outer_ids = jnp.arange(outer_len, dtype=jnp.int32)
    inner_ids = jnp.arange(inner_len, dtype=jnp.int32)
    freq_index = outer_ids[:, None] + outer_len * inner_ids[None, :]
    signed = jnp.where(freq_index < length // 2, freq_index, freq_index - length).astype(
        jnp.float32
    )
    quad = signed * signed / length
    phase = (jnp.pi * azimuth_rate)[:, None, None] * quad[None, :, :]
    return jnp.cos(phase), jnp.sin(phase)


def azimuth(turned, filt_cos, filt_sin):
    columns = turned.shape[1]
    length = turned.shape[2]
    outer_len = 64
    inner_len = length // outer_len
    highest = lax.Precision.HIGH
    signal = turned.astype(jnp.float32).reshape(2, columns, outer_len, inner_len)
    section_one = jnp.einsum(
        "pcab,pqak->qckb", signal, part_tables(outer_len, False), precision=highest
    )
    outer_ids = jnp.arange(outer_len, dtype=jnp.int32)
    inner_ids = jnp.arange(inner_len, dtype=jnp.int32)
    twist = (
        2.0
        * jnp.pi
        * (outer_ids[:, None] * inner_ids[None, :] % length).astype(jnp.float32)
        / length
    )
    twist_cos = jnp.cos(twist)
    twist_sin = jnp.sin(twist)
    turned_re, turned_im = complex_product(section_one[0], section_one[1], twist_cos, -twist_sin)
    spectrum = jnp.einsum(
        "pckb,pqbm->qckm",
        jnp.stack([turned_re, turned_im]),
        part_tables(inner_len, False),
        precision=highest,
    )
    filt_re, filt_im = complex_product(spectrum[0], spectrum[1], filt_cos, -filt_sin)
    back_one = jnp.einsum(
        "pckm,pqmb->qckb",
        jnp.stack([filt_re, filt_im]),
        part_tables(inner_len, True),
        precision=highest,
    )
    undo_re, undo_im = complex_product(back_one[0], back_one[1], twist_cos, twist_sin)
    restored = jnp.einsum(
        "pckb,pqka->qcab",
        jnp.stack([undo_re, undo_im]),
        part_tables(outer_len, True),
        precision=highest,
    )
    return (restored / length).reshape(2, columns, length)


def parity(index):
    return bin(index).count("1") % 2


def multilook(stacked):
    count, columns, pulse_len = stacked.shape
    inner = 128
    shaped = stacked.reshape(count, columns // LOOK_RNG, LOOK_RNG, pulse_len // inner, inner)
    summed = jnp.sum(shaped, axis=2)
    lanes = jnp.arange(inner, dtype=jnp.int32)
    groups = jnp.arange(inner // LOOK_AZ, dtype=jnp.int32)
    pool = (lanes[:, None] // LOOK_AZ == groups[None, :]).astype(jnp.float32)
    looked = jnp.einsum("nrab,bg->nrag", summed, pool, precision=lax.Precision.HIGHEST)
    scale = 1.0 / (LOOK_RNG * LOOK_AZ)
    return looked.reshape(count, columns // LOOK_RNG, pulse_len // LOOK_AZ) * scale


def cross_looks(own_block, partners):
    own_f = own_block.astype(jnp.float32)
    prods = []
    for partner in partners:
        other_f = partner.astype(jnp.float32)
        prods.append(own_f[0] * other_f[0] + own_f[1] * other_f[1])
        prods.append(own_f[1] * other_f[0] - own_f[0] * other_f[1])
    looked = multilook(jnp.stack(prods))
    return looked.reshape(len(partners), 2, *looked.shape[1:])


def per_device(raw_echo, chirp_phase, pulse_counts, azimuth_rate, partner_bits):
    echoes = raw_echo[0]
    pulses_dev = echoes.shape[1]
    band = band_tables(chirp_phase, echoes.shape[2])
    live_pulses = pulse_counts[0]
    first_pulse = lax.axis_index("pulse") * pulses_dev
    compressed = compress(echoes, band, first_pulse, live_pulses)
    chosen = partner_bits[0]
    acq_size = lax.axis_size("acq")
    me = lax.axis_index("acq")
    me_parity = jnp.int32(0)
    for which in range(acq_size.bit_length() - 1):
        me_parity = me_parity ^ ((me >> which) & 1)
    low_bits = (0, 1)
    high_bits = (2, 3)
    edge_pairs = []
    for slot in range(2):
        edge_pairs.append(
            [
                (i, i ^ (1 << (high_bits[slot] if parity(i) else low_bits[slot])))
                for i in range(acq_size)
            ]
        )
    cand_bits = []
    for slot in range(2):
        cand_bits.append(jnp.where(me_parity == 1, low_bits[slot], high_bits[slot]))
        cand_bits.append(jnp.where(me_parity == 1, high_bits[slot], low_bits[slot]))
    preds = tuple(chosen[slot] == bit for slot in range(2) for bit in cand_bits)
    turned = lax.all_to_all(compressed, "pulse", split_axis=1, concat_axis=2, tiled=True)
    filt_cos, filt_sin = filter_tables(azimuth_rate, pulses_dev * lax.axis_size("pulse"))
    *preds, filt_cos, filt_sin, turned = lax.optimization_barrier((*preds, filt_cos, filt_sin, turned))
    focused = azimuth(turned, filt_cos, filt_sin).astype(jnp.bfloat16)
    arrived = [lax.ppermute(focused, "acq", pairs) for pairs in edge_pairs]
    looked = cross_looks(focused, arrived)
    returned = [
        lax.ppermute(looked[slot], "acq", [(dst, src) for src, dst in edge_pairs[slot]])
        for slot in range(2)
    ]
    candidates = []
    for slot in range(2):
        candidates.append(looked[slot])
        back = returned[slot]
        candidates.append(jnp.stack([back[0], -back[1]]))
    results = []
    for slot in range(2):
        pick = candidates[0]
        for index in range(1, len(candidates)):
            pick = jnp.where(preds[slot * len(candidates) + index], candidates[index], pick)
        results.append(pick)
    interfere_real = jnp.stack([item[0] for item in results])[None]
    interfere_imag = jnp.stack([item[1] for item in results])[None]
    return (interfere_real, interfere_imag)


def solution(mesh):
    in_specs = (P("acq", None, "pulse", None), P(), P("acq"), P("pulse"), P("acq", None))
    out_specs = (P("acq", None, "pulse", None), P("acq", None, "pulse", None))
    return jax.shard_map(
        per_device, mesh=mesh, in_specs=in_specs, out_specs=out_specs, check_vma=False
    )
```

```python
import math

import jax
import jax.numpy as jnp
from jax import lax
from jax.experimental import pallas as pl
from jax.experimental.pallas import tpu as pltpu
from jax.sharding import PartitionSpec as P

RNG = 512
TAPS = 1024
LOOK_RNG = 4
LOOK_AZ = 16
BAND_ROWS = 128


def part_tables(length, inverse):
    steps = jnp.arange(length, dtype=jnp.int32)
    angle = 2.0 * jnp.pi * (steps[:, None] * steps[None, :] % length).astype(jnp.float32) / length
    cosine = jnp.cos(angle)
    sine = jnp.sin(angle)
    if inverse:
        sine = -sine
    return jnp.stack([jnp.stack([cosine, -sine]), jnp.stack([sine, cosine])])


def complex_product(left_re, left_im, right_re, right_im):
    return (left_re * right_re - left_im * right_im, left_re * right_im + left_im * right_re)


def band_kernel(phase_ref, band_ref):
    rows = BAND_ROWS
    strip = -(-(TAPS + BAND_ROWS - 1) // 128) * 128
    width = band_ref.shape[3]
    dtype = band_ref.dtype
    amplitude = 2.0 / math.sqrt(TAPS)
    phase = phase_ref[...]
    table_re = (amplitude * jnp.cos(phase)).astype(dtype).astype(jnp.float32)
    table_im = (amplitude * jnp.sin(phase)).astype(dtype).astype(jnp.float32)
    pad = jnp.zeros((1, strip - phase_ref.shape[1]), jnp.float32)
    re_row = jnp.concatenate([table_re, pad], axis=1)
    im_row = jnp.concatenate([table_im, pad], axis=1)
    re_strip = pltpu.roll(jnp.broadcast_to(re_row, (rows, strip)), 0, 1, stride=1, stride_axis=0)
    im_strip = pltpu.roll(jnp.broadcast_to(im_row, (rows, strip)), 0, 1, stride=1, stride_axis=0)
    pieces = (
        (0, 0, re_strip.astype(dtype)),
        (0, 1, (-im_strip).astype(dtype)),
        (1, 0, im_strip.astype(dtype)),
        (1, 1, re_strip.astype(dtype)),
    )
    for start in range(0, band_ref.shape[2], rows):
        stop = min(start + strip, width)
        for part, half, values in pieces:
            band_ref[part, half, start : start + rows, start:stop] = values[:, : stop - start]
            if start > 0:
                band_ref[part, half, start : start + rows, :start] = jnp.zeros((rows, start), dtype)
            if stop < width:
                band_ref[part, half, start : start + rows, stop:] = jnp.zeros((rows, width - stop), dtype)


def band_tables(chirp_phase, width):
    shape = jax.ShapeDtypeStruct((2, 2, RNG, width), jnp.bfloat16)
    band = pl.pallas_call(band_kernel, out_shape=shape)(chirp_phase[None])
    return band.reshape(2, 2 * RNG, width)


def compress(echoes, band, first_pulse, live_pulses):
    pulse_rows = echoes.shape[1]
    dims = (((0, 2), (0, 2)), ((), ()))
    result = lax.dot_general(band, echoes, dims, preferred_element_type=jnp.float32)
    joined = result.reshape(2, RNG, pulse_rows)
    pulse_ids = first_pulse + jnp.arange(pulse_rows, dtype=jnp.int32)
    keep = (pulse_ids < live_pulses).astype(jnp.float32)
    return (joined * keep[None, None, :]).astype(jnp.bfloat16)


def filter_tables(azimuth_rate, length):
    outer_len = 64
    inner_len = length // outer_len
    outer_ids = jnp.arange(outer_len, dtype=jnp.int32)
    inner_ids = jnp.arange(inner_len, dtype=jnp.int32)
    freq_index = outer_ids[:, None] + outer_len * inner_ids[None, :]
    signed = jnp.where(freq_index < length // 2, freq_index, freq_index - length).astype(
        jnp.float32
    )
    quad = signed * signed / length
    phase = (jnp.pi * azimuth_rate)[:, None, None] * quad[None, :, :]
    return jnp.cos(phase), jnp.sin(phase)


def azimuth(turned, filt_cos, filt_sin):
    columns = turned.shape[1]
    length = turned.shape[2]
    outer_len = 64
    inner_len = length // outer_len
    highest = lax.Precision.HIGH
    signal = turned.astype(jnp.float32).reshape(2, columns, outer_len, inner_len)
    section_one = jnp.einsum(
        "pcab,pqak->qckb", signal, part_tables(outer_len, False), precision=highest
    )
    outer_ids = jnp.arange(outer_len, dtype=jnp.int32)
    inner_ids = jnp.arange(inner_len, dtype=jnp.int32)
    twist = (
        2.0
        * jnp.pi
        * (outer_ids[:, None] * inner_ids[None, :] % length).astype(jnp.float32)
        / length
    )
    twist_cos = jnp.cos(twist)
    twist_sin = jnp.sin(twist)
    turned_re, turned_im = complex_product(section_one[0], section_one[1], twist_cos, -twist_sin)
    spectrum = jnp.einsum(
        "pckb,pqbm->qckm",
        jnp.stack([turned_re, turned_im]),
        part_tables(inner_len, False),
        precision=highest,
    )
    filt_re, filt_im = complex_product(spectrum[0], spectrum[1], filt_cos, -filt_sin)
    back_one = jnp.einsum(
        "pckm,pqmb->qckb",
        jnp.stack([filt_re, filt_im]),
        part_tables(inner_len, True),
        precision=highest,
    )
    undo_re, undo_im = complex_product(back_one[0], back_one[1], twist_cos, twist_sin)
    restored = jnp.einsum(
        "pckb,pqka->qcab",
        jnp.stack([undo_re, undo_im]),
        part_tables(outer_len, True),
        precision=highest,
    )
    return (restored / length).reshape(2, columns, length)


def parity(index):
    return bin(index).count("1") % 2


def multilook(stacked):
    count, columns, pulse_len = stacked.shape
    inner = 128
    shaped = stacked.reshape(count, columns // LOOK_RNG, LOOK_RNG, pulse_len // inner, inner)
    summed = jnp.sum(shaped, axis=2)
    lanes = jnp.arange(inner, dtype=jnp.int32)
    groups = jnp.arange(inner // LOOK_AZ, dtype=jnp.int32)
    pool = (lanes[:, None] // LOOK_AZ == groups[None, :]).astype(jnp.float32)
    looked = jnp.einsum("nrab,bg->nrag", summed, pool, precision=lax.Precision.HIGHEST)
    scale = 1.0 / (LOOK_RNG * LOOK_AZ)
    return looked.reshape(count, columns // LOOK_RNG, pulse_len // LOOK_AZ) * scale


def cross_looks(own_block, partners):
    own_f = own_block.astype(jnp.float32)
    prods = []
    for partner in partners:
        other_f = partner.astype(jnp.float32)
        prods.append(own_f[0] * other_f[0] + own_f[1] * other_f[1])
        prods.append(own_f[1] * other_f[0] - own_f[0] * other_f[1])
    looked = multilook(jnp.stack(prods))
    return looked.reshape(len(partners), 2, *looked.shape[1:])


def per_device(raw_echo, chirp_phase, pulse_counts, azimuth_rate, partner_bits):
    echoes = raw_echo[0]
    pulses_dev = echoes.shape[1]
    band = band_tables(chirp_phase, echoes.shape[2])
    live_pulses = pulse_counts[0]
    first_pulse = lax.axis_index("pulse") * pulses_dev
    compressed = compress(echoes, band, first_pulse, live_pulses)
    chosen = partner_bits[0]
    acq_size = lax.axis_size("acq")
    me = lax.axis_index("acq")
    bit_count = acq_size.bit_length() - 1
    preds = tuple(chosen[slot] == which for slot in range(2) for which in range(bit_count))
    turned = lax.all_to_all(compressed, "pulse", split_axis=1, concat_axis=2, tiled=True)
    filt_cos, filt_sin = filter_tables(azimuth_rate, pulses_dev * lax.axis_size("pulse"))
    *preds, filt_cos, filt_sin, turned = lax.optimization_barrier((*preds, filt_cos, filt_sin, turned))
    focused = azimuth(turned, filt_cos, filt_sin).astype(jnp.bfloat16)
    arrived = [
        lax.ppermute(focused, "acq", [(i, i ^ (1 << which)) for i in range(acq_size)])
        for which in range(bit_count)
    ]
    partners = []
    for slot in range(2):
        pick = arrived[0]
        for which in range(1, bit_count):
            pick = jnp.where(preds[slot * bit_count + which], arrived[which], pick)
        partners.append(pick)
    looked = cross_looks(focused, partners)
    results = [looked[slot] for slot in range(2)]
    interfere_real = jnp.stack([item[0] for item in results])[None]
    interfere_imag = jnp.stack([item[1] for item in results])[None]
    return (interfere_real, interfere_imag)


def solution(mesh):
    in_specs = (P("acq", None, "pulse", None), P(), P("acq"), P("pulse"), P("acq", None))
    out_specs = (P("acq", None, "pulse", None), P("acq", None, "pulse", None))
    return jax.shard_map(
        per_device, mesh=mesh, in_specs=in_specs, out_specs=out_specs, check_vma=False
    )
```

```python
import math

import jax
import jax.numpy as jnp
from jax import lax
from jax.experimental import pallas as pl
from jax.experimental.pallas import tpu as pltpu
from jax.sharding import PartitionSpec as P

RNG = 512
TAPS = 1024
LOOK_RNG = 4
LOOK_AZ = 16
BAND_ROWS = 128


def part_tables(length, inverse):
    steps = jnp.arange(length, dtype=jnp.int32)
    angle = 2.0 * jnp.pi * (steps[:, None] * steps[None, :] % length).astype(jnp.float32) / length
    cosine = jnp.cos(angle)
    sine = jnp.sin(angle)
    if inverse:
        sine = -sine
    return jnp.stack([jnp.stack([cosine, -sine]), jnp.stack([sine, cosine])])


def complex_product(left_re, left_im, right_re, right_im):
    return (left_re * right_re - left_im * right_im, left_re * right_im + left_im * right_re)


def band_kernel(phase_ref, band_ref):
    rows = BAND_ROWS
    strip = -(-(TAPS + BAND_ROWS - 1) // 128) * 128
    width = band_ref.shape[3]
    dtype = band_ref.dtype
    amplitude = 2.0 / math.sqrt(TAPS)
    phase = phase_ref[...]
    table_re = (amplitude * jnp.cos(phase)).astype(dtype).astype(jnp.float32)
    table_im = (amplitude * jnp.sin(phase)).astype(dtype).astype(jnp.float32)
    pad = jnp.zeros((1, strip - phase_ref.shape[1]), jnp.float32)
    re_row = jnp.concatenate([table_re, pad], axis=1)
    im_row = jnp.concatenate([table_im, pad], axis=1)
    re_strip = pltpu.roll(jnp.broadcast_to(re_row, (rows, strip)), 0, 1, stride=1, stride_axis=0)
    im_strip = pltpu.roll(jnp.broadcast_to(im_row, (rows, strip)), 0, 1, stride=1, stride_axis=0)
    pieces = (
        (0, 0, re_strip.astype(dtype)),
        (0, 1, (-im_strip).astype(dtype)),
        (1, 0, im_strip.astype(dtype)),
        (1, 1, re_strip.astype(dtype)),
    )
    for start in range(0, band_ref.shape[2], rows):
        stop = min(start + strip, width)
        for part, half, values in pieces:
            band_ref[part, half, start : start + rows, start:stop] = values[:, : stop - start]
            if start > 0:
                band_ref[part, half, start : start + rows, :start] = jnp.zeros((rows, start), dtype)
            if stop < width:
                band_ref[part, half, start : start + rows, stop:] = jnp.zeros((rows, width - stop), dtype)


def band_tables(chirp_phase, width):
    shape = jax.ShapeDtypeStruct((2, 2, RNG, width), jnp.bfloat16)
    band = pl.pallas_call(band_kernel, out_shape=shape)(chirp_phase[None])
    return band.reshape(2, 2 * RNG, width)


def compress(echoes, band, first_pulse, live_pulses):
    pulse_rows = echoes.shape[1]
    dims = (((0, 2), (0, 2)), ((), ()))
    result = lax.dot_general(band, echoes, dims, preferred_element_type=jnp.float32)
    joined = result.reshape(2, RNG, pulse_rows)
    pulse_ids = first_pulse + jnp.arange(pulse_rows, dtype=jnp.int32)
    keep = (pulse_ids < live_pulses).astype(jnp.float32)
    return (joined * keep[None, None, :]).astype(jnp.bfloat16)


def filter_tables(azimuth_rate, length):
    outer_len = 64
    inner_len = length // outer_len
    outer_ids = jnp.arange(outer_len, dtype=jnp.int32)
    inner_ids = jnp.arange(inner_len, dtype=jnp.int32)
    freq_index = outer_ids[:, None] + outer_len * inner_ids[None, :]
    signed = jnp.where(freq_index < length // 2, freq_index, freq_index - length).astype(
        jnp.float32
    )
    quad = signed * signed / length
    phase = (jnp.pi * azimuth_rate)[:, None, None] * quad[None, :, :]
    return jnp.cos(phase), jnp.sin(phase)


def azimuth(turned, filt_cos, filt_sin):
    columns = turned.shape[1]
    length = turned.shape[2]
    outer_len = 64
    inner_len = length // outer_len
    highest = lax.Precision.HIGH
    signal = turned.astype(jnp.float32).reshape(2, columns, outer_len, inner_len)
    section_one = jnp.einsum(
        "pcab,pqak->qckb", signal, part_tables(outer_len, False), precision=highest
    )
    section_one, filt_cos, filt_sin = lax.optimization_barrier((section_one, filt_cos, filt_sin))
    outer_ids = jnp.arange(outer_len, dtype=jnp.int32)
    inner_ids = jnp.arange(inner_len, dtype=jnp.int32)
    twist = (
        2.0
        * jnp.pi
        * (outer_ids[:, None] * inner_ids[None, :] % length).astype(jnp.float32)
        / length
    )
    twist_cos = jnp.cos(twist)
    twist_sin = jnp.sin(twist)
    turned_re, turned_im = complex_product(section_one[0], section_one[1], twist_cos, -twist_sin)
    spectrum = jnp.einsum(
        "pckb,pqbm->qckm",
        jnp.stack([turned_re, turned_im]),
        part_tables(inner_len, False),
        precision=highest,
    )
    filt_re, filt_im = complex_product(spectrum[0], spectrum[1], filt_cos, -filt_sin)
    back_one = jnp.einsum(
        "pckm,pqmb->qckb",
        jnp.stack([filt_re, filt_im]),
        part_tables(inner_len, True),
        precision=highest,
    )
    undo_re, undo_im = complex_product(back_one[0], back_one[1], twist_cos, twist_sin)
    restored = jnp.einsum(
        "pckb,pqka->qcab",
        jnp.stack([undo_re, undo_im]),
        part_tables(outer_len, True),
        precision=highest,
    )
    return (restored / length).reshape(2, columns, length)


def parity(index):
    return bin(index).count("1") % 2


def multilook(stacked):
    count, columns, pulse_len = stacked.shape
    inner = 128
    shaped = stacked.reshape(count, columns // LOOK_RNG, LOOK_RNG, pulse_len // inner, inner)
    summed = jnp.sum(shaped, axis=2)
    lanes = jnp.arange(inner, dtype=jnp.int32)
    groups = jnp.arange(inner // LOOK_AZ, dtype=jnp.int32)
    pool = (lanes[:, None] // LOOK_AZ == groups[None, :]).astype(jnp.float32)
    looked = jnp.einsum("nrab,bg->nrag", summed, pool, precision=lax.Precision.HIGHEST)
    scale = 1.0 / (LOOK_RNG * LOOK_AZ)
    return looked.reshape(count, columns // LOOK_RNG, pulse_len // LOOK_AZ) * scale


def cross_looks(own_block, partners):
    own_f = own_block.astype(jnp.float32)
    prods = []
    for partner in partners:
        other_f = partner.astype(jnp.float32)
        prods.append(own_f[0] * other_f[0] + own_f[1] * other_f[1])
        prods.append(own_f[1] * other_f[0] - own_f[0] * other_f[1])
    looked = multilook(jnp.stack(prods))
    return looked.reshape(len(partners), 2, *looked.shape[1:])


def per_device(raw_echo, chirp_phase, pulse_counts, azimuth_rate, partner_bits):
    echoes = raw_echo[0]
    pulses_dev = echoes.shape[1]
    band = band_tables(chirp_phase, echoes.shape[2])
    live_pulses = pulse_counts[0]
    first_pulse = lax.axis_index("pulse") * pulses_dev
    compressed = compress(echoes, band, first_pulse, live_pulses)
    chosen = partner_bits[0]
    acq_size = lax.axis_size("acq")
    me = lax.axis_index("acq")
    me_parity = jnp.int32(0)
    for which in range(acq_size.bit_length() - 1):
        me_parity = me_parity ^ ((me >> which) & 1)
    low_bits = (0, 1)
    high_bits = (2, 3)
    edge_pairs = []
    for slot in range(2):
        edge_pairs.append(
            [
                (i, i ^ (1 << (high_bits[slot] if parity(i) else low_bits[slot])))
                for i in range(acq_size)
            ]
        )
    cand_bits = []
    for slot in range(2):
        cand_bits.append(jnp.where(me_parity == 1, low_bits[slot], high_bits[slot]))
        cand_bits.append(jnp.where(me_parity == 1, high_bits[slot], low_bits[slot]))
    preds = tuple(chosen[slot] == bit for slot in range(2) for bit in cand_bits)
    turned = lax.all_to_all(compressed, "pulse", split_axis=1, concat_axis=2, tiled=True)
    filt_cos, filt_sin = filter_tables(azimuth_rate, pulses_dev * lax.axis_size("pulse"))
    *preds, turned = lax.optimization_barrier((*preds, turned))
    focused = azimuth(turned, filt_cos, filt_sin).astype(jnp.bfloat16)
    arrived = [lax.ppermute(focused, "acq", pairs) for pairs in edge_pairs]
    looked = cross_looks(focused, arrived)
    returned = [
        lax.ppermute(looked[slot], "acq", [(dst, src) for src, dst in edge_pairs[slot]])
        for slot in range(2)
    ]
    candidates = []
    for slot in range(2):
        candidates.append(looked[slot])
        back = returned[slot]
        candidates.append(jnp.stack([back[0], -back[1]]))
    results = []
    for slot in range(2):
        pick = candidates[0]
        for index in range(1, len(candidates)):
            pick = jnp.where(preds[slot * len(candidates) + index], candidates[index], pick)
        results.append(pick)
    interfere_real = jnp.stack([item[0] for item in results])[None]
    interfere_imag = jnp.stack([item[1] for item in results])[None]
    return (interfere_real, interfere_imag)


def solution(mesh):
    in_specs = (P("acq", None, "pulse", None), P(), P("acq"), P("pulse"), P("acq", None))
    out_specs = (P("acq", None, "pulse", None), P("acq", None, "pulse", None))
    return jax.shard_map(
        per_device, mesh=mesh, in_specs=in_specs, out_specs=out_specs, check_vma=False
    )
```

```python
import math

import jax
import jax.numpy as jnp
from jax import lax
from jax.experimental import pallas as pl
from jax.experimental.pallas import tpu as pltpu
from jax.sharding import PartitionSpec as P

RNG = 512
TAPS = 1024
LOOK_RNG = 4
LOOK_AZ = 16
BAND_ROWS = 128


def part_tables(length, inverse):
    steps = jnp.arange(length, dtype=jnp.int32)
    angle = 2.0 * jnp.pi * (steps[:, None] * steps[None, :] % length).astype(jnp.float32) / length
    cosine = jnp.cos(angle)
    sine = jnp.sin(angle)
    if inverse:
        sine = -sine
    return jnp.stack([jnp.stack([cosine, -sine]), jnp.stack([sine, cosine])])


def complex_product(left_re, left_im, right_re, right_im):
    return (left_re * right_re - left_im * right_im, left_re * right_im + left_im * right_re)


def band_kernel(phase_ref, band_ref):
    rows = BAND_ROWS
    strip = -(-(TAPS + BAND_ROWS - 1) // 128) * 128
    width = band_ref.shape[3]
    dtype = band_ref.dtype
    amplitude = 2.0 / math.sqrt(TAPS)
    phase = phase_ref[...]
    table_re = (amplitude * jnp.cos(phase)).astype(dtype).astype(jnp.float32)
    table_im = (amplitude * jnp.sin(phase)).astype(dtype).astype(jnp.float32)
    pad = jnp.zeros((1, strip - phase_ref.shape[1]), jnp.float32)
    re_row = jnp.concatenate([table_re, pad], axis=1)
    im_row = jnp.concatenate([table_im, pad], axis=1)
    re_strip = pltpu.roll(jnp.broadcast_to(re_row, (rows, strip)), 0, 1, stride=1, stride_axis=0)
    im_strip = pltpu.roll(jnp.broadcast_to(im_row, (rows, strip)), 0, 1, stride=1, stride_axis=0)
    pieces = (
        (0, 0, re_strip.astype(dtype)),
        (0, 1, (-im_strip).astype(dtype)),
        (1, 0, im_strip.astype(dtype)),
        (1, 1, re_strip.astype(dtype)),
    )
    for start in range(0, band_ref.shape[2], rows):
        stop = min(start + strip, width)
        for part, half, values in pieces:
            band_ref[part, half, start : start + rows, start:stop] = values[:, : stop - start]
            if start > 0:
                band_ref[part, half, start : start + rows, :start] = jnp.zeros((rows, start), dtype)
            if stop < width:
                band_ref[part, half, start : start + rows, stop:] = jnp.zeros((rows, width - stop), dtype)


def band_tables(chirp_phase, width):
    shape = jax.ShapeDtypeStruct((2, 2, RNG, width), jnp.bfloat16)
    band = pl.pallas_call(band_kernel, out_shape=shape)(chirp_phase[None])
    return band.reshape(2, 2 * RNG, width)


def compress(echoes, band, first_pulse, live_pulses):
    pulse_rows = echoes.shape[1]
    dims = (((0, 2), (0, 2)), ((), ()))
    result = lax.dot_general(band, echoes, dims, preferred_element_type=jnp.float32)
    joined = result.reshape(2, RNG, pulse_rows)
    pulse_ids = first_pulse + jnp.arange(pulse_rows, dtype=jnp.int32)
    keep = (pulse_ids < live_pulses).astype(jnp.float32)
    return (joined * keep[None, None, :]).astype(jnp.bfloat16)


def filter_tables(azimuth_rate, length):
    outer_len = 64
    inner_len = length // outer_len
    outer_ids = jnp.arange(outer_len, dtype=jnp.int32)
    inner_ids = jnp.arange(inner_len, dtype=jnp.int32)
    freq_index = outer_ids[:, None] + outer_len * inner_ids[None, :]
    signed = jnp.where(freq_index < length // 2, freq_index, freq_index - length).astype(
        jnp.float32
    )
    quad = signed * signed / length
    phase = (jnp.pi * azimuth_rate)[:, None, None] * quad[None, :, :]
    return jnp.cos(phase), jnp.sin(phase)


def azimuth(turned, filt_cos, filt_sin):
    columns = turned.shape[1]
    length = turned.shape[2]
    outer_len = 64
    inner_len = length // outer_len
    highest = lax.Precision.HIGH
    signal = turned.astype(jnp.float32).reshape(2, columns, outer_len, inner_len)
    section_one = jnp.einsum(
        "pcab,pqak->qckb", signal, part_tables(outer_len, False), precision=highest
    )
    outer_ids = jnp.arange(outer_len, dtype=jnp.int32)
    inner_ids = jnp.arange(inner_len, dtype=jnp.int32)
    twist = (
        2.0
        * jnp.pi
        * (outer_ids[:, None] * inner_ids[None, :] % length).astype(jnp.float32)
        / length
    )
    twist_cos = jnp.cos(twist)
    twist_sin = jnp.sin(twist)
    turned_re, turned_im = complex_product(section_one[0], section_one[1], twist_cos, -twist_sin)
    spectrum = jnp.einsum(
        "pckb,pqbm->qckm",
        jnp.stack([turned_re, turned_im]),
        part_tables(inner_len, False),
        precision=highest,
    )
    filt_re, filt_im = complex_product(spectrum[0], spectrum[1], filt_cos, -filt_sin)
    back_one = jnp.einsum(
        "pckm,pqmb->qckb",
        jnp.stack([filt_re, filt_im]),
        part_tables(inner_len, True),
        precision=highest,
    )
    undo_re, undo_im = complex_product(back_one[0], back_one[1], twist_cos, twist_sin)
    restored = jnp.einsum(
        "pckb,pqka->qcab",
        jnp.stack([undo_re, undo_im]),
        part_tables(outer_len, True),
        precision=highest,
    )
    return (restored / length).reshape(2, columns, length)


def parity(index):
    return bin(index).count("1") % 2


def multilook(stacked):
    count, columns, pulse_len = stacked.shape
    inner = 128
    shaped = stacked.reshape(count, columns // LOOK_RNG, LOOK_RNG, pulse_len // inner, inner)
    summed = jnp.sum(shaped, axis=2)
    lanes = jnp.arange(inner, dtype=jnp.int32)
    groups = jnp.arange(inner // LOOK_AZ, dtype=jnp.int32)
    pool = (lanes[:, None] // LOOK_AZ == groups[None, :]).astype(jnp.float32)
    looked = jnp.einsum("nrab,bg->nrag", summed, pool, precision=lax.Precision.HIGHEST)
    scale = 1.0 / (LOOK_RNG * LOOK_AZ)
    return looked.reshape(count, columns // LOOK_RNG, pulse_len // LOOK_AZ) * scale


def cross_looks(own_block, partners):
    own_f = own_block.astype(jnp.float32)
    prods = []
    for partner in partners:
        other_f = partner.astype(jnp.float32)
        prods.append(own_f[0] * other_f[0] + own_f[1] * other_f[1])
        prods.append(own_f[1] * other_f[0] - own_f[0] * other_f[1])
    looked = multilook(jnp.stack(prods))
    return looked.reshape(len(partners), 2, *looked.shape[1:])


def per_device(raw_echo, chirp_phase, pulse_counts, azimuth_rate, partner_bits):
    echoes = raw_echo[0]
    pulses_dev = echoes.shape[1]
    band = band_tables(chirp_phase, echoes.shape[2])
    live_pulses = pulse_counts[0]
    first_pulse = lax.axis_index("pulse") * pulses_dev
    compressed = compress(echoes, band, first_pulse, live_pulses)
    chosen = partner_bits[0]
    acq_size = lax.axis_size("acq")
    me = lax.axis_index("acq")
    me_parity = jnp.int32(0)
    for which in range(acq_size.bit_length() - 1):
        me_parity = me_parity ^ ((me >> which) & 1)
    low_bits = (0, 2)
    high_bits = (1, 3)
    edge_pairs = []
    for slot in range(2):
        edge_pairs.append(
            [
                (i, i ^ (1 << (high_bits[slot] if parity(i) else low_bits[slot])))
                for i in range(acq_size)
            ]
        )
    cand_bits = []
    for slot in range(2):
        cand_bits.append(jnp.where(me_parity == 1, low_bits[slot], high_bits[slot]))
        cand_bits.append(jnp.where(me_parity == 1, high_bits[slot], low_bits[slot]))
    preds = tuple(chosen[slot] == bit for slot in range(2) for bit in cand_bits)
    turned = lax.all_to_all(compressed, "pulse", split_axis=1, concat_axis=2, tiled=True)
    filt_cos, filt_sin = filter_tables(azimuth_rate, pulses_dev * lax.axis_size("pulse"))
    *preds, filt_cos, filt_sin, turned = lax.optimization_barrier((*preds, filt_cos, filt_sin, turned))
    focused = azimuth(turned, filt_cos, filt_sin).astype(jnp.bfloat16)
    arrived = [lax.ppermute(focused, "acq", pairs) for pairs in edge_pairs]
    looked = cross_looks(focused, arrived)
    returned = [
        lax.ppermute(looked[slot], "acq", [(dst, src) for src, dst in edge_pairs[slot]])
        for slot in range(2)
    ]
    candidates = []
    for slot in range(2):
        candidates.append(looked[slot])
        back = returned[slot]
        candidates.append(jnp.stack([back[0], -back[1]]))
    results = []
    for slot in range(2):
        pick = candidates[0]
        for index in range(1, len(candidates)):
            pick = jnp.where(preds[slot * len(candidates) + index], candidates[index], pick)
        results.append(pick)
    interfere_real = jnp.stack([item[0] for item in results])[None]
    interfere_imag = jnp.stack([item[1] for item in results])[None]
    return (interfere_real, interfere_imag)


def solution(mesh):
    in_specs = (P("acq", None, "pulse", None), P(), P("acq"), P("pulse"), P("acq", None))
    out_specs = (P("acq", None, "pulse", None), P("acq", None, "pulse", None))
    return jax.shard_map(
        per_device, mesh=mesh, in_specs=in_specs, out_specs=out_specs, check_vma=False
    )
```

```python
import math

import jax
import jax.numpy as jnp
from jax import lax
from jax.experimental import pallas as pl
from jax.experimental.pallas import tpu as pltpu
from jax.sharding import PartitionSpec as P

RNG = 512
TAPS = 1024
LOOK_RNG = 4
LOOK_AZ = 16
BAND_ROWS = 128


def part_tables(length, inverse):
    steps = jnp.arange(length, dtype=jnp.int32)
    angle = 2.0 * jnp.pi * (steps[:, None] * steps[None, :] % length).astype(jnp.float32) / length
    cosine = jnp.cos(angle)
    sine = jnp.sin(angle)
    if inverse:
        sine = -sine
    return jnp.stack([jnp.stack([cosine, -sine]), jnp.stack([sine, cosine])])


def complex_product(left_re, left_im, right_re, right_im):
    return (left_re * right_re - left_im * right_im, left_re * right_im + left_im * right_re)


def band_kernel(phase_ref, band_ref):
    rows = BAND_ROWS
    strip = -(-(TAPS + BAND_ROWS - 1) // 128) * 128
    width = band_ref.shape[3]
    dtype = band_ref.dtype
    amplitude = 2.0 / math.sqrt(TAPS)
    phase = phase_ref[...]
    table_re = (amplitude * jnp.cos(phase)).astype(dtype).astype(jnp.float32)
    table_im = (amplitude * jnp.sin(phase)).astype(dtype).astype(jnp.float32)
    pad = jnp.zeros((1, strip - phase_ref.shape[1]), jnp.float32)
    re_row = jnp.concatenate([table_re, pad], axis=1)
    im_row = jnp.concatenate([table_im, pad], axis=1)
    re_strip = pltpu.roll(jnp.broadcast_to(re_row, (rows, strip)), 0, 1, stride=1, stride_axis=0)
    im_strip = pltpu.roll(jnp.broadcast_to(im_row, (rows, strip)), 0, 1, stride=1, stride_axis=0)
    pieces = (
        (0, 0, re_strip.astype(dtype)),
        (0, 1, (-im_strip).astype(dtype)),
        (1, 0, im_strip.astype(dtype)),
        (1, 1, re_strip.astype(dtype)),
    )
    for start in range(0, band_ref.shape[2], rows):
        stop = min(start + strip, width)
        for part, half, values in pieces:
            band_ref[part, half, start : start + rows, start:stop] = values[:, : stop - start]
            if start > 0:
                band_ref[part, half, start : start + rows, :start] = jnp.zeros((rows, start), dtype)
            if stop < width:
                band_ref[part, half, start : start + rows, stop:] = jnp.zeros((rows, width - stop), dtype)


def band_tables(chirp_phase, width):
    shape = jax.ShapeDtypeStruct((2, 2, RNG, width), jnp.bfloat16)
    band = pl.pallas_call(band_kernel, out_shape=shape)(chirp_phase[None])
    return band.reshape(2, 2 * RNG, width)


def compress(echoes, band, first_pulse, live_pulses):
    pulse_rows = echoes.shape[1]
    dims = (((0, 2), (0, 2)), ((), ()))
    result = lax.dot_general(band, echoes, dims, preferred_element_type=jnp.float32)
    joined = result.reshape(2, RNG, pulse_rows)
    pulse_ids = first_pulse + jnp.arange(pulse_rows, dtype=jnp.int32)
    keep = (pulse_ids < live_pulses).astype(jnp.float32)
    return (joined * keep[None, None, :]).astype(jnp.bfloat16)


def filter_tables(azimuth_rate, length):
    outer_len = 64
    inner_len = length // outer_len
    outer_ids = jnp.arange(outer_len, dtype=jnp.int32)
    inner_ids = jnp.arange(inner_len, dtype=jnp.int32)
    freq_index = outer_ids[:, None] + outer_len * inner_ids[None, :]
    signed = jnp.where(freq_index < length // 2, freq_index, freq_index - length).astype(
        jnp.float32
    )
    quad = signed * signed / length
    phase = (jnp.pi * azimuth_rate)[:, None, None] * quad[None, :, :]
    return jnp.cos(phase), jnp.sin(phase)


def azimuth(turned, filt_cos, filt_sin):
    columns = turned.shape[1]
    length = turned.shape[2]
    outer_len = 64
    inner_len = length // outer_len
    highest = lax.Precision.HIGH
    signal = turned.astype(jnp.float32).reshape(2, columns, outer_len, inner_len)
    section_one = jnp.einsum(
        "pcab,pqak->qckb", signal, part_tables(outer_len, False), precision=highest
    )
    outer_ids = jnp.arange(outer_len, dtype=jnp.int32)
    inner_ids = jnp.arange(inner_len, dtype=jnp.int32)
    twist = (
        2.0
        * jnp.pi
        * (outer_ids[:, None] * inner_ids[None, :] % length).astype(jnp.float32)
        / length
    )
    twist_cos = jnp.cos(twist)
    twist_sin = jnp.sin(twist)
    turned_re, turned_im = complex_product(section_one[0], section_one[1], twist_cos, -twist_sin)
    spectrum = jnp.einsum(
        "pckb,pqbm->qckm",
        jnp.stack([turned_re, turned_im]),
        part_tables(inner_len, False),
        precision=highest,
    )
    filt_re, filt_im = complex_product(spectrum[0], spectrum[1], filt_cos, -filt_sin)
    back_one = jnp.einsum(
        "pckm,pqmb->qckb",
        jnp.stack([filt_re, filt_im]),
        part_tables(inner_len, True),
        precision=highest,
    )
    undo_re, undo_im = complex_product(back_one[0], back_one[1], twist_cos, twist_sin)
    restored = jnp.einsum(
        "pckb,pqka->qcab",
        jnp.stack([undo_re, undo_im]),
        part_tables(outer_len, True),
        precision=highest,
    )
    return (restored / length).reshape(2, columns, length)


def parity(index):
    return bin(index).count("1") % 2


def multilook(stacked):
    count, columns, pulse_len = stacked.shape
    inner = 128
    shaped = stacked.reshape(count, columns // LOOK_RNG, LOOK_RNG, pulse_len // inner, inner)
    summed = jnp.sum(shaped, axis=2)
    lanes = jnp.arange(inner, dtype=jnp.int32)
    groups = jnp.arange(inner // LOOK_AZ, dtype=jnp.int32)
    pool = (lanes[:, None] // LOOK_AZ == groups[None, :]).astype(jnp.float32)
    looked = jnp.einsum("nrab,bg->nrag", summed, pool, precision=lax.Precision.HIGHEST)
    scale = 1.0 / (LOOK_RNG * LOOK_AZ)
    return looked.reshape(count, columns // LOOK_RNG, pulse_len // LOOK_AZ) * scale


def cross_looks(own_block, partners):
    own_f = own_block.astype(jnp.float32)
    prods = []
    for partner in partners:
        other_f = partner.astype(jnp.float32)
        prods.append(own_f[0] * other_f[0] + own_f[1] * other_f[1])
        prods.append(own_f[1] * other_f[0] - own_f[0] * other_f[1])
    looked = multilook(jnp.stack(prods))
    return looked.reshape(len(partners), 2, *looked.shape[1:])


def per_device(raw_echo, chirp_phase, pulse_counts, azimuth_rate, partner_bits):
    echoes = raw_echo[0]
    pulses_dev = echoes.shape[1]
    band = band_tables(chirp_phase, echoes.shape[2])
    live_pulses = pulse_counts[0]
    first_pulse = lax.axis_index("pulse") * pulses_dev
    compressed = compress(echoes, band, first_pulse, live_pulses)
    chosen = partner_bits[0]
    acq_size = lax.axis_size("acq")
    me = lax.axis_index("acq")
    me_parity = jnp.int32(0)
    for which in range(acq_size.bit_length() - 1):
        me_parity = me_parity ^ ((me >> which) & 1)
    low_bits = (0, 3)
    high_bits = (1, 2)
    edge_pairs = []
    for slot in range(2):
        edge_pairs.append(
            [
                (i, i ^ (1 << (high_bits[slot] if parity(i) else low_bits[slot])))
                for i in range(acq_size)
            ]
        )
    cand_bits = []
    for slot in range(2):
        cand_bits.append(jnp.where(me_parity == 1, low_bits[slot], high_bits[slot]))
        cand_bits.append(jnp.where(me_parity == 1, high_bits[slot], low_bits[slot]))
    preds = tuple(chosen[slot] == bit for slot in range(2) for bit in cand_bits)
    turned = lax.all_to_all(compressed, "pulse", split_axis=1, concat_axis=2, tiled=True)
    filt_cos, filt_sin = filter_tables(azimuth_rate, pulses_dev * lax.axis_size("pulse"))
    *preds, filt_cos, filt_sin, turned = lax.optimization_barrier((*preds, filt_cos, filt_sin, turned))
    focused = azimuth(turned, filt_cos, filt_sin).astype(jnp.bfloat16)
    arrived = [lax.ppermute(focused, "acq", pairs) for pairs in edge_pairs]
    looked = cross_looks(focused, arrived)
    returned = [
        lax.ppermute(looked[slot], "acq", [(dst, src) for src, dst in edge_pairs[slot]])
        for slot in range(2)
    ]
    candidates = []
    for slot in range(2):
        candidates.append(looked[slot])
        back = returned[slot]
        candidates.append(jnp.stack([back[0], -back[1]]))
    results = []
    for slot in range(2):
        pick = candidates[0]
        for index in range(1, len(candidates)):
            pick = jnp.where(preds[slot * len(candidates) + index], candidates[index], pick)
        results.append(pick)
    interfere_real = jnp.stack([item[0] for item in results])[None]
    interfere_imag = jnp.stack([item[1] for item in results])[None]
    return (interfere_real, interfere_imag)


def solution(mesh):
    in_specs = (P("acq", None, "pulse", None), P(), P("acq"), P("pulse"), P("acq", None))
    out_specs = (P("acq", None, "pulse", None), P("acq", None, "pulse", None))
    return jax.shard_map(
        per_device, mesh=mesh, in_specs=in_specs, out_specs=out_specs, check_vma=False
    )
```

```python
import math

import jax
import jax.numpy as jnp
from jax import lax
from jax.experimental import pallas as pl
from jax.experimental.pallas import tpu as pltpu
from jax.sharding import PartitionSpec as P

RNG = 512
TAPS = 1024
LOOK_RNG = 4
LOOK_AZ = 16
BAND_ROWS = 128


def part_tables(length, inverse):
    steps = jnp.arange(length, dtype=jnp.int32)
    angle = 2.0 * jnp.pi * (steps[:, None] * steps[None, :] % length).astype(jnp.float32) / length
    cosine = jnp.cos(angle)
    sine = jnp.sin(angle)
    if inverse:
        sine = -sine
    return jnp.stack([jnp.stack([cosine, -sine]), jnp.stack([sine, cosine])])


def complex_product(left_re, left_im, right_re, right_im):
    return (left_re * right_re - left_im * right_im, left_re * right_im + left_im * right_re)


def band_kernel(phase_ref, band_ref):
    rows = BAND_ROWS
    strip = -(-(TAPS + BAND_ROWS - 1) // 128) * 128
    width = band_ref.shape[3]
    dtype = band_ref.dtype
    amplitude = 2.0 / math.sqrt(TAPS)
    phase = phase_ref[...]
    table_re = (amplitude * jnp.cos(phase)).astype(dtype).astype(jnp.float32)
    table_im = (amplitude * jnp.sin(phase)).astype(dtype).astype(jnp.float32)
    pad = jnp.zeros((1, strip - phase_ref.shape[1]), jnp.float32)
    re_row = jnp.concatenate([table_re, pad], axis=1)
    im_row = jnp.concatenate([table_im, pad], axis=1)
    re_strip = pltpu.roll(jnp.broadcast_to(re_row, (rows, strip)), 0, 1, stride=1, stride_axis=0)
    im_strip = pltpu.roll(jnp.broadcast_to(im_row, (rows, strip)), 0, 1, stride=1, stride_axis=0)
    pieces = (
        (0, 0, re_strip.astype(dtype)),
        (0, 1, (-im_strip).astype(dtype)),
        (1, 0, im_strip.astype(dtype)),
        (1, 1, re_strip.astype(dtype)),
    )
    for start in range(0, band_ref.shape[2], rows):
        stop = min(start + strip, width)
        for part, half, values in pieces:
            band_ref[part, half, start : start + rows, start:stop] = values[:, : stop - start]
            if start > 0:
                band_ref[part, half, start : start + rows, :start] = jnp.zeros((rows, start), dtype)
            if stop < width:
                band_ref[part, half, start : start + rows, stop:] = jnp.zeros((rows, width - stop), dtype)


def band_tables(chirp_phase, width):
    shape = jax.ShapeDtypeStruct((2, 2, RNG, width), jnp.bfloat16)
    band = pl.pallas_call(band_kernel, out_shape=shape)(chirp_phase[None])
    return band.reshape(2, 2 * RNG, width)


def compress(echoes, band, first_pulse, live_pulses):
    pulse_rows = echoes.shape[1]
    dims = (((0, 2), (0, 2)), ((), ()))
    result = lax.dot_general(band, echoes, dims, preferred_element_type=jnp.float32)
    joined = result.reshape(2, RNG, pulse_rows)
    pulse_ids = first_pulse + jnp.arange(pulse_rows, dtype=jnp.int32)
    keep = (pulse_ids < live_pulses).astype(jnp.float32)
    return (joined * keep[None, None, :]).astype(jnp.bfloat16)


def filter_tables(azimuth_rate, length):
    outer_len = 64
    inner_len = length // outer_len
    outer_ids = jnp.arange(outer_len, dtype=jnp.int32)
    inner_ids = jnp.arange(inner_len, dtype=jnp.int32)
    freq_index = outer_ids[:, None] + outer_len * inner_ids[None, :]
    signed = jnp.where(freq_index < length // 2, freq_index, freq_index - length).astype(
        jnp.float32
    )
    quad = signed * signed / length
    phase = (jnp.pi * azimuth_rate)[:, None, None] * quad[None, :, :]
    return jnp.cos(phase), jnp.sin(phase)


def azimuth(turned, filt_cos, filt_sin):
    columns = turned.shape[1]
    length = turned.shape[2]
    outer_len = 64
    inner_len = length // outer_len
    highest = lax.Precision.HIGH
    signal = turned.astype(jnp.float32).reshape(2, columns, outer_len, inner_len)
    section_one = jnp.einsum(
        "pcab,pqak->qckb", signal, part_tables(outer_len, False), precision=highest
    )
    outer_ids = jnp.arange(outer_len, dtype=jnp.int32)
    inner_ids = jnp.arange(inner_len, dtype=jnp.int32)
    twist = (
        2.0
        * jnp.pi
        * (outer_ids[:, None] * inner_ids[None, :] % length).astype(jnp.float32)
        / length
    )
    twist_cos = jnp.cos(twist)
    twist_sin = jnp.sin(twist)
    turned_re, turned_im = complex_product(section_one[0], section_one[1], twist_cos, -twist_sin)
    spectrum = jnp.einsum(
        "pckb,pqbm->qckm",
        jnp.stack([turned_re, turned_im]),
        part_tables(inner_len, False),
        precision=highest,
    )
    filt_re, filt_im = complex_product(spectrum[0], spectrum[1], filt_cos, -filt_sin)
    back_one = jnp.einsum(
        "pckm,pqmb->qckb",
        jnp.stack([filt_re, filt_im]),
        part_tables(inner_len, True),
        precision=highest,
    )
    undo_re, undo_im = complex_product(back_one[0], back_one[1], twist_cos, twist_sin)
    restored = jnp.einsum(
        "pckb,pqka->qcab",
        jnp.stack([undo_re, undo_im]),
        part_tables(outer_len, True),
        precision=highest,
    )
    return (restored / length).reshape(2, columns, length)


def parity(index):
    return bin(index).count("1") % 2


def multilook(stacked):
    count, columns, pulse_len = stacked.shape
    inner = 128
    shaped = stacked.reshape(count, columns // LOOK_RNG, LOOK_RNG, pulse_len // inner, inner)
    summed = jnp.sum(shaped, axis=2)
    lanes = jnp.arange(inner, dtype=jnp.int32)
    groups = jnp.arange(inner // LOOK_AZ, dtype=jnp.int32)
    pool = (lanes[:, None] // LOOK_AZ == groups[None, :]).astype(jnp.float32)
    looked = jnp.einsum("nrab,bg->nrag", summed, pool, precision=lax.Precision.HIGHEST)
    scale = 1.0 / (LOOK_RNG * LOOK_AZ)
    return looked.reshape(count, columns // LOOK_RNG, pulse_len // LOOK_AZ) * scale


def cross_looks(own_block, partners):
    own_f = own_block.astype(jnp.float32)
    prods = []
    for partner in partners:
        other_f = partner.astype(jnp.float32)
        prods.append(own_f[0] * other_f[0] + own_f[1] * other_f[1])
        prods.append(own_f[1] * other_f[0] - own_f[0] * other_f[1])
    looked = multilook(jnp.stack(prods))
    return looked.reshape(len(partners), 2, *looked.shape[1:])


def per_device(raw_echo, chirp_phase, pulse_counts, azimuth_rate, partner_bits):
    echoes = raw_echo[0]
    pulses_dev = echoes.shape[1]
    band = band_tables(chirp_phase, echoes.shape[2])
    live_pulses = pulse_counts[0]
    first_pulse = lax.axis_index("pulse") * pulses_dev
    compressed = compress(echoes, band, first_pulse, live_pulses)
    chosen = partner_bits[0]
    acq_size = lax.axis_size("acq")
    me = lax.axis_index("acq")
    me_parity = jnp.int32(0)
    for which in range(acq_size.bit_length() - 1):
        me_parity = me_parity ^ ((me >> which) & 1)
    low_bits = (0, 2)
    high_bits = (1, 3)
    edge_pairs = []
    for slot in range(2):
        edge_pairs.append(
            [
                (i, i ^ (1 << (high_bits[slot] if parity(i) else low_bits[slot])))
                for i in range(acq_size)
            ]
        )
    cand_bits = []
    for slot in range(2):
        cand_bits.append(jnp.where(me_parity == 1, low_bits[slot], high_bits[slot]))
        cand_bits.append(jnp.where(me_parity == 1, high_bits[slot], low_bits[slot]))
    preds = tuple(chosen[slot] == bit for slot in range(2) for bit in cand_bits)
    turned = lax.all_to_all(compressed, "pulse", split_axis=1, concat_axis=2, tiled=True)
    filt_cos, filt_sin = filter_tables(azimuth_rate, pulses_dev * lax.axis_size("pulse"))
    *preds, filt_cos, filt_sin, turned = lax.optimization_barrier((*preds, filt_cos, filt_sin, turned))
    focused = azimuth(turned, filt_cos, filt_sin).astype(jnp.bfloat16)
    arrived = [lax.ppermute(focused, "acq", pairs) for pairs in edge_pairs]
    looked = cross_looks(focused, arrived)
    returned = [
        lax.ppermute(looked[slot], "acq", [(dst, src) for src, dst in edge_pairs[slot]])
        for slot in range(2)
    ]
    candidates = []
    for slot in range(2):
        candidates.append(looked[slot])
        back = returned[slot]
        candidates.append(jnp.stack([back[0], -back[1]]))
    count = len(candidates)
    picked = [jnp.broadcast_to(candidates[0][part][None], (2, *candidates[0].shape[1:])) for part in range(2)]
    for index in range(1, count):
        choose = jnp.stack([preds[slot * count + index] for slot in range(2)])[:, None, None]
        for part in range(2):
            picked[part] = jnp.where(choose, candidates[index][part][None], picked[part])
    interfere_real = picked[0][None]
    interfere_imag = picked[1][None]
    return (interfere_real, interfere_imag)


def solution(mesh):
    in_specs = (P("acq", None, "pulse", None), P(), P("acq"), P("pulse"), P("acq", None))
    out_specs = (P("acq", None, "pulse", None), P("acq", None, "pulse", None))
    return jax.shard_map(
        per_device, mesh=mesh, in_specs=in_specs, out_specs=out_specs, check_vma=False
    )
```

```python
import math

import jax
import jax.numpy as jnp
from jax import lax
from jax.experimental import pallas as pl
from jax.experimental.pallas import tpu as pltpu
from jax.sharding import PartitionSpec as P

RNG = 512
TAPS = 1024
LOOK_RNG = 4
LOOK_AZ = 16
BAND_ROWS = 128


def part_tables(length, inverse):
    steps = jnp.arange(length, dtype=jnp.int32)
    angle = 2.0 * jnp.pi * (steps[:, None] * steps[None, :] % length).astype(jnp.float32) / length
    cosine = jnp.cos(angle)
    sine = jnp.sin(angle)
    if inverse:
        sine = -sine
    return jnp.stack([jnp.stack([cosine, -sine]), jnp.stack([sine, cosine])])


def complex_product(left_re, left_im, right_re, right_im):
    return (left_re * right_re - left_im * right_im, left_re * right_im + left_im * right_re)


def band_kernel(phase_ref, band_ref):
    rows = BAND_ROWS
    strip = -(-(TAPS + BAND_ROWS - 1) // 128) * 128
    width = band_ref.shape[3]
    dtype = band_ref.dtype
    amplitude = 2.0 / math.sqrt(TAPS)
    phase = phase_ref[...]
    table_re = (amplitude * jnp.cos(phase)).astype(dtype).astype(jnp.float32)
    table_im = (amplitude * jnp.sin(phase)).astype(dtype).astype(jnp.float32)
    pad = jnp.zeros((1, strip - phase_ref.shape[1]), jnp.float32)
    re_row = jnp.concatenate([table_re, pad], axis=1)
    im_row = jnp.concatenate([table_im, pad], axis=1)
    re_strip = pltpu.roll(jnp.broadcast_to(re_row, (rows, strip)), 0, 1, stride=1, stride_axis=0)
    im_strip = pltpu.roll(jnp.broadcast_to(im_row, (rows, strip)), 0, 1, stride=1, stride_axis=0)
    pieces = (
        (0, 0, re_strip.astype(dtype)),
        (0, 1, (-im_strip).astype(dtype)),
        (1, 0, im_strip.astype(dtype)),
        (1, 1, re_strip.astype(dtype)),
    )
    for start in range(0, band_ref.shape[2], rows):
        stop = min(start + strip, width)
        for part, half, values in pieces:
            band_ref[part, half, start : start + rows, start:stop] = values[:, : stop - start]
            if start > 0:
                band_ref[part, half, start : start + rows, :start] = jnp.zeros((rows, start), dtype)
            if stop < width:
                band_ref[part, half, start : start + rows, stop:] = jnp.zeros((rows, width - stop), dtype)


def band_tables(chirp_phase, width):
    shape = jax.ShapeDtypeStruct((2, 2, RNG, width), jnp.bfloat16)
    band = pl.pallas_call(band_kernel, out_shape=shape)(chirp_phase[None])
    return band.reshape(2, 2 * RNG, width)


def compress(echoes, band, first_pulse, live_pulses):
    pulse_rows = echoes.shape[1]
    dims = (((0, 2), (0, 2)), ((), ()))
    result = lax.dot_general(band, echoes, dims, preferred_element_type=jnp.float32)
    joined = result.reshape(2, RNG, pulse_rows)
    pulse_ids = first_pulse + jnp.arange(pulse_rows, dtype=jnp.int32)
    keep = (pulse_ids < live_pulses).astype(jnp.float32)
    return (joined * keep[None, None, :]).astype(jnp.bfloat16)


def filter_tables(azimuth_rate, length):
    outer_len = 64
    inner_len = length // outer_len
    outer_ids = jnp.arange(outer_len, dtype=jnp.int32)
    inner_ids = jnp.arange(inner_len, dtype=jnp.int32)
    freq_index = outer_ids[:, None] + outer_len * inner_ids[None, :]
    signed = jnp.where(freq_index < length // 2, freq_index, freq_index - length).astype(
        jnp.float32
    )
    quad = signed * signed / length
    phase = (jnp.pi * azimuth_rate)[:, None, None] * quad[None, :, :]
    return jnp.cos(phase), jnp.sin(phase)


def azimuth(turned, filt_cos, filt_sin):
    columns = turned.shape[1]
    length = turned.shape[2]
    outer_len = 64
    inner_len = length // outer_len
    highest = lax.Precision.HIGH
    signal = turned.astype(jnp.float32).reshape(2, columns, outer_len, inner_len)
    section_one = jnp.einsum(
        "pcab,pqak->qckb", signal, part_tables(outer_len, False), precision=highest
    )
    outer_ids = jnp.arange(outer_len, dtype=jnp.int32)
    inner_ids = jnp.arange(inner_len, dtype=jnp.int32)
    twist = (
        2.0
        * jnp.pi
        * (outer_ids[:, None] * inner_ids[None, :] % length).astype(jnp.float32)
        / length
    )
    twist_cos = jnp.cos(twist)
    twist_sin = jnp.sin(twist)
    turned_re, turned_im = complex_product(section_one[0], section_one[1], twist_cos, -twist_sin)
    spectrum = jnp.einsum(
        "pckb,pqbm->qckm",
        jnp.stack([turned_re, turned_im]),
        part_tables(inner_len, False),
        precision=highest,
    )
    filt_re, filt_im = complex_product(spectrum[0], spectrum[1], filt_cos, -filt_sin)
    back_one = jnp.einsum(
        "pckm,pqmb->qckb",
        jnp.stack([filt_re, filt_im]),
        part_tables(inner_len, True),
        precision=highest,
    )
    undo_re, undo_im = complex_product(back_one[0], back_one[1], twist_cos, twist_sin)
    restored = jnp.einsum(
        "pckb,pqka->qcab",
        jnp.stack([undo_re, undo_im]),
        part_tables(outer_len, True),
        precision=highest,
    )
    return (restored / length).reshape(2, columns, length)


def parity(index):
    return bin(index).count("1") % 2


def multilook(stacked):
    count, columns, pulse_len = stacked.shape
    inner = 128
    shaped = stacked.reshape(count, columns // LOOK_RNG, LOOK_RNG, pulse_len // inner, inner)
    summed = jnp.sum(shaped, axis=2)
    lanes = jnp.arange(inner, dtype=jnp.int32)
    groups = jnp.arange(inner // LOOK_AZ, dtype=jnp.int32)
    pool = (lanes[:, None] // LOOK_AZ == groups[None, :]).astype(jnp.float32)
    looked = jnp.einsum("nrab,bg->nrag", summed, pool, precision=lax.Precision.HIGH)
    scale = 1.0 / (LOOK_RNG * LOOK_AZ)
    return looked.reshape(count, columns // LOOK_RNG, pulse_len // LOOK_AZ) * scale


def cross_looks(own_block, partners):
    own_f = own_block.astype(jnp.float32)
    prods = []
    for partner in partners:
        other_f = partner.astype(jnp.float32)
        prods.append(own_f[0] * other_f[0] + own_f[1] * other_f[1])
        prods.append(own_f[1] * other_f[0] - own_f[0] * other_f[1])
    looked = multilook(jnp.stack(prods))
    return looked.reshape(len(partners), 2, *looked.shape[1:])


def per_device(raw_echo, chirp_phase, pulse_counts, azimuth_rate, partner_bits):
    echoes = raw_echo[0]
    pulses_dev = echoes.shape[1]
    band = band_tables(chirp_phase, echoes.shape[2])
    live_pulses = pulse_counts[0]
    first_pulse = lax.axis_index("pulse") * pulses_dev
    compressed = compress(echoes, band, first_pulse, live_pulses)
    chosen = partner_bits[0]
    acq_size = lax.axis_size("acq")
    me = lax.axis_index("acq")
    me_parity = jnp.int32(0)
    for which in range(acq_size.bit_length() - 1):
        me_parity = me_parity ^ ((me >> which) & 1)
    low_bits = (0, 2)
    high_bits = (1, 3)
    edge_pairs = []
    for slot in range(2):
        edge_pairs.append(
            [
                (i, i ^ (1 << (high_bits[slot] if parity(i) else low_bits[slot])))
                for i in range(acq_size)
            ]
        )
    cand_bits = []
    for slot in range(2):
        cand_bits.append(jnp.where(me_parity == 1, low_bits[slot], high_bits[slot]))
        cand_bits.append(jnp.where(me_parity == 1, high_bits[slot], low_bits[slot]))
    preds = tuple(chosen[slot] == bit for slot in range(2) for bit in cand_bits)
    turned = lax.all_to_all(compressed, "pulse", split_axis=1, concat_axis=2, tiled=True)
    filt_cos, filt_sin = filter_tables(azimuth_rate, pulses_dev * lax.axis_size("pulse"))
    *preds, filt_cos, filt_sin, turned = lax.optimization_barrier((*preds, filt_cos, filt_sin, turned))
    focused = azimuth(turned, filt_cos, filt_sin).astype(jnp.bfloat16)
    arrived = [lax.ppermute(focused, "acq", pairs) for pairs in edge_pairs]
    looked = cross_looks(focused, arrived)
    returned = [
        lax.ppermute(looked[slot], "acq", [(dst, src) for src, dst in edge_pairs[slot]])
        for slot in range(2)
    ]
    candidates = []
    for slot in range(2):
        candidates.append(looked[slot])
        back = returned[slot]
        candidates.append(jnp.stack([back[0], -back[1]]))
    count = len(candidates)
    picked = [jnp.broadcast_to(candidates[0][part][None], (2, *candidates[0].shape[1:])) for part in range(2)]
    for index in range(1, count):
        choose = jnp.stack([preds[slot * count + index] for slot in range(2)])[:, None, None]
        for part in range(2):
            picked[part] = jnp.where(choose, candidates[index][part][None], picked[part])
    interfere_real = picked[0][None]
    interfere_imag = picked[1][None]
    return (interfere_real, interfere_imag)


def solution(mesh):
    in_specs = (P("acq", None, "pulse", None), P(), P("acq"), P("pulse"), P("acq", None))
    out_specs = (P("acq", None, "pulse", None), P("acq", None, "pulse", None))
    return jax.shard_map(
        per_device, mesh=mesh, in_specs=in_specs, out_specs=out_specs, check_vma=False
    )
```

```python
import math

import jax
import jax.numpy as jnp
from jax import lax
from jax.experimental import pallas as pl
from jax.experimental.pallas import tpu as pltpu
from jax.sharding import PartitionSpec as P

RNG = 512
TAPS = 1024
LOOK_RNG = 4
LOOK_AZ = 16
BAND_ROWS = 128


def part_tables(length, inverse):
    steps = jnp.arange(length, dtype=jnp.int32)
    angle = 2.0 * jnp.pi * (steps[:, None] * steps[None, :] % length).astype(jnp.float32) / length
    cosine = jnp.cos(angle)
    sine = jnp.sin(angle)
    if inverse:
        sine = -sine
    return jnp.stack([jnp.stack([cosine, -sine]), jnp.stack([sine, cosine])])


def complex_product(left_re, left_im, right_re, right_im):
    return (left_re * right_re - left_im * right_im, left_re * right_im + left_im * right_re)


def band_kernel(phase_ref, band_ref):
    rows = BAND_ROWS
    strip = -(-(TAPS + BAND_ROWS - 1) // 128) * 128
    width = band_ref.shape[3]
    dtype = band_ref.dtype
    amplitude = 2.0 / math.sqrt(TAPS)
    phase = phase_ref[...]
    table_re = (amplitude * jnp.cos(phase)).astype(dtype).astype(jnp.float32)
    table_im = (amplitude * jnp.sin(phase)).astype(dtype).astype(jnp.float32)
    pad = jnp.zeros((1, strip - phase_ref.shape[1]), jnp.float32)
    re_row = jnp.concatenate([table_re, pad], axis=1)
    im_row = jnp.concatenate([table_im, pad], axis=1)
    re_strip = pltpu.roll(jnp.broadcast_to(re_row, (rows, strip)), 0, 1, stride=1, stride_axis=0)
    im_strip = pltpu.roll(jnp.broadcast_to(im_row, (rows, strip)), 0, 1, stride=1, stride_axis=0)
    pieces = (
        (0, 0, re_strip.astype(dtype)),
        (0, 1, (-im_strip).astype(dtype)),
        (1, 0, im_strip.astype(dtype)),
        (1, 1, re_strip.astype(dtype)),
    )
    for start in range(0, band_ref.shape[2], rows):
        stop = min(start + strip, width)
        for part, half, values in pieces:
            band_ref[part, half, start : start + rows, start:stop] = values[:, : stop - start]
            if start > 0:
                band_ref[part, half, start : start + rows, :start] = jnp.zeros((rows, start), dtype)
            if stop < width:
                band_ref[part, half, start : start + rows, stop:] = jnp.zeros((rows, width - stop), dtype)


def band_tables(chirp_phase, width):
    shape = jax.ShapeDtypeStruct((2, 2, RNG, width), jnp.bfloat16)
    band = pl.pallas_call(band_kernel, out_shape=shape)(chirp_phase[None])
    return band.reshape(2, 2 * RNG, width)


def compress(echoes, band, first_pulse, live_pulses):
    pulse_rows = echoes.shape[1]
    dims = (((0, 2), (0, 2)), ((), ()))
    result = lax.dot_general(band, echoes, dims, preferred_element_type=jnp.float32)
    joined = result.reshape(2, RNG, pulse_rows)
    pulse_ids = first_pulse + jnp.arange(pulse_rows, dtype=jnp.int32)
    keep = (pulse_ids < live_pulses).astype(jnp.float32)
    return (joined * keep[None, None, :]).astype(jnp.bfloat16)


def filter_tables(azimuth_rate, length):
    outer_len = 64
    inner_len = length // outer_len
    outer_ids = jnp.arange(outer_len, dtype=jnp.int32)
    inner_ids = jnp.arange(inner_len, dtype=jnp.int32)
    freq_index = outer_ids[:, None] + outer_len * inner_ids[None, :]
    signed = jnp.where(freq_index < length // 2, freq_index, freq_index - length).astype(
        jnp.float32
    )
    quad = signed * signed / length
    phase = (jnp.pi * azimuth_rate)[:, None, None] * quad[None, :, :]
    return jnp.cos(phase), jnp.sin(phase)


def azimuth(turned, filt_cos, filt_sin):
    columns = turned.shape[1]
    length = turned.shape[2]
    outer_len = 64
    inner_len = length // outer_len
    highest = lax.Precision.HIGH
    signal = turned.reshape(2, columns, outer_len, inner_len)
    table = part_tables(outer_len, False)
    table_hi = table.astype(turned.dtype)
    table_lo = (table - table_hi.astype(jnp.float32)).astype(turned.dtype)
    section_one = jnp.einsum(
        "pcab,pqak->qckb", signal, table_hi, preferred_element_type=jnp.float32
    ) + jnp.einsum("pcab,pqak->qckb", signal, table_lo, preferred_element_type=jnp.float32)
    outer_ids = jnp.arange(outer_len, dtype=jnp.int32)
    inner_ids = jnp.arange(inner_len, dtype=jnp.int32)
    twist = (
        2.0
        * jnp.pi
        * (outer_ids[:, None] * inner_ids[None, :] % length).astype(jnp.float32)
        / length
    )
    twist_cos = jnp.cos(twist)
    twist_sin = jnp.sin(twist)
    turned_re, turned_im = complex_product(section_one[0], section_one[1], twist_cos, -twist_sin)
    spectrum = jnp.einsum(
        "pckb,pqbm->qckm",
        jnp.stack([turned_re, turned_im]),
        part_tables(inner_len, False),
        precision=highest,
    )
    filt_re, filt_im = complex_product(spectrum[0], spectrum[1], filt_cos, -filt_sin)
    back_one = jnp.einsum(
        "pckm,pqmb->qckb",
        jnp.stack([filt_re, filt_im]),
        part_tables(inner_len, True),
        precision=highest,
    )
    undo_re, undo_im = complex_product(back_one[0], back_one[1], twist_cos, twist_sin)
    restored = jnp.einsum(
        "pckb,pqka->qcab",
        jnp.stack([undo_re, undo_im]),
        part_tables(outer_len, True),
        precision=highest,
    )
    return (restored / length).reshape(2, columns, length)


def parity(index):
    return bin(index).count("1") % 2


def multilook(stacked):
    count, columns, pulse_len = stacked.shape
    inner = 128
    shaped = stacked.reshape(count, columns // LOOK_RNG, LOOK_RNG, pulse_len // inner, inner)
    summed = jnp.sum(shaped, axis=2)
    lanes = jnp.arange(inner, dtype=jnp.int32)
    groups = jnp.arange(inner // LOOK_AZ, dtype=jnp.int32)
    pool = (lanes[:, None] // LOOK_AZ == groups[None, :]).astype(jnp.float32)
    looked = jnp.einsum("nrab,bg->nrag", summed, pool, precision=lax.Precision.HIGH)
    scale = 1.0 / (LOOK_RNG * LOOK_AZ)
    return looked.reshape(count, columns // LOOK_RNG, pulse_len // LOOK_AZ) * scale


def cross_looks(own_block, partners):
    own_f = own_block.astype(jnp.float32)
    prods = []
    for partner in partners:
        other_f = partner.astype(jnp.float32)
        prods.append(own_f[0] * other_f[0] + own_f[1] * other_f[1])
        prods.append(own_f[1] * other_f[0] - own_f[0] * other_f[1])
    looked = multilook(jnp.stack(prods))
    return looked.reshape(len(partners), 2, *looked.shape[1:])


def per_device(raw_echo, chirp_phase, pulse_counts, azimuth_rate, partner_bits):
    echoes = raw_echo[0]
    pulses_dev = echoes.shape[1]
    band = band_tables(chirp_phase, echoes.shape[2])
    live_pulses = pulse_counts[0]
    first_pulse = lax.axis_index("pulse") * pulses_dev
    compressed = compress(echoes, band, first_pulse, live_pulses)
    chosen = partner_bits[0]
    acq_size = lax.axis_size("acq")
    me = lax.axis_index("acq")
    me_parity = jnp.int32(0)
    for which in range(acq_size.bit_length() - 1):
        me_parity = me_parity ^ ((me >> which) & 1)
    low_bits = (0, 2)
    high_bits = (1, 3)
    edge_pairs = []
    for slot in range(2):
        edge_pairs.append(
            [
                (i, i ^ (1 << (high_bits[slot] if parity(i) else low_bits[slot])))
                for i in range(acq_size)
            ]
        )
    cand_bits = []
    for slot in range(2):
        cand_bits.append(jnp.where(me_parity == 1, low_bits[slot], high_bits[slot]))
        cand_bits.append(jnp.where(me_parity == 1, high_bits[slot], low_bits[slot]))
    preds = tuple(chosen[slot] == bit for slot in range(2) for bit in cand_bits)
    turned = lax.all_to_all(compressed, "pulse", split_axis=1, concat_axis=2, tiled=True)
    filt_cos, filt_sin = filter_tables(azimuth_rate, pulses_dev * lax.axis_size("pulse"))
    *preds, filt_cos, filt_sin, turned = lax.optimization_barrier((*preds, filt_cos, filt_sin, turned))
    focused = azimuth(turned, filt_cos, filt_sin).astype(jnp.bfloat16)
    arrived = [lax.ppermute(focused, "acq", pairs) for pairs in edge_pairs]
    looked = cross_looks(focused, arrived)
    returned = [
        lax.ppermute(looked[slot], "acq", [(dst, src) for src, dst in edge_pairs[slot]])
        for slot in range(2)
    ]
    candidates = []
    for slot in range(2):
        candidates.append(looked[slot])
        back = returned[slot]
        candidates.append(jnp.stack([back[0], -back[1]]))
    count = len(candidates)
    picked = [jnp.broadcast_to(candidates[0][part][None], (2, *candidates[0].shape[1:])) for part in range(2)]
    for index in range(1, count):
        choose = jnp.stack([preds[slot * count + index] for slot in range(2)])[:, None, None]
        for part in range(2):
            picked[part] = jnp.where(choose, candidates[index][part][None], picked[part])
    interfere_real = picked[0][None]
    interfere_imag = picked[1][None]
    return (interfere_real, interfere_imag)


def solution(mesh):
    in_specs = (P("acq", None, "pulse", None), P(), P("acq"), P("pulse"), P("acq", None))
    out_specs = (P("acq", None, "pulse", None), P("acq", None, "pulse", None))
    return jax.shard_map(
        per_device, mesh=mesh, in_specs=in_specs, out_specs=out_specs, check_vma=False
    )
```
